128 devices in a mesh: section: 8 (over x, core), ctx: 16 (over z, y).
Axes of the slice: x: 4, y: 4, z: 4, core: 2. Of those that a mesh axis runs over, the one named last changes fastest.
Arguments:
- section_inputs: bfloat16 [8, 8192, 6144], P('section', 'ctx'), may hold values from -6 to 6
- input_gains: float32 [8, 3, 6144], P('section'), may hold values from 0.5 to 1.5
- out_gain: float32 [8, 6144], P('section'), may hold values from 0.5 to 1.5
- decay_rates: float32 [8, 48], P('section'), may hold values from 1e-05 to 0.001
- carry_state: float32 [8, 48, 128, 128], P('section'), may hold values from -48 to 48
Outputs:
- next_inputs: bfloat16 [8, 8192, 6144], P('section', 'ctx')
- end_state: float32 [8, 48, 128, 128], P('section', 'ctx')
The draws below stay inside these ranges and needn't reach their ends.
All inputs are finite; a program needn't handle non-finite values.
Results may differ from the reference program's by a relative error of at most 0.012.
Values may be sent and summed in bfloat16 or wider, within the bound.
No kernel may reach another device: no remote copies, remote signals or barrier semaphores. Data moves between devices by JAX's collectives and lax.ppermute only.
A program may use at most 320 MiB of HBM per device.

```python
import math
import jax
import jax.numpy as jnp
from jax import lax

HEADS = 48
HD = 128
D = 6144
BLOCK = 256
SEQ = 8192
N_SECTION = 8


def level_of(own_key, shape, shards, smallest, high):
    def one(dim, parts):
        heights = jax.random.uniform(jax.random.fold_in(jax.random.fold_in(own_key, 6), dim), (parts,), jnp.float32, smallest / len(shards), high / len(shards))
        return jnp.repeat(jnp.exp(heights), shape[dim] // parts).reshape((-1,) + (1,) * (len(shape) - dim - 1))

    gain = one(*shards[0])
    for cut in shards[1:]:
        gain = gain * one(*cut)
    return gain


def scatter_about(stream_key, extent, spread, limit, pieces=(), kind=jnp.bfloat16):
    level = level_of(stream_key, extent, pieces, -0.22, 0.18) if pieces else 1.0
    result = jax.random.normal(stream_key, extent, jnp.float32) * spread * level
    return jnp.minimum(jnp.maximum(result, -limit), limit).astype(kind)


def setup_inputs(seed: int = 0) -> dict:
    key_list = jax.random.split(jax.random.key(seed), 6)
    return {
        "section_inputs": scatter_about(key_list[0], (N_SECTION, SEQ, D), 1.0, 6.0, ((0, 8), (1, 16))),
        "input_gains": jnp.clip(1.0 + 0.1 * jax.random.normal(key_list[1], (N_SECTION, 3, D), jnp.float32), 0.5, 1.5),
        "out_gain": jnp.clip(1.0 + 0.1 * jax.random.normal(key_list[2], (N_SECTION, D), jnp.float32), 0.5, 1.5),
        "decay_rates": jnp.clip(jnp.exp(math.log(0.001) - 4.6051703 * jax.random.uniform(key_list[3], (N_SECTION, HEADS), jnp.float32) ** level_of(key_list[3], (N_SECTION, HEADS), ((0, 8),), -0.2, 0.2)), 9.999999747378752e-06, 0.001),
        "carry_state": scatter_about(key_list[4], (N_SECTION, HEADS, HD, HD), 8.0, 48.0, ((0, 8),), jnp.float32),
    }


EPSILON = 1e-05

def layer(rows, gains, gain_out, rates, carry):
    seq, width = rows.shape
    heads = rates.shape[0]
    head_dim = width // heads
    nblocks = seq // BLOCK
    wide = rows.astype(jnp.float32)
    queries = jax.nn.silu(wide * gains[0]).astype(jnp.bfloat16).reshape(nblocks, BLOCK, heads, head_dim)
    keys = (jax.nn.silu(wide * gains[1]) * head_dim ** (-0.5)).astype(jnp.bfloat16).reshape(nblocks, BLOCK, heads, head_dim)
    values = (wide * gains[2]).astype(jnp.bfloat16).reshape(nblocks, BLOCK, heads, head_dim)
    blocks_wide = wide.reshape(nblocks, BLOCK, width)
    position = jnp.arange(BLOCK).astype(jnp.float32)
    offset = position[:, None] - position[None, :]
    mask = jnp.where(offset[None] >= 0, jnp.exp(-rates[:, None, None] * jnp.maximum(offset, 0.0)[None]), jnp.float32(0.0))
    tail = jnp.exp(-rates[None, :] * (BLOCK - 1 - position)[:, None])
    lead = jnp.exp(-rates[None, :] * (position + 1.0)[:, None])
    block_decay = jnp.exp(-rates * BLOCK)

    def advance(state, items):
        query_b, key_b, value_b, wide_b = items
        scores = jnp.einsum('ihd,jhd->hij', query_b.astype(jnp.float32), key_b.astype(jnp.float32))
        weights = (scores * mask).astype(jnp.bfloat16)
        local = jnp.einsum('hij,jhd->ihd', weights.astype(jnp.float32), value_b.astype(jnp.float32))
        rounded = state.astype(jnp.bfloat16)
        cross = jnp.einsum('ihd,hde->ihe', query_b.astype(jnp.float32), rounded.astype(jnp.float32))
        total = local + lead[:, :, None] * cross
        normed = total * lax.rsqrt(lax.optimization_barrier(jnp.mean(total * total, axis=-1, keepdims=True)) + EPSILON)
        out_rows = (wide_b + normed.reshape(BLOCK, width) * gain_out).astype(jnp.bfloat16)
        scaled = (key_b.astype(jnp.float32) * tail[:, :, None]).astype(jnp.bfloat16)
        update = jnp.einsum('jhd,jhe->hde', scaled.astype(jnp.float32), value_b.astype(jnp.float32))
        return (block_decay[:, None, None] * state + update, out_rows)
    final, outs = lax.scan(advance, carry.astype(jnp.float32), (queries, keys, values, blocks_wide))
    return (outs.reshape(seq, width), final)

def reference(section_inputs, input_gains, out_gain, decay_rates, carry_state):
    outs, finals = lax.map(lambda items: layer(*items), (section_inputs, input_gains, out_gain, decay_rates, carry_state))
    next_inputs = jnp.roll(outs, 1, axis=0)
    return (next_inputs, finals)
```

```python
import functools

import jax
import jax.numpy as jnp
from jax import lax
from jax.experimental import pallas as pl
from jax.experimental.pallas import tpu as pltpu
from jax.sharding import PartitionSpec as P

BLOCK = 256
EPSILON = 1e-05
HEADS_PER_STEP = 4


def _silu(v):
    return v / (1.0 + jnp.exp(-v))


def _dot_nt(a, b):
    return lax.dot_general(a, b, (((1,), (1,)), ((), ())), preferred_element_type=jnp.float32)


def _dot_tn(a, b):
    return lax.dot_general(a, b, (((0,), (0,)), ((), ())), preferred_element_type=jnp.float32)


def _dot(a, b):
    return lax.dot_general(a, b, (((1,), (0,)), ((), ())), preferred_element_type=jnp.float32)


def _block_state(keys_b, values_b, rate, pos):
    tail = jnp.exp(-rate * (BLOCK - 1 - pos))
    scaled = (keys_b.astype(jnp.float32) * tail).astype(jnp.bfloat16)
    return _dot_tn(scaled, values_b)


def _summary_kernel(rates_ref, x_ref, g_ref, o_ref, *, hg, head_dim, nblocks):
    step = pl.program_id(0)
    pos = lax.broadcasted_iota(jnp.int32, (BLOCK, 1), 0).astype(jnp.float32)
    for hh in range(hg):
        rate = jnp.full((1, 1), rates_ref[step * hg + hh], jnp.float32)
        cols = slice(hh * head_dim, (hh + 1) * head_dim)
        decay = jnp.exp(-rate * BLOCK)
        acc = None
        for b in range(nblocks):
            rows = slice(b * BLOCK, (b + 1) * BLOCK)
            x = x_ref[0, rows, cols].astype(jnp.float32)
            keys_b = (_silu(x * g_ref[0, 1:2, cols]) * head_dim ** (-0.5)).astype(jnp.bfloat16)
            values_b = (x * g_ref[0, 2:3, cols]).astype(jnp.bfloat16)
            update = _block_state(keys_b, values_b, rate, pos)
            acc = update if acc is None else decay * acc + update
        o_ref[hh] = acc


def _output_kernel(rates_ref, x_ref, g_ref, go_ref, s_ref, o_ref, *, hg, head_dim, nblocks):
    step = pl.program_id(0)
    pos = lax.broadcasted_iota(jnp.int32, (BLOCK, 1), 0).astype(jnp.float32)
    row = lax.broadcasted_iota(jnp.int32, (BLOCK, BLOCK), 0)
    col = lax.broadcasted_iota(jnp.int32, (BLOCK, BLOCK), 1)
    offset = (row - col).astype(jnp.float32)
    causal = row >= col
    for hh in range(hg):
        rate = jnp.full((1, 1), rates_ref[step * hg + hh], jnp.float32)
        cols = slice(hh * head_dim, (hh + 1) * head_dim)
        mask = jnp.where(causal, jnp.exp(-rate * jnp.maximum(offset, 0.0)), 0.0)
        lead = jnp.exp(-rate * (pos + 1.0))
        decay = jnp.exp(-rate * BLOCK)
        state = s_ref[hh]
        for b in range(nblocks):
            rows = slice(b * BLOCK, (b + 1) * BLOCK)
            x = x_ref[0, rows, cols].astype(jnp.float32)
            queries_b = _silu(x * g_ref[0, 0:1, cols]).astype(jnp.bfloat16)
            keys_b = (_silu(x * g_ref[0, 1:2, cols]) * head_dim ** (-0.5)).astype(jnp.bfloat16)
            values_b = (x * g_ref[0, 2:3, cols]).astype(jnp.bfloat16)
            scores = _dot_nt(queries_b, keys_b)
            weights = (scores * mask).astype(jnp.bfloat16)
            local = _dot(weights, values_b)
            cross = _dot(queries_b, state.astype(jnp.bfloat16))
            total = local + lead * cross
            normed = total * lax.rsqrt(jnp.mean(total * total, axis=-1, keepdims=True) + EPSILON)
            o_ref[0, rows, cols] = (x + normed * go_ref[0:1, cols]).astype(o_ref.dtype)
            if b + 1 < nblocks:
                state = decay * state + _block_state(keys_b, values_b, rate, pos)


def _summaries(rates, rows, gains, head_dim):
    _, count, width = rows.shape
    heads = width // head_dim
    hg = HEADS_PER_STEP
    cw = hg * head_dim
    kernel = functools.partial(_summary_kernel, hg=hg, head_dim=head_dim, nblocks=count // BLOCK)
    return pl.pallas_call(
        kernel,
        grid_spec=pltpu.PrefetchScalarGridSpec(
            num_scalar_prefetch=1,
            grid=(heads // hg,),
            in_specs=[
                pl.BlockSpec((1, count, cw), lambda i, r: (0, 0, i)),
                pl.BlockSpec((1, 3, cw), lambda i, r: (0, 0, i)),
            ],
            out_specs=pl.BlockSpec((hg, head_dim, head_dim), lambda i, r: (i, 0, 0)),
        ),
        out_shape=jax.ShapeDtypeStruct((heads, head_dim, head_dim), jnp.float32),
        cost_estimate=pl.CostEstimate(
            flops=2 * count * width * head_dim, transcendentals=count * width,
            bytes_accessed=count * width * 2 + heads * head_dim * head_dim * 4,
        ),
    )(rates, rows, gains)


def _outputs(rates, rows, gains, gain_out, states, head_dim):
    _, count, width = rows.shape
    heads = width // head_dim
    hg = HEADS_PER_STEP
    cw = hg * head_dim
    kernel = functools.partial(_output_kernel, hg=hg, head_dim=head_dim, nblocks=count // BLOCK)
    return pl.pallas_call(
        kernel,
        grid_spec=pltpu.PrefetchScalarGridSpec(
            num_scalar_prefetch=1,
            grid=(heads // hg,),
            in_specs=[
                pl.BlockSpec((1, count, cw), lambda i, r: (0, 0, i)),
                pl.BlockSpec((1, 3, cw), lambda i, r: (0, 0, i)),
                pl.BlockSpec((1, cw), lambda i, r: (0, i)),
                pl.BlockSpec((hg, head_dim, head_dim), lambda i, r: (i, 0, 0)),
            ],
            out_specs=pl.BlockSpec((1, count, cw), lambda i, r: (0, 0, i)),
        ),
        out_shape=jax.ShapeDtypeStruct(rows.shape, rows.dtype),
        cost_estimate=pl.CostEstimate(
            flops=8 * count * BLOCK * width, transcendentals=3 * count * width,
            bytes_accessed=2 * count * width * 2 + heads * head_dim * head_dim * 4,
        ),
    )(rates, rows, gains, gain_out, states)


def on_device(section_inputs, input_gains, out_gain, decay_rates, carry_state):
    _, count, width = section_inputs.shape
    rates = decay_rates[0]
    heads = rates.shape[0]
    head_dim = width // heads
    group_size = lax.axis_size("ctx")
    own_heads = heads // group_size
    place = lax.axis_index("ctx")

    summary = _summaries(rates, section_inputs, input_gains, head_dim)
    gathered = lax.all_to_all(summary, "ctx", 0, 0, tiled=True)
    gathered = gathered.reshape(group_size, own_heads, head_dim, head_dim)

    start = place * own_heads
    carry_part = lax.dynamic_slice_in_dim(carry_state[0], start, own_heads, 0)
    rate_part = lax.dynamic_slice_in_dim(rates, start, own_heads, 0)
    target = jnp.arange(group_size + 1)[:, None]
    source = jnp.arange(group_size)[None, :]
    gap = (target - 1 - source).astype(jnp.float32)
    weights = jnp.where(
        (source < target)[:, :, None],
        jnp.exp(-rate_part[None, None, :] * count * jnp.maximum(gap, 0.0)[:, :, None]),
        0.0,
    )
    carry_weights = jnp.exp(-rate_part[None, :] * count * target.astype(jnp.float32))
    prefixes = jnp.einsum(
        "tsh,shde->thde", weights, gathered, precision=lax.Precision.HIGHEST
    ) + carry_weights[:, :, None, None] * carry_part[None]
    end_part = prefixes[group_size]
    incoming = lax.all_to_all(
        prefixes[:group_size].reshape(heads, head_dim, head_dim), "ctx", 0, 0, tiled=True
    )

    rows_out = _outputs(rates, section_inputs, input_gains, out_gain, incoming, head_dim)
    count_s = lax.axis_size("section")
    pairs = [(src, (src + 1) % count_s) for src in range(count_s)]
    next_rows = lax.ppermute(rows_out, "section", pairs)
    return (next_rows, end_part[None])


def solution(mesh):
    return jax.shard_map(
        on_device,
        mesh=mesh,
        in_specs=(
            P("section", "ctx", None),
            P("section", None, None),
            P("section", None),
            P("section", None),
            P("section", None, None, None),
        ),
        out_specs=(P("section", "ctx", None), P("section", "ctx", None, None)),
        check_vma=False,
    )
```

```python
import functools

import jax
import jax.numpy as jnp
from jax import lax
from jax.experimental import pallas as pl
from jax.experimental.pallas import tpu as pltpu
from jax.sharding import PartitionSpec as P

BLOCK = 256
EPSILON = 1e-05
HEADS_PER_STEP = 4


def _silu(v):
    return v / (1.0 + jnp.exp(-v))


def _dot_nt(a, b):
    return lax.dot_general(a, b, (((1,), (1,)), ((), ())), preferred_element_type=jnp.float32)


def _dot_tn(a, b):
    return lax.dot_general(a, b, (((0,), (0,)), ((), ())), preferred_element_type=jnp.float32)


def _dot(a, b):
    return lax.dot_general(a, b, (((1,), (0,)), ((), ())), preferred_element_type=jnp.float32)


def _block_state(keys_b, values_b, rate, pos):
    tail = jnp.exp(-rate * (BLOCK - 1 - pos))
    scaled = (keys_b.astype(jnp.float32) * tail).astype(jnp.bfloat16)
    return _dot_tn(scaled, values_b)


def _summary_kernel(rates_ref, x_ref, g_ref, o_ref, *, hg, head_dim, nblocks):
    step = pl.program_id(0)
    pos = lax.broadcasted_iota(jnp.int32, (BLOCK, 1), 0).astype(jnp.float32)
    for hh in range(hg):
        rate = jnp.full((1, 1), rates_ref[step * hg + hh], jnp.float32)
        cols = slice(hh * head_dim, (hh + 1) * head_dim)
        decay = jnp.exp(-rate * BLOCK)
        acc = None
        for b in range(nblocks):
            rows = slice(b * BLOCK, (b + 1) * BLOCK)
            x = x_ref[0, rows, cols].astype(jnp.float32)
            keys_b = (_silu(x * g_ref[0, 1:2, cols]) * head_dim ** (-0.5)).astype(jnp.bfloat16)
            values_b = (x * g_ref[0, 2:3, cols]).astype(jnp.bfloat16)
            update = _block_state(keys_b, values_b, rate, pos)
            acc = update if acc is None else decay * acc + update
        o_ref[hh] = acc


def _output_kernel(rates_ref, x_ref, g_ref, go_ref, s_ref, o_ref, *, hg, head_dim, nblocks):
    step = pl.program_id(0)
    pos = lax.broadcasted_iota(jnp.int32, (BLOCK, 1), 0).astype(jnp.float32)
    row = lax.broadcasted_iota(jnp.int32, (BLOCK, BLOCK), 0)
    col = lax.broadcasted_iota(jnp.int32, (BLOCK, BLOCK), 1)
    offset = (row - col).astype(jnp.float32)
    causal = row >= col
    for hh in range(hg):
        rate = jnp.full((1, 1), rates_ref[step * hg + hh], jnp.float32)
        cols = slice(hh * head_dim, (hh + 1) * head_dim)
        mask = jnp.where(causal, jnp.exp(-rate * jnp.maximum(offset, 0.0)), 0.0)
        lead = jnp.exp(-rate * (pos + 1.0))
        decay = jnp.exp(-rate * BLOCK)
        state = s_ref[hh].astype(jnp.float32)
        for b in range(nblocks):
            rows = slice(b * BLOCK, (b + 1) * BLOCK)
            x = x_ref[0, rows, cols].astype(jnp.float32)
            queries_b = _silu(x * g_ref[0, 0:1, cols]).astype(jnp.bfloat16)
            keys_b = (_silu(x * g_ref[0, 1:2, cols]) * head_dim ** (-0.5)).astype(jnp.bfloat16)
            values_b = (x * g_ref[0, 2:3, cols]).astype(jnp.bfloat16)
            scores = _dot_nt(queries_b, keys_b)
            weights = (scores * mask).astype(jnp.bfloat16)
            local = _dot(weights, values_b)
            cross = _dot(queries_b, state.astype(jnp.bfloat16))
            total = local + lead * cross
            normed = total * lax.rsqrt(jnp.mean(total * total, axis=-1, keepdims=True) + EPSILON)
            o_ref[0, rows, cols] = (x + normed * go_ref[0:1, cols]).astype(o_ref.dtype)
            if b + 1 < nblocks:
                state = decay * state + _block_state(keys_b, values_b, rate, pos)


def _summaries(rates, rows, gains, head_dim):
    _, count, width = rows.shape
    heads = width // head_dim
    hg = HEADS_PER_STEP
    cw = hg * head_dim
    kernel = functools.partial(_summary_kernel, hg=hg, head_dim=head_dim, nblocks=count // BLOCK)
    return pl.pallas_call(
        kernel,
        grid_spec=pltpu.PrefetchScalarGridSpec(
            num_scalar_prefetch=1,
            grid=(heads // hg,),
            in_specs=[
                pl.BlockSpec((1, count, cw), lambda i, r: (0, 0, i)),
                pl.BlockSpec((1, 3, cw), lambda i, r: (0, 0, i)),
            ],
            out_specs=pl.BlockSpec((hg, head_dim, head_dim), lambda i, r: (i, 0, 0)),
        ),
        out_shape=jax.ShapeDtypeStruct((heads, head_dim, head_dim), jnp.float32),
        cost_estimate=pl.CostEstimate(
            flops=2 * count * width * head_dim, transcendentals=count * width,
            bytes_accessed=count * width * 2 + heads * head_dim * head_dim * 4,
        ),
    )(rates, rows, gains)


def _outputs(rates, rows, gains, gain_out, states, head_dim):
    _, count, width = rows.shape
    heads = width // head_dim
    hg = HEADS_PER_STEP
    cw = hg * head_dim
    kernel = functools.partial(_output_kernel, hg=hg, head_dim=head_dim, nblocks=count // BLOCK)
    return pl.pallas_call(
        kernel,
        grid_spec=pltpu.PrefetchScalarGridSpec(
            num_scalar_prefetch=1,
            grid=(heads // hg,),
            in_specs=[
                pl.BlockSpec((1, count, cw), lambda i, r: (0, 0, i)),
                pl.BlockSpec((1, 3, cw), lambda i, r: (0, 0, i)),
                pl.BlockSpec((1, cw), lambda i, r: (0, i)),
                pl.BlockSpec((hg, head_dim, head_dim), lambda i, r: (i, 0, 0)),
            ],
            out_specs=pl.BlockSpec((1, count, cw), lambda i, r: (0, 0, i)),
        ),
        out_shape=jax.ShapeDtypeStruct(rows.shape, rows.dtype),
        cost_estimate=pl.CostEstimate(
            flops=8 * count * BLOCK * width, transcendentals=3 * count * width,
            bytes_accessed=2 * count * width * 2 + heads * head_dim * head_dim * 4,
        ),
    )(rates, rows, gains, gain_out, states)


def on_device(section_inputs, input_gains, out_gain, decay_rates, carry_state):
    _, count, width = section_inputs.shape
    rates = decay_rates[0]
    heads = rates.shape[0]
    head_dim = width // heads
    group_size = lax.axis_size("ctx")
    own_heads = heads // group_size
    place = lax.axis_index("ctx")
    count_s = lax.axis_size("section")
    pairs = [(src, (src + 1) % count_s) for src in range(count_s)]

    prev_rows = lax.ppermute(section_inputs, "section", pairs)
    prev_gains, prev_gain_out, prev_rates = lax.ppermute(
        (input_gains, out_gain, decay_rates), "section", pairs
    )

    summary = _summaries(rates, section_inputs, input_gains, head_dim)
    gathered = lax.all_to_all(summary.astype(jnp.bfloat16), "ctx", 0, 0, tiled=True)
    gathered = gathered.astype(jnp.float32).reshape(group_size, own_heads, head_dim, head_dim)

    start = place * own_heads
    carry_part = lax.dynamic_slice_in_dim(carry_state[0], start, own_heads, 0)
    rate_part = lax.dynamic_slice_in_dim(rates, start, own_heads, 0)
    target = jnp.arange(group_size + 1)[:, None]
    source = jnp.arange(group_size)[None, :]
    gap = (target - 1 - source).astype(jnp.float32)
    weights = jnp.where(
        (source < target)[:, :, None],
        jnp.exp(-rate_part[None, None, :] * count * jnp.maximum(gap, 0.0)[:, :, None]),
        0.0,
    )
    carry_weights = jnp.exp(-rate_part[None, :] * count * target.astype(jnp.float32))
    prefixes = jnp.einsum(
        "tsh,shde->thde", weights, gathered, precision=lax.Precision.HIGHEST
    ) + carry_weights[:, :, None, None] * carry_part[None]
    end_part = prefixes[group_size]
    incoming = lax.all_to_all(
        prefixes[:group_size].astype(jnp.bfloat16).reshape(heads, head_dim, head_dim),
        "ctx", 0, 0, tiled=True,
    )
    prev_incoming = lax.ppermute(incoming, "section", pairs)

    next_rows = _outputs(
        prev_rates[0], prev_rows, prev_gains, prev_gain_out, prev_incoming, head_dim
    )
    return (next_rows, end_part[None])


def solution(mesh):
    return jax.shard_map(
        on_device,
        mesh=mesh,
        in_specs=(
            P("section", "ctx", None),
            P("section", None, None),
            P("section", None),
            P("section", None),
            P("section", None, None, None),
        ),
        out_specs=(P("section", "ctx", None), P("section", "ctx", None, None)),
        check_vma=False,
    )
```

```python
import functools

import jax
import jax.numpy as jnp
from jax import lax
from jax.experimental import pallas as pl
from jax.experimental.pallas import tpu as pltpu
from jax.sharding import PartitionSpec as P

BLOCK = 256
EPSILON = 1e-05
HEADS_PER_STEP = 4


def _silu(v):
    return v / (1.0 + jnp.exp(-v))


def _dot_nt(a, b):
    return lax.dot_general(a, b, (((1,), (1,)), ((), ())), preferred_element_type=jnp.float32)


def _dot_tn(a, b):
    return lax.dot_general(a, b, (((0,), (0,)), ((), ())), preferred_element_type=jnp.float32)


def _dot(a, b):
    return lax.dot_general(a, b, (((1,), (0,)), ((), ())), preferred_element_type=jnp.float32)


def _block_state(keys_b, values_b, rate, pos):
    tail = jnp.exp(-rate * (BLOCK - 1 - pos))
    scaled = (keys_b.astype(jnp.float32) * tail).astype(jnp.bfloat16)
    return _dot_tn(scaled, values_b)


def _summary_kernel(rates_ref, x_ref, g_ref, o_ref, *, hg, head_dim, nblocks):
    step = pl.program_id(0)
    pos = lax.broadcasted_iota(jnp.int32, (BLOCK, 1), 0).astype(jnp.float32)
    for hh in range(hg):
        rate = jnp.full((1, 1), rates_ref[step * hg + hh], jnp.float32)
        cols = slice(hh * head_dim, (hh + 1) * head_dim)
        decay = jnp.exp(-rate * BLOCK)
        acc = None
        for b in range(nblocks):
            rows = slice(b * BLOCK, (b + 1) * BLOCK)
            x = x_ref[0, rows, cols].astype(jnp.float32)
            keys_b = (_silu(x * g_ref[0, 1:2, cols]) * head_dim ** (-0.5)).astype(jnp.bfloat16)
            values_b = (x * g_ref[0, 2:3, cols]).astype(jnp.bfloat16)
            update = _block_state(keys_b, values_b, rate, pos)
            acc = update if acc is None else decay * acc + update
        o_ref[hh] = acc.astype(o_ref.dtype)


def _local_kernel(rates_ref, x_ref, g_ref, q_ref, l_ref, r_ref, *, hg, head_dim, nblocks):
    step = pl.program_id(0)
    pos = lax.broadcasted_iota(jnp.int32, (BLOCK, 1), 0).astype(jnp.float32)
    row = lax.broadcasted_iota(jnp.int32, (BLOCK, BLOCK), 0)
    col = lax.broadcasted_iota(jnp.int32, (BLOCK, BLOCK), 1)
    offset = (row - col).astype(jnp.float32)
    causal = row >= col
    for hh in range(hg):
        rate = jnp.full((1, 1), rates_ref[step * hg + hh], jnp.float32)
        cols = slice(hh * head_dim, (hh + 1) * head_dim)
        mask = jnp.where(causal, jnp.exp(-rate * jnp.maximum(offset, 0.0)), 0.0)
        decay = jnp.exp(-rate * BLOCK)
        running = None
        for b in range(nblocks):
            rows = slice(b * BLOCK, (b + 1) * BLOCK)
            x = x_ref[0, rows, cols].astype(jnp.float32)
            queries_b = _silu(x * g_ref[0, 0:1, cols]).astype(jnp.bfloat16)
            keys_b = (_silu(x * g_ref[0, 1:2, cols]) * head_dim ** (-0.5)).astype(jnp.bfloat16)
            values_b = (x * g_ref[0, 2:3, cols]).astype(jnp.bfloat16)
            scores = _dot_nt(queries_b, keys_b)
            weights = (scores * mask).astype(jnp.bfloat16)
            q_ref[0, rows, cols] = queries_b
            l_ref[0, rows, cols] = _dot(weights, values_b)
            if b + 1 < nblocks:
                update = _block_state(keys_b, values_b, rate, pos)
                running = update if running is None else decay * running + update
                r_ref[b, hh] = running


def _final_kernel(rates_ref, x_ref, q_ref, l_ref, r_ref, s_ref, go_ref, o_ref, *, hg, head_dim, nblocks):
    step = pl.program_id(0)
    pos = lax.broadcasted_iota(jnp.int32, (BLOCK, 1), 0).astype(jnp.float32)
    for hh in range(hg):
        rate = jnp.full((1, 1), rates_ref[step * hg + hh], jnp.float32)
        cols = slice(hh * head_dim, (hh + 1) * head_dim)
        lead = jnp.exp(-rate * (pos + 1.0))
        decay = jnp.exp(-rate * BLOCK)
        entering = s_ref[hh].astype(jnp.float32)
        state = entering
        for b in range(nblocks):
            rows = slice(b * BLOCK, (b + 1) * BLOCK)
            if b > 0:
                state = decay * state + (r_ref[b - 1, hh] - decay * r_ref[b - 2, hh] if b > 1 else r_ref[0, hh])
            cross = _dot(q_ref[0, rows, cols], state.astype(jnp.bfloat16))
            total = l_ref[0, rows, cols] + lead * cross
            normed = total * lax.rsqrt(jnp.mean(total * total, axis=-1, keepdims=True) + EPSILON)
            x = x_ref[0, rows, cols].astype(jnp.float32)
            o_ref[0, rows, cols] = (x + normed * go_ref[0:1, cols]).astype(o_ref.dtype)


def _summaries(rates, rows, gains, head_dim):
    _, count, width = rows.shape
    heads = width // head_dim
    hg = HEADS_PER_STEP
    cw = hg * head_dim
    kernel = functools.partial(_summary_kernel, hg=hg, head_dim=head_dim, nblocks=count // BLOCK)
    return pl.pallas_call(
        kernel,
        grid_spec=pltpu.PrefetchScalarGridSpec(
            num_scalar_prefetch=1,
            grid=(heads // hg,),
            in_specs=[
                pl.BlockSpec((1, count, cw), lambda i, r: (0, 0, i)),
                pl.BlockSpec((1, 3, cw), lambda i, r: (0, 0, i)),
            ],
            out_specs=pl.BlockSpec((hg, head_dim, head_dim), lambda i, r: (i, 0, 0)),
        ),
        out_shape=jax.ShapeDtypeStruct((heads, head_dim, head_dim), jnp.bfloat16),
        cost_estimate=pl.CostEstimate(
            flops=2 * count * width * head_dim, transcendentals=count * width,
            bytes_accessed=count * width * 2 + heads * head_dim * head_dim * 4,
        ),
    )(rates, rows, gains)


def _outputs(rates, rows, gains, gain_out, states, head_dim):
    _, count, width = rows.shape
    heads = width // head_dim
    hg = HEADS_PER_STEP
    cw = hg * head_dim
    nblocks = count // BLOCK
    row_spec = pl.BlockSpec((1, count, cw), lambda i, r: (0, 0, i))
    run_spec = pl.BlockSpec((nblocks - 1, hg, head_dim, head_dim), lambda i, r: (0, i, 0, 0))
    local_kernel = functools.partial(_local_kernel, hg=hg, head_dim=head_dim, nblocks=nblocks)
    queries, local, running = pl.pallas_call(
        local_kernel,
        grid_spec=pltpu.PrefetchScalarGridSpec(
            num_scalar_prefetch=1,
            grid=(heads // hg,),
            in_specs=[row_spec, pl.BlockSpec((1, 3, cw), lambda i, r: (0, 0, i))],
            out_specs=[row_spec, row_spec, run_spec],
        ),
        out_shape=[
            jax.ShapeDtypeStruct(rows.shape, jnp.bfloat16),
            jax.ShapeDtypeStruct(rows.shape, jnp.float32),
            jax.ShapeDtypeStruct((nblocks - 1, heads, head_dim, head_dim), jnp.float32),
        ],
        cost_estimate=pl.CostEstimate(
            flops=6 * count * BLOCK * width, transcendentals=3 * count * width,
            bytes_accessed=count * width * 8,
        ),
    )(rates, rows, gains)
    final_kernel = functools.partial(_final_kernel, hg=hg, head_dim=head_dim, nblocks=nblocks)
    return pl.pallas_call(
        final_kernel,
        grid_spec=pltpu.PrefetchScalarGridSpec(
            num_scalar_prefetch=1,
            grid=(heads // hg,),
            in_specs=[
                row_spec, row_spec, row_spec, run_spec,
                pl.BlockSpec((hg, head_dim, head_dim), lambda i, r: (i, 0, 0)),
                pl.BlockSpec((1, cw), lambda i, r: (0, i)),
            ],
            out_specs=row_spec,
        ),
        out_shape=jax.ShapeDtypeStruct(rows.shape, rows.dtype),
        cost_estimate=pl.CostEstimate(
            flops=2 * count * width * head_dim, transcendentals=count * width,
            bytes_accessed=count * width * 10,
        ),
    )(rates, rows, queries, local, running, states, gain_out)


def on_device(section_inputs, input_gains, out_gain, decay_rates, carry_state):
    _, count, width = section_inputs.shape
    rates = decay_rates[0]
    heads = rates.shape[0]
    head_dim = width // heads
    group_size = lax.axis_size("ctx")
    own_heads = heads // group_size
    place = lax.axis_index("ctx")
    count_s = lax.axis_size("section")
    pairs = [(src, (src + 1) % count_s) for src in range(count_s)]

    prev_rows = lax.ppermute(section_inputs, "section", pairs)
    prev_gains, prev_gain_out, prev_rates = lax.ppermute(
        (input_gains, out_gain, decay_rates), "section", pairs
    )

    summary = _summaries(rates, section_inputs, input_gains, head_dim)
    gathered = lax.all_to_all(summary, "ctx", 0, 0, tiled=True)
    gathered = gathered.astype(jnp.float32).reshape(group_size, own_heads, head_dim, head_dim)

    start = place * own_heads
    carry_part = lax.dynamic_slice_in_dim(carry_state[0], start, own_heads, 0)
    rate_part = lax.dynamic_slice_in_dim(rates, start, own_heads, 0)
    target = jnp.arange(group_size + 1)[:, None]
    source = jnp.arange(group_size)[None, :]
    gap = (target - 1 - source).astype(jnp.float32)
    weights = jnp.where(
        (source < target)[:, :, None],
        jnp.exp(-rate_part[None, None, :] * count * jnp.maximum(gap, 0.0)[:, :, None]),
        0.0,
    )
    carry_weights = jnp.exp(-rate_part[None, :] * count * target.astype(jnp.float32))
    prefixes = jnp.einsum(
        "tsh,shde->thde", weights, gathered, precision=lax.Precision.HIGHEST
    ) + carry_weights[:, :, None, None] * carry_part[None]
    end_part = prefixes[group_size]
    incoming = lax.all_to_all(
        prefixes[:group_size].astype(jnp.bfloat16).reshape(heads, head_dim, head_dim),
        "ctx", 0, 0, tiled=True,
    )
    prev_incoming = lax.ppermute(incoming, "section", pairs)

    next_rows = _outputs(
        prev_rates[0], prev_rows, prev_gains, prev_gain_out, prev_incoming, head_dim
    )
    return (next_rows, end_part[None])


def solution(mesh):
    return jax.shard_map(
        on_device,
        mesh=mesh,
        in_specs=(
            P("section", "ctx", None),
            P("section", None, None),
            P("section", None),
            P("section", None),
            P("section", None, None, None),
        ),
        out_specs=(P("section", "ctx", None), P("section", "ctx", None, None)),
        check_vma=False,
    )
```

```python
import functools

import jax
import jax.numpy as jnp
from jax import lax
from jax.experimental import pallas as pl
from jax.experimental.pallas import tpu as pltpu
from jax.sharding import PartitionSpec as P

BLOCK = 256
EPSILON = 1e-05
HEADS_PER_STEP = 4
STATE_CHUNKS = 4


def _silu(v):
    return v / (1.0 + jnp.exp(-v))


def _dot_nt(a, b):
    return lax.dot_general(a, b, (((1,), (1,)), ((), ())), preferred_element_type=jnp.float32)


def _dot_tn(a, b):
    return lax.dot_general(a, b, (((0,), (0,)), ((), ())), preferred_element_type=jnp.float32)


def _dot(a, b):
    return lax.dot_general(a, b, (((1,), (0,)), ((), ())), preferred_element_type=jnp.float32)


def _block_state(keys_b, values_b, rate, pos):
    tail = jnp.exp(-rate * (BLOCK - 1 - pos))
    scaled = (keys_b.astype(jnp.float32) * tail).astype(jnp.bfloat16)
    return _dot_tn(scaled, values_b)


def _summary_kernel(rates_ref, x_ref, g_ref, o_ref, *, hg, head_dim, nblocks):
    step = pl.program_id(0)
    pos = lax.broadcasted_iota(jnp.int32, (BLOCK, 1), 0).astype(jnp.float32)
    for hh in range(hg):
        rate = jnp.full((1, 1), rates_ref[step * hg + hh], jnp.float32)
        cols = slice(hh * head_dim, (hh + 1) * head_dim)
        decay = jnp.exp(-rate * BLOCK)
        acc = None
        for b in range(nblocks):
            rows = slice(b * BLOCK, (b + 1) * BLOCK)
            x = x_ref[0, rows, cols].astype(jnp.float32)
            keys_b = (_silu(x * g_ref[0, 1:2, cols]) * head_dim ** (-0.5)).astype(jnp.bfloat16)
            values_b = (x * g_ref[0, 2:3, cols]).astype(jnp.bfloat16)
            update = _block_state(keys_b, values_b, rate, pos)
            acc = update if acc is None else decay * acc + update
        o_ref[hh] = acc.astype(o_ref.dtype)


def _output_kernel(rates_ref, x_ref, g_ref, go_ref, s_ref, *rest, hg, head_dim, nblocks, first):
    o_ref = rest[-1]
    step = pl.program_id(0) + first
    pos = lax.broadcasted_iota(jnp.int32, (BLOCK, 1), 0).astype(jnp.float32)
    row = lax.broadcasted_iota(jnp.int32, (BLOCK, BLOCK), 0)
    col = lax.broadcasted_iota(jnp.int32, (BLOCK, BLOCK), 1)
    offset = (row - col).astype(jnp.float32)
    causal = row >= col
    for hh in range(hg):
        rate = jnp.full((1, 1), rates_ref[step * hg + hh], jnp.float32)
        cols = slice(hh * head_dim, (hh + 1) * head_dim)
        mask = jnp.where(causal, jnp.exp(-rate * jnp.maximum(offset, 0.0)), 0.0)
        lead = jnp.exp(-rate * (pos + 1.0))
        decay = jnp.exp(-rate * BLOCK)
        state = s_ref[hh].astype(jnp.float32)
        for b in range(nblocks):
            rows = slice(b * BLOCK, (b + 1) * BLOCK)
            x = x_ref[0, rows, cols].astype(jnp.float32)
            queries_b = _silu(x * g_ref[0, 0:1, cols]).astype(jnp.bfloat16)
            keys_b = (_silu(x * g_ref[0, 1:2, cols]) * head_dim ** (-0.5)).astype(jnp.bfloat16)
            values_b = (x * g_ref[0, 2:3, cols]).astype(jnp.bfloat16)
            scores = _dot_nt(queries_b, keys_b)
            weights = (scores * mask).astype(jnp.bfloat16)
            local = _dot(weights, values_b)
            cross = _dot(queries_b, state.astype(jnp.bfloat16))
            total = local + lead * cross
            normed = total * lax.rsqrt(jnp.mean(total * total, axis=-1, keepdims=True) + EPSILON)
            o_ref[0, rows, cols] = (x + normed * go_ref[0:1, cols]).astype(o_ref.dtype)
            if b + 1 < nblocks:
                state = decay * state + _block_state(keys_b, values_b, rate, pos)


def _summaries(rates, rows, gains, head_dim):
    _, count, width = rows.shape
    heads = width // head_dim
    hg = HEADS_PER_STEP
    cw = hg * head_dim
    kernel = functools.partial(_summary_kernel, hg=hg, head_dim=head_dim, nblocks=count // BLOCK)
    return pl.pallas_call(
        kernel,
        grid_spec=pltpu.PrefetchScalarGridSpec(
            num_scalar_prefetch=1,
            grid=(heads // hg,),
            in_specs=[
                pl.BlockSpec((1, count, cw), lambda i, r: (0, 0, i)),
                pl.BlockSpec((1, 3, cw), lambda i, r: (0, 0, i)),
            ],
            out_specs=pl.BlockSpec((hg, head_dim, head_dim), lambda i, r: (i, 0, 0)),
        ),
        out_shape=jax.ShapeDtypeStruct((heads, head_dim, head_dim), jnp.bfloat16),
        cost_estimate=pl.CostEstimate(
            flops=2 * count * width * head_dim, transcendentals=count * width,
            bytes_accessed=count * width * 2 + heads * head_dim * head_dim * 4,
        ),
    )(rates, rows, gains)


def _outputs(rates, rows, gains, gain_out, states, head_dim, first, previous):
    _, count, width = rows.shape
    hg = HEADS_PER_STEP
    cw = hg * head_dim
    steps = states.shape[0] // hg
    base = first // hg
    kernel = functools.partial(
        _output_kernel, hg=hg, head_dim=head_dim, nblocks=count // BLOCK, first=base
    )
    row_spec = pl.BlockSpec((1, count, cw), lambda i, r: (0, 0, i + base))
    in_specs = [
        row_spec,
        pl.BlockSpec((1, 3, cw), lambda i, r: (0, 0, i + base)),
        pl.BlockSpec((1, cw), lambda i, r: (0, i + base)),
        pl.BlockSpec((hg, head_dim, head_dim), lambda i, r: (i, 0, 0)),
    ]
    operands = [rates, rows, gains, gain_out, states]
    aliases = {}
    if previous is not None:
        in_specs.append(pl.BlockSpec(memory_space=pl.ANY))
        operands.append(previous)
        aliases = {len(operands) - 1: 0}
    share = steps * cw
    return pl.pallas_call(
        kernel,
        grid_spec=pltpu.PrefetchScalarGridSpec(
            num_scalar_prefetch=1,
            grid=(steps,),
            in_specs=in_specs,
            out_specs=row_spec,
        ),
        out_shape=jax.ShapeDtypeStruct(rows.shape, rows.dtype),
        input_output_aliases=aliases,
        cost_estimate=pl.CostEstimate(
            flops=8 * count * BLOCK * share, transcendentals=3 * count * share,
            bytes_accessed=2 * count * share * 2 + steps * hg * head_dim * head_dim * 2,
        ),
    )(*operands)


def on_device(section_inputs, input_gains, out_gain, decay_rates, carry_state):
    _, count, width = section_inputs.shape
    rates = decay_rates[0]
    heads = rates.shape[0]
    head_dim = width // heads
    group_size = lax.axis_size("ctx")
    own_heads = heads // group_size
    place = lax.axis_index("ctx")
    count_s = lax.axis_size("section")
    pairs = [(src, (src + 1) % count_s) for src in range(count_s)]

    prev_rows, prev_gains, prev_gain_out, prev_rates = lax.ppermute(
        (section_inputs, input_gains, out_gain, decay_rates), "section", pairs
    )

    summary = _summaries(rates, section_inputs, input_gains, head_dim)
    gathered = lax.all_to_all(summary, "ctx", 0, 0, tiled=True)
    gathered = gathered.astype(jnp.float32).reshape(group_size, own_heads, head_dim, head_dim)

    start = place * own_heads
    carry_part = lax.dynamic_slice_in_dim(carry_state[0], start, own_heads, 0)
    rate_part = lax.dynamic_slice_in_dim(rates, start, own_heads, 0)
    target = jnp.arange(group_size + 1)[:, None]
    source = jnp.arange(group_size)[None, :]
    gap = (target - 1 - source).astype(jnp.float32)
    weights = jnp.where(
        (source < target)[:, :, None],
        jnp.exp(-rate_part[None, None, :] * count * jnp.maximum(gap, 0.0)[:, :, None]),
        0.0,
    )
    carry_weights = jnp.exp(-rate_part[None, :] * count * target.astype(jnp.float32))
    prefixes = jnp.einsum(
        "tsh,shde->thde", weights, gathered, precision=lax.Precision.HIGHEST
    ) + carry_weights[:, :, None, None] * carry_part[None]
    end_part = prefixes[group_size]
    incoming = lax.all_to_all(
        prefixes[:group_size].astype(jnp.bfloat16).reshape(heads, head_dim, head_dim),
        "ctx", 0, 0, tiled=True,
    )
    prev_gains, prev_gain_out, prev_rates, incoming = lax.optimization_barrier(
        (prev_gains, prev_gain_out, prev_rates, incoming)
    )
    chunk = heads // STATE_CHUNKS
    next_rows = None
    for part in range(STATE_CHUNKS):
        piece = lax.ppermute(incoming[part * chunk : (part + 1) * chunk], "section", pairs)
        next_rows = _outputs(
            prev_rates[0], prev_rows, prev_gains, prev_gain_out, piece, head_dim,
            part * chunk, next_rows,
        )
    return (next_rows, end_part[None])


def solution(mesh):
    return jax.shard_map(
        on_device,
        mesh=mesh,
        in_specs=(
            P("section", "ctx", None),
            P("section", None, None),
            P("section", None),
            P("section", None),
            P("section", None, None, None),
        ),
        out_specs=(P("section", "ctx", None), P("section", "ctx", None, None)),
        check_vma=False,
    )
```

```python
import functools

import jax
import jax.numpy as jnp
from jax import lax
from jax.experimental import pallas as pl
from jax.experimental.pallas import tpu as pltpu
from jax.sharding import PartitionSpec as P

BLOCK = 256
EPSILON = 1e-05
HEADS_PER_STEP = 4
STATE_CHUNKS = 4


def _silu(v):
    return 0.5 * v * (1.0 + jnp.tanh(0.5 * v))


def _dot_nt(a, b):
    return lax.dot_general(a, b, (((1,), (1,)), ((), ())), preferred_element_type=jnp.float32)


def _dot_tn(a, b):
    return lax.dot_general(a, b, (((0,), (0,)), ((), ())), preferred_element_type=jnp.float32)


def _dot(a, b):
    return lax.dot_general(a, b, (((1,), (0,)), ((), ())), preferred_element_type=jnp.float32)


def _block_state(keys_b, values_b, rate, pos):
    tail = jnp.exp(-rate * (BLOCK - 1 - pos))
    scaled = (keys_b.astype(jnp.float32) * tail).astype(jnp.bfloat16)
    return _dot_tn(scaled, values_b)


def _summary_kernel(rates_ref, x_ref, g_ref, o_ref, *, hg, head_dim, nblocks):
    step = pl.program_id(0)
    pos = lax.broadcasted_iota(jnp.int32, (BLOCK, 1), 0).astype(jnp.float32)
    for hh in range(hg):
        rate = jnp.full((1, 1), rates_ref[step * hg + hh], jnp.float32)
        cols = slice(hh * head_dim, (hh + 1) * head_dim)
        decay = jnp.exp(-rate * BLOCK)
        acc = None
        for b in range(nblocks):
            rows = slice(b * BLOCK, (b + 1) * BLOCK)
            x = x_ref[0, rows, cols].astype(jnp.float32)
            keys_b = (_silu(x * g_ref[0, 1:2, cols]) * head_dim ** (-0.5)).astype(jnp.bfloat16)
            values_b = (x * g_ref[0, 2:3, cols]).astype(jnp.bfloat16)
            update = _block_state(keys_b, values_b, rate, pos)
            acc = update if acc is None else decay * acc + update
        o_ref[hh] = acc.astype(o_ref.dtype)


def _output_kernel(rates_ref, x_ref, g_ref, go_ref, s_ref, *rest, hg, head_dim, nblocks, first):
    o_ref = rest[-1]
    step = pl.program_id(0) + first
    pos = lax.broadcasted_iota(jnp.int32, (BLOCK, 1), 0).astype(jnp.float32)
    pos_row = lax.broadcasted_iota(jnp.int32, (1, BLOCK), 1).astype(jnp.float32)
    row = lax.broadcasted_iota(jnp.int32, (BLOCK, BLOCK), 0)
    col = lax.broadcasted_iota(jnp.int32, (BLOCK, BLOCK), 1)
    causal = row >= col
    for hh in range(hg):
        rate = jnp.full((1, 1), rates_ref[step * hg + hh], jnp.float32)
        cols = slice(hh * head_dim, (hh + 1) * head_dim)
        lead = jnp.exp(-rate * (pos + 1.0))
        mask = jnp.where(causal, lead * jnp.exp(rate * (pos_row + 1.0)), 0.0)
        decay = jnp.exp(-rate * BLOCK)
        state = s_ref[hh].astype(jnp.float32)
        for b in range(nblocks):
            rows = slice(b * BLOCK, (b + 1) * BLOCK)
            x = x_ref[0, rows, cols].astype(jnp.float32)
            queries_b = _silu(x * g_ref[0, 0:1, cols]).astype(jnp.bfloat16)
            keys_b = (_silu(x * g_ref[0, 1:2, cols]) * head_dim ** (-0.5)).astype(jnp.bfloat16)
            values_b = (x * g_ref[0, 2:3, cols]).astype(jnp.bfloat16)
            scores = _dot_nt(queries_b, keys_b)
            weights = (scores * mask).astype(jnp.bfloat16)
            local = _dot(weights, values_b)
            cross = _dot(queries_b, state.astype(jnp.bfloat16))
            total = local + lead * cross
            normed = total * lax.rsqrt(jnp.mean(total * total, axis=-1, keepdims=True) + EPSILON)
            o_ref[0, rows, cols] = (x + normed * go_ref[0:1, cols]).astype(o_ref.dtype)
            if b + 1 < nblocks:
                state = decay * state + _block_state(keys_b, values_b, rate, pos)


def _summaries(rates, rows, gains, head_dim):
    _, count, width = rows.shape
    heads = width // head_dim
    hg = HEADS_PER_STEP
    cw = hg * head_dim
    kernel = functools.partial(_summary_kernel, hg=hg, head_dim=head_dim, nblocks=count // BLOCK)
    return pl.pallas_call(
        kernel,
        grid_spec=pltpu.PrefetchScalarGridSpec(
            num_scalar_prefetch=1,
            grid=(heads // hg,),
            in_specs=[
                pl.BlockSpec((1, count, cw), lambda i, r: (0, 0, i)),
                pl.BlockSpec((1, 3, cw), lambda i, r: (0, 0, i)),
            ],
            out_specs=pl.BlockSpec((hg, head_dim, head_dim), lambda i, r: (i, 0, 0)),
        ),
        out_shape=jax.ShapeDtypeStruct((heads, head_dim, head_dim), jnp.bfloat16),
        cost_estimate=pl.CostEstimate(
            flops=2 * count * width * head_dim, transcendentals=count * width,
            bytes_accessed=count * width * 2 + heads * head_dim * head_dim * 4,
        ),
    )(rates, rows, gains)


def _outputs(rates, rows, gains, gain_out, states, head_dim, first, previous):
    _, count, width = rows.shape
    hg = HEADS_PER_STEP
    cw = hg * head_dim
    steps = states.shape[0] // hg
    base = first // hg
    kernel = functools.partial(
        _output_kernel, hg=hg, head_dim=head_dim, nblocks=count // BLOCK, first=base
    )
    row_spec = pl.BlockSpec((1, count, cw), lambda i, r: (0, 0, i + base))
    in_specs = [
        row_spec,
        pl.BlockSpec((1, 3, cw), lambda i, r: (0, 0, i + base)),
        pl.BlockSpec((1, cw), lambda i, r: (0, i + base)),
        pl.BlockSpec((hg, head_dim, head_dim), lambda i, r: (i, 0, 0)),
    ]
    operands = [rates, rows, gains, gain_out, states]
    aliases = {}
    if previous is not None:
        in_specs.append(pl.BlockSpec(memory_space=pl.ANY))
        operands.append(previous)
        aliases = {len(operands) - 1: 0}
    share = steps * cw
    return pl.pallas_call(
        kernel,
        grid_spec=pltpu.PrefetchScalarGridSpec(
            num_scalar_prefetch=1,
            grid=(steps,),
            in_specs=in_specs,
            out_specs=row_spec,
        ),
        out_shape=jax.ShapeDtypeStruct(rows.shape, rows.dtype),
        input_output_aliases=aliases,
        cost_estimate=pl.CostEstimate(
            flops=8 * count * BLOCK * share, transcendentals=3 * count * share,
            bytes_accessed=2 * count * share * 2 + steps * hg * head_dim * head_dim * 2,
        ),
    )(*operands)


def on_device(section_inputs, input_gains, out_gain, decay_rates, carry_state):
    _, count, width = section_inputs.shape
    rates = decay_rates[0]
    heads = rates.shape[0]
    head_dim = width // heads
    group_size = lax.axis_size("ctx")
    own_heads = heads // group_size
    place = lax.axis_index("ctx")
    count_s = lax.axis_size("section")
    pairs = [(src, (src + 1) % count_s) for src in range(count_s)]

    prev_rows, prev_gains, prev_gain_out, prev_rates = lax.ppermute(
        (section_inputs, input_gains, out_gain, decay_rates), "section", pairs
    )

    summary = _summaries(rates, section_inputs, input_gains, head_dim)
    gathered = lax.all_to_all(summary, "ctx", 0, 0, tiled=True)
    gathered = gathered.astype(jnp.float32).reshape(group_size, own_heads, head_dim, head_dim)

    start = place * own_heads
    carry_part = lax.dynamic_slice_in_dim(carry_state[0], start, own_heads, 0)
    rate_part = lax.dynamic_slice_in_dim(rates, start, own_heads, 0)
    target = jnp.arange(group_size)[:, None]
    source = jnp.arange(group_size)[None, :]
    gap = (target - 1 - source).astype(jnp.float32)
    weights = jnp.where(
        (source < target)[:, :, None],
        jnp.exp(-rate_part[None, None, :] * count * jnp.maximum(gap, 0.0)[:, :, None]),
        0.0,
    )
    carry_weights = jnp.exp(-rate_part[None, :] * count * target.astype(jnp.float32))
    prefixes = jnp.einsum(
        "tsh,shde->thde", weights, gathered, precision=lax.Precision.HIGHEST
    ) + carry_weights[:, :, None, None] * carry_part[None]
    end_weights = jnp.exp(
        -rate_part[None, :] * count * (group_size - 1 - source[0]).astype(jnp.float32)[:, None]
    )
    end_part = jnp.einsum(
        "sh,shde->hde", end_weights, gathered, precision=lax.Precision.HIGHEST
    ) + jnp.exp(-rate_part * count * group_size)[:, None, None] * carry_part
    incoming = lax.all_to_all(
        prefixes.astype(jnp.bfloat16).reshape(heads, head_dim, head_dim),
        "ctx", 0, 0, tiled=True,
    )
    prev_gains, prev_gain_out, prev_rates, incoming = lax.optimization_barrier(
        (prev_gains, prev_gain_out, prev_rates, incoming)
    )
    chunk = heads // STATE_CHUNKS
    next_rows = None
    for part in range(STATE_CHUNKS):
        piece = lax.ppermute(incoming[part * chunk : (part + 1) * chunk], "section", pairs)
        next_rows = _outputs(
            prev_rates[0], prev_rows, prev_gains, prev_gain_out, piece, head_dim,
            part * chunk, next_rows,
        )
    return (next_rows, end_part[None])


def solution(mesh):
    return jax.shard_map(
        on_device,
        mesh=mesh,
        in_specs=(
            P("section", "ctx", None),
            P("section", None, None),
            P("section", None),
            P("section", None),
            P("section", None, None, None),
        ),
        out_specs=(P("section", "ctx", None), P("section", "ctx", None, None)),
        check_vma=False,
    )
```

```python
import functools

import jax
import jax.numpy as jnp
from jax import lax
from jax.experimental import pallas as pl
from jax.experimental.pallas import tpu as pltpu
from jax.sharding import PartitionSpec as P

BLOCK = 256
EPSILON = 1e-05
HEADS_PER_STEP = 4
STATE_CHUNKS = 4


def _silu(v):
    return 0.5 * v * (1.0 + jnp.tanh(0.5 * v))


def _dot_nt(a, b):
    return lax.dot_general(a, b, (((1,), (1,)), ((), ())), preferred_element_type=jnp.float32)


def _dot_tn(a, b):
    return lax.dot_general(a, b, (((0,), (0,)), ((), ())), preferred_element_type=jnp.float32)


def _dot(a, b):
    return lax.dot_general(a, b, (((1,), (0,)), ((), ())), preferred_element_type=jnp.float32)


def _block_state(keys_b, values_b, rate, pos):
    tail = jnp.exp(-rate * (BLOCK - 1 - pos))
    scaled = (keys_b.astype(jnp.float32) * tail).astype(jnp.bfloat16)
    return _dot_tn(scaled, values_b)


def _summary_kernel(rates_ref, x_ref, g_ref, o_ref, *, hg, head_dim, nblocks):
    step = pl.program_id(0)
    pos = lax.broadcasted_iota(jnp.int32, (BLOCK, 1), 0).astype(jnp.float32)
    for hh in range(hg):
        rate = jnp.full((1, 1), rates_ref[step * hg + hh], jnp.float32)
        cols = slice(hh * head_dim, (hh + 1) * head_dim)
        decay = jnp.exp(-rate * BLOCK)
        acc = None
        for b in range(nblocks):
            rows = slice(b * BLOCK, (b + 1) * BLOCK)
            x = x_ref[0, rows, cols].astype(jnp.float32)
            keys_b = (_silu(x * g_ref[0, 1:2, cols]) * head_dim ** (-0.5)).astype(jnp.bfloat16)
            values_b = (x * g_ref[0, 2:3, cols]).astype(jnp.bfloat16)
            update = _block_state(keys_b, values_b, rate, pos)
            acc = update if acc is None else decay * acc + update
        o_ref[hh] = acc.astype(o_ref.dtype)


def _local_kernel(rates_ref, x_ref, g_ref, q_ref, l_ref, r_ref, *, hg, head_dim, nblocks):
    step = pl.program_id(0)
    pos = lax.broadcasted_iota(jnp.int32, (BLOCK, 1), 0).astype(jnp.float32)
    pos_row = lax.broadcasted_iota(jnp.int32, (1, BLOCK), 1).astype(jnp.float32)
    row = lax.broadcasted_iota(jnp.int32, (BLOCK, BLOCK), 0)
    col = lax.broadcasted_iota(jnp.int32, (BLOCK, BLOCK), 1)
    causal = row >= col
    for hh in range(hg):
        rate = jnp.full((1, 1), rates_ref[step * hg + hh], jnp.float32)
        cols = slice(hh * head_dim, (hh + 1) * head_dim)
        lead = jnp.exp(-rate * (pos + 1.0))
        mask = jnp.where(causal, lead * jnp.exp(rate * (pos_row + 1.0)), 0.0)
        decay = jnp.exp(-rate * BLOCK)
        running = None
        for b in range(nblocks):
            rows = slice(b * BLOCK, (b + 1) * BLOCK)
            x = x_ref[0, rows, cols].astype(jnp.float32)
            queries_b = _silu(x * g_ref[0, 0:1, cols]).astype(jnp.bfloat16)
            keys_b = (_silu(x * g_ref[0, 1:2, cols]) * head_dim ** (-0.5)).astype(jnp.bfloat16)
            values_b = (x * g_ref[0, 2:3, cols]).astype(jnp.bfloat16)
            scores = _dot_nt(queries_b, keys_b)
            weights = (scores * mask).astype(jnp.bfloat16)
            q_ref[0, rows, cols] = queries_b
            l_ref[0, rows, cols] = _dot(weights, values_b)
            if b + 1 < nblocks:
                update = _block_state(keys_b, values_b, rate, pos)
                running = update if running is None else decay * running + update
                r_ref[b, hh] = running


def _final_kernel(rates_ref, x_ref, q_ref, l_ref, r_ref, s_ref, go_ref, *rest, hg, head_dim, nblocks, first):
    o_ref = rest[-1]
    step = pl.program_id(0) + first
    pos = lax.broadcasted_iota(jnp.int32, (BLOCK, 1), 0).astype(jnp.float32)
    for hh in range(hg):
        rate = jnp.full((1, 1), rates_ref[step * hg + hh], jnp.float32)
        cols = slice(hh * head_dim, (hh + 1) * head_dim)
        lead = jnp.exp(-rate * (pos + 1.0))
        decay_b = jnp.ones_like(rate)
        entering = s_ref[hh].astype(jnp.float32)
        for b in range(nblocks):
            rows = slice(b * BLOCK, (b + 1) * BLOCK)
            if b == 0:
                state = entering
            else:
                decay_b = decay_b * jnp.exp(-rate * BLOCK)
                state = decay_b * entering + r_ref[b - 1, hh]
            cross = _dot(q_ref[0, rows, cols], state.astype(jnp.bfloat16))
            total = l_ref[0, rows, cols] + lead * cross
            normed = total * lax.rsqrt(jnp.mean(total * total, axis=-1, keepdims=True) + EPSILON)
            x = x_ref[0, rows, cols].astype(jnp.float32)
            o_ref[0, rows, cols] = (x + normed * go_ref[0:1, cols]).astype(o_ref.dtype)


def _summaries(rates, rows, gains, head_dim):
    _, count, width = rows.shape
    heads = width // head_dim
    hg = HEADS_PER_STEP
    cw = hg * head_dim
    kernel = functools.partial(_summary_kernel, hg=hg, head_dim=head_dim, nblocks=count // BLOCK)
    return pl.pallas_call(
        kernel,
        grid_spec=pltpu.PrefetchScalarGridSpec(
            num_scalar_prefetch=1,
            grid=(heads // hg,),
            in_specs=[
                pl.BlockSpec((1, count, cw), lambda i, r: (0, 0, i)),
                pl.BlockSpec((1, 3, cw), lambda i, r: (0, 0, i)),
            ],
            out_specs=pl.BlockSpec((hg, head_dim, head_dim), lambda i, r: (i, 0, 0)),
        ),
        out_shape=jax.ShapeDtypeStruct((heads, head_dim, head_dim), jnp.bfloat16),
        cost_estimate=pl.CostEstimate(
            flops=2 * count * width * head_dim, transcendentals=count * width,
            bytes_accessed=count * width * 2 + heads * head_dim * head_dim * 4,
        ),
    )(rates, rows, gains)


def _local_part(rates, rows, gains, head_dim):
    _, count, width = rows.shape
    heads = width // head_dim
    hg = HEADS_PER_STEP
    cw = hg * head_dim
    nblocks = count // BLOCK
    row_spec = pl.BlockSpec((1, count, cw), lambda i, r: (0, 0, i))
    run_spec = pl.BlockSpec((nblocks - 1, hg, head_dim, head_dim), lambda i, r: (0, i, 0, 0))
    kernel = functools.partial(_local_kernel, hg=hg, head_dim=head_dim, nblocks=nblocks)
    return pl.pallas_call(
        kernel,
        grid_spec=pltpu.PrefetchScalarGridSpec(
            num_scalar_prefetch=1,
            grid=(heads // hg,),
            in_specs=[row_spec, pl.BlockSpec((1, 3, cw), lambda i, r: (0, 0, i))],
            out_specs=[row_spec, row_spec, run_spec],
        ),
        out_shape=[
            jax.ShapeDtypeStruct(rows.shape, jnp.bfloat16),
            jax.ShapeDtypeStruct(rows.shape, jnp.float32),
            jax.ShapeDtypeStruct((nblocks - 1, heads, head_dim, head_dim), jnp.float32),
        ],
        cost_estimate=pl.CostEstimate(
            flops=6 * count * BLOCK * width, transcendentals=3 * count * width,
            bytes_accessed=count * width * 8,
        ),
    )(rates, rows, gains)


def _outputs(rates, rows, queries, local, running, gain_out, states, head_dim, first, previous):
    _, count, width = rows.shape
    hg = HEADS_PER_STEP
    cw = hg * head_dim
    nblocks = count // BLOCK
    steps = states.shape[0] // hg
    base = first // hg
    kernel = functools.partial(
        _final_kernel, hg=hg, head_dim=head_dim, nblocks=nblocks, first=base
    )
    row_spec = pl.BlockSpec((1, count, cw), lambda i, r: (0, 0, i + base))
    in_specs = [
        row_spec, row_spec, row_spec,
        pl.BlockSpec((nblocks - 1, hg, head_dim, head_dim), lambda i, r: (0, i + base, 0, 0)),
        pl.BlockSpec((hg, head_dim, head_dim), lambda i, r: (i, 0, 0)),
        pl.BlockSpec((1, cw), lambda i, r: (0, i + base)),
    ]
    operands = [rates, rows, queries, local, running, states, gain_out]
    aliases = {}
    if previous is not None:
        in_specs.append(pl.BlockSpec(memory_space=pl.ANY))
        operands.append(previous)
        aliases = {len(operands) - 1: 0}
    share = steps * cw
    return pl.pallas_call(
        kernel,
        grid_spec=pltpu.PrefetchScalarGridSpec(
            num_scalar_prefetch=1,
            grid=(steps,),
            in_specs=in_specs,
            out_specs=row_spec,
        ),
        out_shape=jax.ShapeDtypeStruct(rows.shape, rows.dtype),
        input_output_aliases=aliases,
        cost_estimate=pl.CostEstimate(
            flops=2 * count * share * head_dim, transcendentals=count * share,
            bytes_accessed=count * share * 10,
        ),
    )(*operands)


def on_device(section_inputs, input_gains, out_gain, decay_rates, carry_state):
    _, count, width = section_inputs.shape
    rates = decay_rates[0]
    heads = rates.shape[0]
    head_dim = width // heads
    group_size = lax.axis_size("ctx")
    own_heads = heads // group_size
    place = lax.axis_index("ctx")
    count_s = lax.axis_size("section")
    pairs = [(src, (src + 1) % count_s) for src in range(count_s)]

    prev_gains, prev_gain_out, prev_rates = lax.ppermute(
        (input_gains, out_gain, decay_rates), "section", pairs
    )
    sent, prev_gains, prev_gain_out, prev_rates = lax.optimization_barrier(
        (section_inputs, prev_gains, prev_gain_out, prev_rates)
    )
    prev_rows = lax.ppermute(sent, "section", pairs)

    summary = _summaries(rates, section_inputs, input_gains, head_dim)
    gathered = lax.all_to_all(summary, "ctx", 0, 0, tiled=True)
    gathered = gathered.astype(jnp.float32).reshape(group_size, own_heads, head_dim, head_dim)

    start = place * own_heads
    carry_part = lax.dynamic_slice_in_dim(carry_state[0], start, own_heads, 0)
    rate_part = lax.dynamic_slice_in_dim(rates, start, own_heads, 0)
    target = jnp.arange(group_size)[:, None]
    source = jnp.arange(group_size)[None, :]
    gap = (target - 1 - source).astype(jnp.float32)
    weights = jnp.where(
        (source < target)[:, :, None],
        jnp.exp(-rate_part[None, None, :] * count * jnp.maximum(gap, 0.0)[:, :, None]),
        0.0,
    )
    carry_weights = jnp.exp(-rate_part[None, :] * count * target.astype(jnp.float32))
    prefixes = jnp.einsum(
        "tsh,shde->thde", weights, gathered, precision=lax.Precision.HIGHEST
    ) + carry_weights[:, :, None, None] * carry_part[None]
    end_weights = jnp.exp(
        -rate_part[None, :] * count * (group_size - 1 - source[0]).astype(jnp.float32)[:, None]
    )
    end_part = jnp.einsum(
        "sh,shde->hde", end_weights, gathered, precision=lax.Precision.HIGHEST
    ) + jnp.exp(-rate_part * count * group_size)[:, None, None] * carry_part
    queries, local, running = _local_part(prev_rates[0], prev_rows, prev_gains, head_dim)
    incoming = lax.all_to_all(
        prefixes.astype(jnp.bfloat16).reshape(heads, head_dim, head_dim),
        "ctx", 0, 0, tiled=True,
    )
    incoming, queries, local, running = lax.optimization_barrier((incoming, queries, local, running))
    chunk = heads // STATE_CHUNKS
    next_rows = None
    for part in range(STATE_CHUNKS):
        piece = lax.ppermute(incoming[part * chunk : (part + 1) * chunk], "section", pairs)
        next_rows = _outputs(
            prev_rates[0], prev_rows, queries, local, running, prev_gain_out, piece, head_dim,
            part * chunk, next_rows,
        )
    return (next_rows, end_part[None])


def solution(mesh):
    return jax.shard_map(
        on_device,
        mesh=mesh,
        in_specs=(
            P("section", "ctx", None),
            P("section", None, None),
            P("section", None),
            P("section", None),
            P("section", None, None, None),
        ),
        out_specs=(P("section", "ctx", None), P("section", "ctx", None, None)),
        check_vma=False,
    )
```

```python
import functools

import jax
import jax.numpy as jnp
from jax import lax
from jax.experimental import pallas as pl
from jax.experimental.pallas import tpu as pltpu
from jax.sharding import PartitionSpec as P

BLOCK = 256
EPSILON = 1e-05
HEADS_PER_STEP = 4
STATE_CHUNKS = 4


def _silu_half(u):
    return u + u * jnp.tanh(u)


def _row_mean(v):
    ones = jnp.full((v.shape[-1], v.shape[-1]), 1.0 / v.shape[-1], jnp.float32)
    return lax.dot_general(
        v, ones, (((1,), (0,)), ((), ())),
        precision=lax.Precision.HIGHEST, preferred_element_type=jnp.float32,
    )


def _dot_nt(a, b):
    return lax.dot_general(a, b, (((1,), (1,)), ((), ())), preferred_element_type=jnp.float32)


def _dot_tn(a, b):
    return lax.dot_general(a, b, (((0,), (0,)), ((), ())), preferred_element_type=jnp.float32)


def _dot(a, b):
    return lax.dot_general(a, b, (((1,), (0,)), ((), ())), preferred_element_type=jnp.float32)


def _block_state(keys_b, values_b, rate, pos):
    tail = jnp.exp(-rate * (BLOCK - 1 - pos))
    scaled = (keys_b.astype(jnp.float32) * tail).astype(jnp.bfloat16)
    return _dot_tn(scaled, values_b)


def _summary_kernel(rates_ref, x_ref, g_ref, o_ref, *, hg, head_dim, nblocks):
    step = pl.program_id(0)
    pos = lax.broadcasted_iota(jnp.int32, (BLOCK, 1), 0).astype(jnp.float32)
    for hh in range(hg):
        rate = jnp.full((1, 1), rates_ref[step * hg + hh], jnp.float32)
        cols = slice(hh * head_dim, (hh + 1) * head_dim)
        decay = jnp.exp(-rate * BLOCK)
        half_k = 0.5 * g_ref[0, 1:2, cols]
        acc = None
        for b in range(nblocks):
            rows = slice(b * BLOCK, (b + 1) * BLOCK)
            x = x_ref[0, rows, cols].astype(jnp.float32)
            keys_b = (_silu_half(x * half_k) * head_dim ** (-0.5)).astype(jnp.bfloat16)
            values_b = (x * g_ref[0, 2:3, cols]).astype(jnp.bfloat16)
            update = _block_state(keys_b, values_b, rate, pos)
            acc = update if acc is None else decay * acc + update
        o_ref[hh] = acc.astype(o_ref.dtype)


def _output_kernel(rates_ref, x_ref, g_ref, go_ref, s_ref, *rest, hg, head_dim, nblocks, first):
    o_ref = rest[-1]
    step = pl.program_id(0) + first
    pos = lax.broadcasted_iota(jnp.int32, (BLOCK, 1), 0).astype(jnp.float32)
    pos_row = lax.broadcasted_iota(jnp.int32, (1, BLOCK), 1).astype(jnp.float32)
    row = lax.broadcasted_iota(jnp.int32, (BLOCK, BLOCK), 0)
    col = lax.broadcasted_iota(jnp.int32, (BLOCK, BLOCK), 1)
    causal = row >= col
    for hh in range(hg):
        rate = jnp.full((1, 1), rates_ref[step * hg + hh], jnp.float32)
        cols = slice(hh * head_dim, (hh + 1) * head_dim)
        lead = jnp.exp(-rate * (pos + 1.0))
        mask = jnp.where(causal, lead * jnp.exp(rate * (pos_row + 1.0)), 0.0)
        decay = jnp.exp(-rate * BLOCK)
        state = s_ref[hh].astype(jnp.float32)
        half_q = 0.5 * g_ref[0, 0:1, cols]
        half_k = 0.5 * g_ref[0, 1:2, cols]
        for b in range(nblocks):
            rows = slice(b * BLOCK, (b + 1) * BLOCK)
            x = x_ref[0, rows, cols].astype(jnp.float32)
            queries_b = _silu_half(x * half_q).astype(jnp.bfloat16)
            keys_b = (_silu_half(x * half_k) * head_dim ** (-0.5)).astype(jnp.bfloat16)
            values_b = (x * g_ref[0, 2:3, cols]).astype(jnp.bfloat16)
            scores = _dot_nt(queries_b, keys_b)
            weights = (scores * mask).astype(jnp.bfloat16)
            local = _dot(weights, values_b)
            cross = _dot(queries_b, state.astype(jnp.bfloat16))
            total = local + lead * cross
            normed = total * lax.rsqrt(_row_mean(total * total) + EPSILON)
            o_ref[0, rows, cols] = (x + normed * go_ref[0:1, cols]).astype(o_ref.dtype)
            if b + 1 < nblocks:
                state = decay * state + _block_state(keys_b, values_b, rate, pos)


def _summaries(rates, rows, gains, head_dim):
    _, count, width = rows.shape
    heads = width // head_dim
    hg = HEADS_PER_STEP
    cw = hg * head_dim
    kernel = functools.partial(_summary_kernel, hg=hg, head_dim=head_dim, nblocks=count // BLOCK)
    return pl.pallas_call(
        kernel,
        grid_spec=pltpu.PrefetchScalarGridSpec(
            num_scalar_prefetch=1,
            grid=(heads // hg,),
            in_specs=[
                pl.BlockSpec((1, count, cw), lambda i, r: (0, 0, i)),
                pl.BlockSpec((1, 3, cw), lambda i, r: (0, 0, i)),
            ],
            out_specs=pl.BlockSpec((hg, head_dim, head_dim), lambda i, r: (i, 0, 0)),
        ),
        out_shape=jax.ShapeDtypeStruct((heads, head_dim, head_dim), jnp.bfloat16),
        cost_estimate=pl.CostEstimate(
            flops=2 * count * width * head_dim, transcendentals=count * width,
            bytes_accessed=count * width * 2 + heads * head_dim * head_dim * 4,
        ),
    )(rates, rows, gains)


def _outputs(rates, rows, gains, gain_out, states, head_dim, first, previous):
    _, count, width = rows.shape
    hg = HEADS_PER_STEP
    cw = hg * head_dim
    steps = states.shape[0] // hg
    base = first // hg
    kernel = functools.partial(
        _output_kernel, hg=hg, head_dim=head_dim, nblocks=count // BLOCK, first=base
    )
    row_spec = pl.BlockSpec((1, count, cw), lambda i, r: (0, 0, i + base))
    in_specs = [
        row_spec,
        pl.BlockSpec((1, 3, cw), lambda i, r: (0, 0, i + base)),
        pl.BlockSpec((1, cw), lambda i, r: (0, i + base)),
        pl.BlockSpec((hg, head_dim, head_dim), lambda i, r: (i, 0, 0)),
    ]
    operands = [rates, rows, gains, gain_out, states]
    aliases = {}
    if previous is not None:
        in_specs.append(pl.BlockSpec(memory_space=pl.ANY))
        operands.append(previous)
        aliases = {len(operands) - 1: 0}
    share = steps * cw
    return pl.pallas_call(
        kernel,
        grid_spec=pltpu.PrefetchScalarGridSpec(
            num_scalar_prefetch=1,
            grid=(steps,),
            in_specs=in_specs,
            out_specs=row_spec,
        ),
        out_shape=jax.ShapeDtypeStruct(rows.shape, rows.dtype),
        input_output_aliases=aliases,
        cost_estimate=pl.CostEstimate(
            flops=8 * count * BLOCK * share, transcendentals=3 * count * share,
            bytes_accessed=2 * count * share * 2 + steps * hg * head_dim * head_dim * 2,
        ),
    )(*operands)


def on_device(section_inputs, input_gains, out_gain, decay_rates, carry_state):
    _, count, width = section_inputs.shape
    rates = decay_rates[0]
    heads = rates.shape[0]
    head_dim = width // heads
    group_size = lax.axis_size("ctx")
    own_heads = heads // group_size
    place = lax.axis_index("ctx")
    count_s = lax.axis_size("section")
    pairs = [(src, (src + 1) % count_s) for src in range(count_s)]

    prev_rows, prev_gains, prev_gain_out, prev_rates = lax.ppermute(
        (section_inputs, input_gains, out_gain, decay_rates), "section", pairs
    )

    summary = _summaries(rates, section_inputs, input_gains, head_dim)
    gathered = lax.all_to_all(summary, "ctx", 0, 0, tiled=True)
    gathered = gathered.astype(jnp.float32).reshape(group_size, own_heads, head_dim, head_dim)

    start = place * own_heads
    carry_part = lax.dynamic_slice_in_dim(carry_state[0], start, own_heads, 0)
    rate_part = lax.dynamic_slice_in_dim(rates, start, own_heads, 0)
    target = jnp.arange(group_size)[:, None]
    source = jnp.arange(group_size)[None, :]
    gap = (target - 1 - source).astype(jnp.float32)
    weights = jnp.where(
        (source < target)[:, :, None],
        jnp.exp(-rate_part[None, None, :] * count * jnp.maximum(gap, 0.0)[:, :, None]),
        0.0,
    )
    carry_weights = jnp.exp(-rate_part[None, :] * count * target.astype(jnp.float32))
    prefixes = jnp.einsum(
        "tsh,shde->thde", weights, gathered, precision=lax.Precision.HIGHEST
    ) + carry_weights[:, :, None, None] * carry_part[None]
    end_weights = jnp.exp(
        -rate_part[None, :] * count * (group_size - 1 - source[0]).astype(jnp.float32)[:, None]
    )
    end_part = jnp.einsum(
        "sh,shde->hde", end_weights, gathered, precision=lax.Precision.HIGHEST
    ) + jnp.exp(-rate_part * count * group_size)[:, None, None] * carry_part
    incoming = lax.all_to_all(
        prefixes.astype(jnp.bfloat16).reshape(heads, head_dim, head_dim),
        "ctx", 0, 0, tiled=True,
    )
    prev_gains, prev_gain_out, prev_rates, incoming = lax.optimization_barrier(
        (prev_gains, prev_gain_out, prev_rates, incoming)
    )
    chunk = heads // STATE_CHUNKS
    next_rows = None
    for part in range(STATE_CHUNKS):
        piece = lax.ppermute(incoming[part * chunk : (part + 1) * chunk], "section", pairs)
        next_rows = _outputs(
            prev_rates[0], prev_rows, prev_gains, prev_gain_out, piece, head_dim,
            part * chunk, next_rows,
        )
    return (next_rows, end_part[None])


def solution(mesh):
    return jax.shard_map(
        on_device,
        mesh=mesh,
        in_specs=(
            P("section", "ctx", None),
            P("section", None, None),
            P("section", None),
            P("section", None),
            P("section", None, None, None),
        ),
        out_specs=(P("section", "ctx", None), P("section", "ctx", None, None)),
        check_vma=False,
    )
```

```python
import functools

import jax
import jax.numpy as jnp
from jax import lax
from jax.experimental import pallas as pl
from jax.experimental.pallas import tpu as pltpu
from jax.sharding import PartitionSpec as P

BLOCK = 256
EPSILON = 1e-05
HEADS_PER_STEP = 4
STATE_CHUNKS = 4


def _silu(v):
    return 0.5 * v * (1.0 + jnp.tanh(0.5 * v))


def _dot_nt(a, b):
    return lax.dot_general(a, b, (((1,), (1,)), ((), ())), preferred_element_type=jnp.float32)


def _dot_tn(a, b):
    return lax.dot_general(a, b, (((0,), (0,)), ((), ())), preferred_element_type=jnp.float32)


def _dot(a, b):
    return lax.dot_general(a, b, (((1,), (0,)), ((), ())), preferred_element_type=jnp.float32)


def _block_state(keys_b, values_b, rate, pos):
    tail = jnp.exp(-rate * (BLOCK - 1 - pos))
    scaled = (keys_b.astype(jnp.float32) * tail).astype(jnp.bfloat16)
    return _dot_tn(scaled, values_b)


def _summary_kernel(rates_ref, x_ref, g_ref, o_ref, *, hg, head_dim, nblocks):
    step = pl.program_id(0)
    pos = lax.broadcasted_iota(jnp.int32, (BLOCK, 1), 0).astype(jnp.float32)
    for hh in range(hg):
        rate = jnp.full((1, 1), rates_ref[step * hg + hh], jnp.float32)
        cols = slice(hh * head_dim, (hh + 1) * head_dim)
        decay = jnp.exp(-rate * BLOCK)
        acc = None
        for b in range(nblocks):
            rows = slice(b * BLOCK, (b + 1) * BLOCK)
            x = x_ref[0, rows, cols].astype(jnp.float32)
            keys_b = (_silu(x * g_ref[0, 1:2, cols]) * head_dim ** (-0.5)).astype(jnp.bfloat16)
            values_b = (x * g_ref[0, 2:3, cols]).astype(jnp.bfloat16)
            update = _block_state(keys_b, values_b, rate, pos)
            acc = update if acc is None else decay * acc + update
        o_ref[hh] = acc.astype(o_ref.dtype)


def _output_kernel(rates_ref, x_ref, g_ref, go_ref, s_ref, *rest, hg, head_dim, nblocks, first):
    o_ref = rest[-1]
    step = pl.program_id(0) + first
    pos = lax.broadcasted_iota(jnp.int32, (BLOCK, 1), 0).astype(jnp.float32)
    pos_row = lax.broadcasted_iota(jnp.int32, (1, BLOCK), 1).astype(jnp.float32)
    row = lax.broadcasted_iota(jnp.int32, (BLOCK, BLOCK), 0)
    col = lax.broadcasted_iota(jnp.int32, (BLOCK, BLOCK), 1)
    causal = row >= col
    for hh in range(hg):
        rate = jnp.full((1, 1), rates_ref[step * hg + hh], jnp.float32)
        cols = slice(hh * head_dim, (hh + 1) * head_dim)
        lead = jnp.exp(-rate * (pos + 1.0))
        mask = jnp.where(causal, lead * jnp.exp(rate * (pos_row + 1.0)), 0.0)
        decay = jnp.exp(-rate * BLOCK)
        state = s_ref[hh].astype(jnp.float32)
        for b in range(nblocks):
            rows = slice(b * BLOCK, (b + 1) * BLOCK)
            x = x_ref[0, rows, cols].astype(jnp.float32)
            queries_b = _silu(x * g_ref[0, 0:1, cols]).astype(jnp.bfloat16)
            keys_b = (_silu(x * g_ref[0, 1:2, cols]) * head_dim ** (-0.5)).astype(jnp.bfloat16)
            values_b = (x * g_ref[0, 2:3, cols]).astype(jnp.bfloat16)
            scores = _dot_nt(queries_b, keys_b)
            weights = (scores * mask).astype(jnp.bfloat16)
            local = _dot(weights, values_b)
            cross = _dot(queries_b, state.astype(jnp.bfloat16))
            total = local + lead * cross
            normed = total * lax.rsqrt(jnp.mean(total * total, axis=-1, keepdims=True) + EPSILON)
            o_ref[0, rows, cols] = (x + normed * go_ref[0:1, cols]).astype(o_ref.dtype)
            if b + 1 < nblocks:
                state = decay * state + _block_state(keys_b, values_b, rate, pos)


def _scan_kernel(place_ref, rates_ref, s_ref, c_ref, p_ref, e_ref, *, count, own, sources):
    for hh in range(own):
        rate = jnp.full((1, 1), rates_ref[place_ref[0] * own + hh], jnp.float32)
        decay = jnp.exp(-rate * count)
        state = c_ref[0, hh]
        for c in range(sources):
            p_ref[c, hh] = state.astype(p_ref.dtype)
            state = decay * state + s_ref[c, hh].astype(jnp.float32)
        e_ref[0, hh] = state


def _scan(place, rates, gathered, carry, count):
    sources, own, hd, _ = gathered.shape
    kernel = functools.partial(_scan_kernel, count=count, own=own, sources=sources)
    return pl.pallas_call(
        kernel,
        grid_spec=pltpu.PrefetchScalarGridSpec(
            num_scalar_prefetch=2,
            grid=(1,),
            in_specs=[
                pl.BlockSpec((sources, own, hd, hd), lambda i, p, r: (0, 0, 0, 0)),
                pl.BlockSpec((1, own, hd, hd), lambda i, p, r: (0, p[0], 0, 0)),
            ],
            out_specs=[
                pl.BlockSpec((sources, own, hd, hd), lambda i, p, r: (0, 0, 0, 0)),
                pl.BlockSpec((1, own, hd, hd), lambda i, p, r: (0, 0, 0, 0)),
            ],
        ),
        out_shape=[
            jax.ShapeDtypeStruct(gathered.shape, gathered.dtype),
            jax.ShapeDtypeStruct((1, own, hd, hd), jnp.float32),
        ],
        cost_estimate=pl.CostEstimate(
            flops=2 * gathered.size, transcendentals=0,
            bytes_accessed=4 * gathered.size + 8 * own * hd * hd,
        ),
    )(place, rates, gathered, carry)


def _summaries(rates, rows, gains, head_dim):
    _, count, width = rows.shape
    heads = width // head_dim
    hg = HEADS_PER_STEP
    cw = hg * head_dim
    kernel = functools.partial(_summary_kernel, hg=hg, head_dim=head_dim, nblocks=count // BLOCK)
    return pl.pallas_call(
        kernel,
        grid_spec=pltpu.PrefetchScalarGridSpec(
            num_scalar_prefetch=1,
            grid=(heads // hg,),
            in_specs=[
                pl.BlockSpec((1, count, cw), lambda i, r: (0, 0, i)),
                pl.BlockSpec((1, 3, cw), lambda i, r: (0, 0, i)),
            ],
            out_specs=pl.BlockSpec((hg, head_dim, head_dim), lambda i, r: (i, 0, 0)),
        ),
        out_shape=jax.ShapeDtypeStruct((heads, head_dim, head_dim), jnp.bfloat16),
        cost_estimate=pl.CostEstimate(
            flops=2 * count * width * head_dim, transcendentals=count * width,
            bytes_accessed=count * width * 2 + heads * head_dim * head_dim * 4,
        ),
    )(rates, rows, gains)


def _outputs(rates, rows, gains, gain_out, states, head_dim, first, previous):
    _, count, width = rows.shape
    hg = HEADS_PER_STEP
    cw = hg * head_dim
    steps = states.shape[0] // hg
    base = first // hg
    kernel = functools.partial(
        _output_kernel, hg=hg, head_dim=head_dim, nblocks=count // BLOCK, first=base
    )
    row_spec = pl.BlockSpec((1, count, cw), lambda i, r: (0, 0, i + base))
    in_specs = [
        row_spec,
        pl.BlockSpec((1, 3, cw), lambda i, r: (0, 0, i + base)),
        pl.BlockSpec((1, cw), lambda i, r: (0, i + base)),
        pl.BlockSpec((hg, head_dim, head_dim), lambda i, r: (i, 0, 0)),
    ]
    operands = [rates, rows, gains, gain_out, states]
    aliases = {}
    if previous is not None:
        in_specs.append(pl.BlockSpec(memory_space=pl.ANY))
        operands.append(previous)
        aliases = {len(operands) - 1: 0}
    share = steps * cw
    return pl.pallas_call(
        kernel,
        grid_spec=pltpu.PrefetchScalarGridSpec(
            num_scalar_prefetch=1,
            grid=(steps,),
            in_specs=in_specs,
            out_specs=row_spec,
        ),
        out_shape=jax.ShapeDtypeStruct(rows.shape, rows.dtype),
        input_output_aliases=aliases,
        cost_estimate=pl.CostEstimate(
            flops=8 * count * BLOCK * share, transcendentals=3 * count * share,
            bytes_accessed=2 * count * share * 2 + steps * hg * head_dim * head_dim * 2,
        ),
    )(*operands)


def on_device(section_inputs, input_gains, out_gain, decay_rates, carry_state):
    _, count, width = section_inputs.shape
    rates = decay_rates[0]
    heads = rates.shape[0]
    head_dim = width // heads
    group_size = lax.axis_size("ctx")
    own_heads = heads // group_size
    place = lax.axis_index("ctx")
    count_s = lax.axis_size("section")
    pairs = [(src, (src + 1) % count_s) for src in range(count_s)]

    prev_rows, prev_gains, prev_gain_out, prev_rates = lax.ppermute(
        (section_inputs, input_gains, out_gain, decay_rates), "section", pairs
    )

    summary = _summaries(rates, section_inputs, input_gains, head_dim)
    gathered = lax.all_to_all(summary, "ctx", 0, 0, tiled=True)
    gathered = gathered.reshape(group_size, own_heads, head_dim, head_dim)
    prefixes, end_part = _scan(
        place.reshape(1).astype(jnp.int32), rates, gathered, carry_state, count
    )
    incoming = lax.all_to_all(
        prefixes.reshape(heads, head_dim, head_dim), "ctx", 0, 0, tiled=True
    )
    prev_gains, prev_gain_out, prev_rates, incoming = lax.optimization_barrier(
        (prev_gains, prev_gain_out, prev_rates, incoming)
    )
    chunk = heads // STATE_CHUNKS
    next_rows = None
    for part in range(STATE_CHUNKS):
        piece = lax.ppermute(incoming[part * chunk : (part + 1) * chunk], "section", pairs)
        next_rows = _outputs(
            prev_rates[0], prev_rows, prev_gains, prev_gain_out, piece, head_dim,
            part * chunk, next_rows,
        )
    return (next_rows, end_part)


def solution(mesh):
    return jax.shard_map(
        on_device,
        mesh=mesh,
        in_specs=(
            P("section", "ctx", None),
            P("section", None, None),
            P("section", None),
            P("section", None),
            P("section", None, None, None),
        ),
        out_specs=(P("section", "ctx", None), P("section", "ctx", None, None)),
        check_vma=False,
    )
```

```python
import functools

import jax
import jax.numpy as jnp
from jax import lax
from jax.experimental import pallas as pl
from jax.experimental.pallas import tpu as pltpu
from jax.sharding import PartitionSpec as P

BLOCK = 256
EPSILON = 1e-05
HEADS_PER_STEP = 4
STATE_CHUNKS = 4


def _silu_half(u):
    return u + u * jnp.tanh(u)


def _row_mean(v):
    ones = jnp.full((v.shape[-1], v.shape[-1]), 1.0 / v.shape[-1], jnp.bfloat16)
    high = v.astype(jnp.bfloat16)
    low = (v - high.astype(jnp.float32)).astype(jnp.bfloat16)
    return _dot(high, ones) + _dot(low, ones)


def _dot_nt(a, b):
    return lax.dot_general(a, b, (((1,), (1,)), ((), ())), preferred_element_type=jnp.float32)


def _dot_tn(a, b):
    return lax.dot_general(a, b, (((0,), (0,)), ((), ())), preferred_element_type=jnp.float32)


def _dot(a, b):
    return lax.dot_general(a, b, (((1,), (0,)), ((), ())), preferred_element_type=jnp.float32)


def _block_state(keys_b, values_b, rate, pos):
    tail = jnp.exp(-rate * (BLOCK - 1 - pos))
    scaled = (keys_b.astype(jnp.float32) * tail).astype(jnp.bfloat16)
    return _dot_tn(scaled, values_b)


def _summary_kernel(rates_ref, x_ref, g_ref, o_ref, *, hg, head_dim, nblocks):
    step = pl.program_id(0)
    pos = lax.broadcasted_iota(jnp.int32, (BLOCK, 1), 0).astype(jnp.float32)
    for hh in range(hg):
        rate = jnp.full((1, 1), rates_ref[step * hg + hh], jnp.float32)
        cols = slice(hh * head_dim, (hh + 1) * head_dim)
        decay = jnp.exp(-rate * BLOCK)
        half_k = 0.5 * g_ref[0, 1:2, cols]
        acc = None
        for b in range(nblocks):
            rows = slice(b * BLOCK, (b + 1) * BLOCK)
            x = x_ref[0, rows, cols].astype(jnp.float32)
            keys_b = (_silu_half(x * half_k) * head_dim ** (-0.5)).astype(jnp.bfloat16)
            values_b = (x * g_ref[0, 2:3, cols]).astype(jnp.bfloat16)
            update = _block_state(keys_b, values_b, rate, pos)
            acc = update if acc is None else decay * acc + update
        o_ref[hh] = acc.astype(o_ref.dtype)


def _output_kernel(rates_ref, x_ref, g_ref, go_ref, s_ref, *rest, hg, head_dim, nblocks, first):
    o_ref = rest[-1]
    step = pl.program_id(0) + first
    pos = lax.broadcasted_iota(jnp.int32, (BLOCK, 1), 0).astype(jnp.float32)
    pos_row = lax.broadcasted_iota(jnp.int32, (1, BLOCK), 1).astype(jnp.float32)
    row = lax.broadcasted_iota(jnp.int32, (BLOCK, BLOCK), 0)
    col = lax.broadcasted_iota(jnp.int32, (BLOCK, BLOCK), 1)
    causal = row >= col
    for hh in range(hg):
        rate = jnp.full((1, 1), rates_ref[step * hg + hh], jnp.float32)
        cols = slice(hh * head_dim, (hh + 1) * head_dim)
        lead = jnp.exp(-rate * (pos + 1.0))
        mask = jnp.where(causal, lead * jnp.exp(rate * (pos_row + 1.0)), 0.0)
        decay = jnp.exp(-rate * BLOCK)
        state = s_ref[hh].astype(jnp.float32)
        half_q = 0.5 * g_ref[0, 0:1, cols]
        half_k = 0.5 * g_ref[0, 1:2, cols]
        for b in range(nblocks):
            rows = slice(b * BLOCK, (b + 1) * BLOCK)
            x = x_ref[0, rows, cols].astype(jnp.float32)
            queries_b = _silu_half(x * half_q).astype(jnp.bfloat16)
            keys_b = (_silu_half(x * half_k) * head_dim ** (-0.5)).astype(jnp.bfloat16)
            values_b = (x * g_ref[0, 2:3, cols]).astype(jnp.bfloat16)
            scores = _dot_nt(queries_b, keys_b)
            weights = (scores * mask).astype(jnp.bfloat16)
            local = _dot(weights, values_b)
            cross = _dot(queries_b, state.astype(jnp.bfloat16))
            total = local + lead * cross
            normed = total * lax.rsqrt(_row_mean(total * total) + EPSILON)
            o_ref[0, rows, cols] = (x + normed * go_ref[0:1, cols]).astype(o_ref.dtype)
            if b + 1 < nblocks:
                state = decay * state + _block_state(keys_b, values_b, rate, pos)


def _scan_kernel(place_ref, rates_ref, s_ref, c_ref, p_ref, e_ref, *, count, own, sources):
    for hh in range(own):
        rate = jnp.full((1, 1), rates_ref[place_ref[0] * own + hh], jnp.float32)
        decay = jnp.exp(-rate * count)
        state = c_ref[0, hh]
        for c in range(sources):
            p_ref[c, hh] = state.astype(p_ref.dtype)
            state = decay * state + s_ref[c, hh].astype(jnp.float32)
        e_ref[0, hh] = state


def _scan(place, rates, gathered, carry, count):
    sources, own, hd, _ = gathered.shape
    kernel = functools.partial(_scan_kernel, count=count, own=own, sources=sources)
    return pl.pallas_call(
        kernel,
        grid_spec=pltpu.PrefetchScalarGridSpec(
            num_scalar_prefetch=2,
            grid=(1,),
            in_specs=[
                pl.BlockSpec((sources, own, hd, hd), lambda i, p, r: (0, 0, 0, 0)),
                pl.BlockSpec((1, own, hd, hd), lambda i, p, r: (0, p[0], 0, 0)),
            ],
            out_specs=[
                pl.BlockSpec((sources, own, hd, hd), lambda i, p, r: (0, 0, 0, 0)),
                pl.BlockSpec((1, own, hd, hd), lambda i, p, r: (0, 0, 0, 0)),
            ],
        ),
        out_shape=[
            jax.ShapeDtypeStruct(gathered.shape, gathered.dtype),
            jax.ShapeDtypeStruct((1, own, hd, hd), jnp.float32),
        ],
        cost_estimate=pl.CostEstimate(
            flops=2 * gathered.size, transcendentals=0,
            bytes_accessed=4 * gathered.size + 8 * own * hd * hd,
        ),
    )(place, rates, gathered, carry)


def _summaries(rates, rows, gains, head_dim):
    _, count, width = rows.shape
    heads = width // head_dim
    hg = HEADS_PER_STEP
    cw = hg * head_dim
    kernel = functools.partial(_summary_kernel, hg=hg, head_dim=head_dim, nblocks=count // BLOCK)
    return pl.pallas_call(
        kernel,
        grid_spec=pltpu.PrefetchScalarGridSpec(
            num_scalar_prefetch=1,
            grid=(heads // hg,),
            in_specs=[
                pl.BlockSpec((1, count, cw), lambda i, r: (0, 0, i)),
                pl.BlockSpec((1, 3, cw), lambda i, r: (0, 0, i)),
            ],
            out_specs=pl.BlockSpec((hg, head_dim, head_dim), lambda i, r: (i, 0, 0)),
        ),
        out_shape=jax.ShapeDtypeStruct((heads, head_dim, head_dim), jnp.bfloat16),
        cost_estimate=pl.CostEstimate(
            flops=2 * count * width * head_dim, transcendentals=count * width,
            bytes_accessed=count * width * 2 + heads * head_dim * head_dim * 4,
        ),
    )(rates, rows, gains)


def _outputs(rates, rows, gains, gain_out, states, head_dim, first, previous):
    _, count, width = rows.shape
    hg = HEADS_PER_STEP
    cw = hg * head_dim
    steps = states.shape[0] // hg
    base = first // hg
    kernel = functools.partial(
        _output_kernel, hg=hg, head_dim=head_dim, nblocks=count // BLOCK, first=base
    )
    row_spec = pl.BlockSpec((1, count, cw), lambda i, r: (0, 0, i + base))
    in_specs = [
        row_spec,
        pl.BlockSpec((1, 3, cw), lambda i, r: (0, 0, i + base)),
        pl.BlockSpec((1, cw), lambda i, r: (0, i + base)),
        pl.BlockSpec((hg, head_dim, head_dim), lambda i, r: (i, 0, 0)),
    ]
    operands = [rates, rows, gains, gain_out, states]
    aliases = {}
    if previous is not None:
        in_specs.append(pl.BlockSpec(memory_space=pl.ANY))
        operands.append(previous)
        aliases = {len(operands) - 1: 0}
    share = steps * cw
    return pl.pallas_call(
        kernel,
        grid_spec=pltpu.PrefetchScalarGridSpec(
            num_scalar_prefetch=1,
            grid=(steps,),
            in_specs=in_specs,
            out_specs=row_spec,
        ),
        out_shape=jax.ShapeDtypeStruct(rows.shape, rows.dtype),
        input_output_aliases=aliases,
        cost_estimate=pl.CostEstimate(
            flops=8 * count * BLOCK * share, transcendentals=3 * count * share,
            bytes_accessed=2 * count * share * 2 + steps * hg * head_dim * head_dim * 2,
        ),
    )(*operands)


def on_device(section_inputs, input_gains, out_gain, decay_rates, carry_state):
    _, count, width = section_inputs.shape
    rates = decay_rates[0]
    heads = rates.shape[0]
    head_dim = width // heads
    group_size = lax.axis_size("ctx")
    own_heads = heads // group_size
    place = lax.axis_index("ctx")
    count_s = lax.axis_size("section")
    pairs = [(src, (src + 1) % count_s) for src in range(count_s)]

    prev_rows, prev_gains, prev_gain_out, prev_rates = lax.ppermute(
        (section_inputs, input_gains, out_gain, decay_rates), "section", pairs
    )

    summary = _summaries(rates, section_inputs, input_gains, head_dim)
    gathered = lax.all_to_all(summary, "ctx", 0, 0, tiled=True)
    gathered = gathered.reshape(group_size, own_heads, head_dim, head_dim)
    prefixes, end_part = _scan(
        place.reshape(1).astype(jnp.int32), rates, gathered, carry_state, count
    )
    incoming = lax.all_to_all(
        prefixes.reshape(heads, head_dim, head_dim), "ctx", 0, 0, tiled=True
    )
    prev_gains, prev_gain_out, prev_rates, incoming = lax.optimization_barrier(
        (prev_gains, prev_gain_out, prev_rates, incoming)
    )
    chunk = heads // STATE_CHUNKS
    next_rows = None
    for part in range(STATE_CHUNKS):
        piece = lax.ppermute(incoming[part * chunk : (part + 1) * chunk], "section", pairs)
        next_rows = _outputs(
            prev_rates[0], prev_rows, prev_gains, prev_gain_out, piece, head_dim,
            part * chunk, next_rows,
        )
    return (next_rows, end_part)


def solution(mesh):
    return jax.shard_map(
        on_device,
        mesh=mesh,
        in_specs=(
            P("section", "ctx", None),
            P("section", None, None),
            P("section", None),
            P("section", None),
            P("section", None, None, None),
        ),
        out_specs=(P("section", "ctx", None), P("section", "ctx", None, None)),
        check_vma=False,
    )
```

```python
import functools

import jax
import jax.numpy as jnp
from jax import lax
from jax.experimental import pallas as pl
from jax.experimental.pallas import tpu as pltpu
from jax.sharding import PartitionSpec as P

BLOCK = 256
EPSILON = 1e-05
HEADS_PER_STEP = 6
STATE_CHUNKS = 4


def _silu(v):
    return 0.5 * v * (1.0 + jnp.tanh(0.5 * v))


def _dot_nt(a, b):
    return lax.dot_general(a, b, (((1,), (1,)), ((), ())), preferred_element_type=jnp.float32)


def _dot_tn(a, b):
    return lax.dot_general(a, b, (((0,), (0,)), ((), ())), preferred_element_type=jnp.float32)


def _dot(a, b):
    return lax.dot_general(a, b, (((1,), (0,)), ((), ())), preferred_element_type=jnp.float32)


def _block_state(keys_b, values_b, rate, pos):
    tail = jnp.exp(-rate * (BLOCK - 1 - pos))
    scaled = (keys_b.astype(jnp.float32) * tail).astype(jnp.bfloat16)
    return _dot_tn(scaled, values_b)


def _summary_kernel(rates_ref, x_ref, g_ref, o_ref, *, hg, head_dim, nblocks):
    step = pl.program_id(0)
    pos = lax.broadcasted_iota(jnp.int32, (BLOCK, 1), 0).astype(jnp.float32)
    for hh in range(hg):
        rate = jnp.full((1, 1), rates_ref[step * hg + hh], jnp.float32)
        cols = slice(hh * head_dim, (hh + 1) * head_dim)
        decay = jnp.exp(-rate * BLOCK)
        acc = None
        for b in range(nblocks):
            rows = slice(b * BLOCK, (b + 1) * BLOCK)
            x = x_ref[0, rows, cols].astype(jnp.float32)
            keys_b = (_silu(x * g_ref[0, 1:2, cols]) * head_dim ** (-0.5)).astype(jnp.bfloat16)
            values_b = (x * g_ref[0, 2:3, cols]).astype(jnp.bfloat16)
            update = _block_state(keys_b, values_b, rate, pos)
            acc = update if acc is None else decay * acc + update
        o_ref[hh] = acc.astype(o_ref.dtype)


def _output_kernel(rates_ref, x_ref, g_ref, go_ref, s_ref, *rest, hg, head_dim, nblocks, first):
    o_ref = rest[-1]
    step = pl.program_id(0) + first
    pos = lax.broadcasted_iota(jnp.int32, (BLOCK, 1), 0).astype(jnp.float32)
    pos_row = lax.broadcasted_iota(jnp.int32, (1, BLOCK), 1).astype(jnp.float32)
    row = lax.broadcasted_iota(jnp.int32, (BLOCK, BLOCK), 0)
    col = lax.broadcasted_iota(jnp.int32, (BLOCK, BLOCK), 1)
    causal = row >= col
    for hh in range(hg):
        rate = jnp.full((1, 1), rates_ref[step * hg + hh], jnp.float32)
        cols = slice(hh * head_dim, (hh + 1) * head_dim)
        lead = jnp.exp(-rate * (pos + 1.0))
        mask = jnp.where(causal, lead * jnp.exp(rate * (pos_row + 1.0)), 0.0)
        decay = jnp.exp(-rate * BLOCK)
        state = s_ref[hh].astype(jnp.float32)
        for b in range(nblocks):
            rows = slice(b * BLOCK, (b + 1) * BLOCK)
            x = x_ref[0, rows, cols].astype(jnp.float32)
            queries_b = _silu(x * g_ref[0, 0:1, cols]).astype(jnp.bfloat16)
            keys_b = (_silu(x * g_ref[0, 1:2, cols]) * head_dim ** (-0.5)).astype(jnp.bfloat16)
            values_b = (x * g_ref[0, 2:3, cols]).astype(jnp.bfloat16)
            scores = _dot_nt(queries_b, keys_b)
            weights = (scores * mask).astype(jnp.bfloat16)
            local = _dot(weights, values_b)
            cross = _dot(queries_b, state.astype(jnp.bfloat16))
            total = local + lead * cross
            normed = total * lax.rsqrt(jnp.mean(total * total, axis=-1, keepdims=True) + EPSILON)
            o_ref[0, rows, cols] = (x + normed * go_ref[0:1, cols]).astype(o_ref.dtype)
            if b + 1 < nblocks:
                state = decay * state + _block_state(keys_b, values_b, rate, pos)


def _scan_kernel(place_ref, rates_ref, s_ref, c_ref, p_ref, e_ref, *, count, own, sources):
    for hh in range(own):
        rate = jnp.full((1, 1), rates_ref[place_ref[0] * own + hh], jnp.float32)
        decay = jnp.exp(-rate * count)
        state = c_ref[0, hh]
        for c in range(sources):
            p_ref[c, hh] = state.astype(p_ref.dtype)
            state = decay * state + s_ref[c, hh].astype(jnp.float32)
        e_ref[0, hh] = state


def _scan(place, rates, gathered, carry, count):
    sources, own, hd, _ = gathered.shape
    kernel = functools.partial(_scan_kernel, count=count, own=own, sources=sources)
    return pl.pallas_call(
        kernel,
        grid_spec=pltpu.PrefetchScalarGridSpec(
            num_scalar_prefetch=2,
            grid=(1,),
            in_specs=[
                pl.BlockSpec((sources, own, hd, hd), lambda i, p, r: (0, 0, 0, 0)),
                pl.BlockSpec((1, own, hd, hd), lambda i, p, r: (0, p[0], 0, 0)),
            ],
            out_specs=[
                pl.BlockSpec((sources, own, hd, hd), lambda i, p, r: (0, 0, 0, 0)),
                pl.BlockSpec((1, own, hd, hd), lambda i, p, r: (0, 0, 0, 0)),
            ],
        ),
        out_shape=[
            jax.ShapeDtypeStruct(gathered.shape, gathered.dtype),
            jax.ShapeDtypeStruct((1, own, hd, hd), jnp.float32),
        ],
        cost_estimate=pl.CostEstimate(
            flops=2 * gathered.size, transcendentals=0,
            bytes_accessed=4 * gathered.size + 8 * own * hd * hd,
        ),
    )(place, rates, gathered, carry)


def _summaries(rates, rows, gains, head_dim):
    _, count, width = rows.shape
    heads = width // head_dim
    hg = HEADS_PER_STEP
    cw = hg * head_dim
    kernel = functools.partial(_summary_kernel, hg=hg, head_dim=head_dim, nblocks=count // BLOCK)
    return pl.pallas_call(
        kernel,
        grid_spec=pltpu.PrefetchScalarGridSpec(
            num_scalar_prefetch=1,
            grid=(heads // hg,),
            in_specs=[
                pl.BlockSpec((1, count, cw), lambda i, r: (0, 0, i)),
                pl.BlockSpec((1, 3, cw), lambda i, r: (0, 0, i)),
            ],
            out_specs=pl.BlockSpec((hg, head_dim, head_dim), lambda i, r: (i, 0, 0)),
        ),
        out_shape=jax.ShapeDtypeStruct((heads, head_dim, head_dim), jnp.bfloat16),
        cost_estimate=pl.CostEstimate(
            flops=2 * count * width * head_dim, transcendentals=count * width,
            bytes_accessed=count * width * 2 + heads * head_dim * head_dim * 4,
        ),
    )(rates, rows, gains)


def _outputs(rates, rows, gains, gain_out, states, head_dim, first, previous):
    _, count, width = rows.shape
    hg = HEADS_PER_STEP
    cw = hg * head_dim
    steps = states.shape[0] // hg
    base = first // hg
    kernel = functools.partial(
        _output_kernel, hg=hg, head_dim=head_dim, nblocks=count // BLOCK, first=base
    )
    row_spec = pl.BlockSpec((1, count, cw), lambda i, r: (0, 0, i + base))
    in_specs = [
        row_spec,
        pl.BlockSpec((1, 3, cw), lambda i, r: (0, 0, i + base)),
        pl.BlockSpec((1, cw), lambda i, r: (0, i + base)),
        pl.BlockSpec((hg, head_dim, head_dim), lambda i, r: (i, 0, 0)),
    ]
    operands = [rates, rows, gains, gain_out, states]
    aliases = {}
    if previous is not None:
        in_specs.append(pl.BlockSpec(memory_space=pl.ANY))
        operands.append(previous)
        aliases = {len(operands) - 1: 0}
    share = steps * cw
    return pl.pallas_call(
        kernel,
        grid_spec=pltpu.PrefetchScalarGridSpec(
            num_scalar_prefetch=1,
            grid=(steps,),
            in_specs=in_specs,
            out_specs=row_spec,
        ),
        out_shape=jax.ShapeDtypeStruct(rows.shape, rows.dtype),
        input_output_aliases=aliases,
        cost_estimate=pl.CostEstimate(
            flops=8 * count * BLOCK * share, transcendentals=3 * count * share,
            bytes_accessed=2 * count * share * 2 + steps * hg * head_dim * head_dim * 2,
        ),
    )(*operands)


def on_device(section_inputs, input_gains, out_gain, decay_rates, carry_state):
    _, count, width = section_inputs.shape
    rates = decay_rates[0]
    heads = rates.shape[0]
    head_dim = width // heads
    group_size = lax.axis_size("ctx")
    own_heads = heads // group_size
    place = lax.axis_index("ctx")
    count_s = lax.axis_size("section")
    pairs = [(src, (src + 1) % count_s) for src in range(count_s)]

    prev_rows, prev_gains, prev_gain_out, prev_rates = lax.ppermute(
        (section_inputs, input_gains, out_gain, decay_rates), "section", pairs
    )

    summary = _summaries(rates, section_inputs, input_gains, head_dim)
    gathered = lax.all_to_all(summary, "ctx", 0, 0, tiled=True)
    gathered = gathered.reshape(group_size, own_heads, head_dim, head_dim)
    prefixes, end_part = _scan(
        place.reshape(1).astype(jnp.int32), rates, gathered, carry_state, count
    )
    incoming = lax.all_to_all(
        prefixes.reshape(heads, head_dim, head_dim), "ctx", 0, 0, tiled=True
    )
    prev_gains, prev_gain_out, prev_rates, incoming = lax.optimization_barrier(
        (prev_gains, prev_gain_out, prev_rates, incoming)
    )
    chunk = heads // STATE_CHUNKS
    next_rows = None
    for part in range(STATE_CHUNKS):
        piece = lax.ppermute(incoming[part * chunk : (part + 1) * chunk], "section", pairs)
        next_rows = _outputs(
            prev_rates[0], prev_rows, prev_gains, prev_gain_out, piece, head_dim,
            part * chunk, next_rows,
        )
    return (next_rows, end_part)


def solution(mesh):
    return jax.shard_map(
        on_device,
        mesh=mesh,
        in_specs=(
            P("section", "ctx", None),
            P("section", None, None),
            P("section", None),
            P("section", None),
            P("section", None, None, None),
        ),
        out_specs=(P("section", "ctx", None), P("section", "ctx", None, None)),
        check_vma=False,
    )
```

```python
import functools

import jax
import jax.numpy as jnp
from jax import lax
from jax.experimental import pallas as pl
from jax.experimental.pallas import tpu as pltpu
from jax.sharding import PartitionSpec as P

BLOCK = 256
EPSILON = 1e-05
HEADS_PER_STEP = 6
SUMMARY_HEADS_PER_STEP = 12
STATE_CHUNKS = 4


def _silu(v):
    return 0.5 * v * (1.0 + jnp.tanh(0.5 * v))


def _dot_nt(a, b):
    return lax.dot_general(a, b, (((1,), (1,)), ((), ())), preferred_element_type=jnp.float32)


def _dot_tn(a, b):
    return lax.dot_general(a, b, (((0,), (0,)), ((), ())), preferred_element_type=jnp.float32)


def _dot(a, b):
    return lax.dot_general(a, b, (((1,), (0,)), ((), ())), preferred_element_type=jnp.float32)


def _block_state(keys_b, values_b, rate, pos):
    tail = jnp.exp(-rate * (BLOCK - 1 - pos))
    scaled = (keys_b.astype(jnp.float32) * tail).astype(jnp.bfloat16)
    return _dot_tn(scaled, values_b)


def _summary_kernel(rates_ref, x_ref, g_ref, o_ref, *, hg, head_dim, nblocks):
    step = pl.program_id(0)
    pos = lax.broadcasted_iota(jnp.int32, (BLOCK, 1), 0).astype(jnp.float32)
    for hh in range(hg):
        rate = jnp.full((1, 1), rates_ref[step * hg + hh], jnp.float32)
        cols = slice(hh * head_dim, (hh + 1) * head_dim)
        decay = jnp.exp(-rate * BLOCK)
        acc = None
        for b in range(nblocks):
            rows = slice(b * BLOCK, (b + 1) * BLOCK)
            x = x_ref[0, rows, cols].astype(jnp.float32)
            keys_b = (_silu(x * g_ref[0, 1:2, cols]) * head_dim ** (-0.5)).astype(jnp.bfloat16)
            values_b = (x * g_ref[0, 2:3, cols]).astype(jnp.bfloat16)
            update = _block_state(keys_b, values_b, rate, pos)
            acc = update if acc is None else decay * acc + update
        o_ref[hh] = acc.astype(o_ref.dtype)


def _output_kernel(rates_ref, x_ref, g_ref, go_ref, s_ref, *rest, hg, head_dim, nblocks, first):
    o_ref = rest[-1]
    step = pl.program_id(0) + first
    pos = lax.broadcasted_iota(jnp.int32, (BLOCK, 1), 0).astype(jnp.float32)
    pos_row = lax.broadcasted_iota(jnp.int32, (1, BLOCK), 1).astype(jnp.float32)
    row = lax.broadcasted_iota(jnp.int32, (BLOCK, BLOCK), 0)
    col = lax.broadcasted_iota(jnp.int32, (BLOCK, BLOCK), 1)
    causal = row >= col
    for hh in range(hg):
        rate = jnp.full((1, 1), rates_ref[step * hg + hh], jnp.float32)
        cols = slice(hh * head_dim, (hh + 1) * head_dim)
        lead = jnp.exp(-rate * (pos + 1.0))
        mask = jnp.where(causal, lead * jnp.exp(rate * (pos_row + 1.0)), 0.0)
        decay = jnp.exp(-rate * BLOCK)
        state = s_ref[hh].astype(jnp.float32)
        for b in range(nblocks):
            rows = slice(b * BLOCK, (b + 1) * BLOCK)
            x = x_ref[0, rows, cols].astype(jnp.float32)
            queries_b = _silu(x * g_ref[0, 0:1, cols]).astype(jnp.bfloat16)
            keys_b = (_silu(x * g_ref[0, 1:2, cols]) * head_dim ** (-0.5)).astype(jnp.bfloat16)
            values_b = (x * g_ref[0, 2:3, cols]).astype(jnp.bfloat16)
            scores = _dot_nt(queries_b, keys_b)
            weights = (scores * mask).astype(jnp.bfloat16)
            local = _dot(weights, values_b)
            cross = _dot(queries_b, state.astype(jnp.bfloat16))
            total = local + lead * cross
            normed = total * lax.rsqrt(jnp.mean(total * total, axis=-1, keepdims=True) + EPSILON)
            o_ref[0, rows, cols] = (x + normed * go_ref[0:1, cols]).astype(o_ref.dtype)
            if b + 1 < nblocks:
                state = decay * state + _block_state(keys_b, values_b, rate, pos)


def _scan_kernel(place_ref, rates_ref, s_ref, c_ref, p_ref, e_ref, *, count, own, sources):
    for hh in range(own):
        rate = jnp.full((1, 1), rates_ref[place_ref[0] * own + hh], jnp.float32)
        decay = jnp.exp(-rate * count)
        state = c_ref[0, hh]
        for c in range(sources):
            p_ref[c, hh] = state.astype(p_ref.dtype)
            state = decay * state + s_ref[c, hh].astype(jnp.float32)
        e_ref[0, hh] = state


def _scan(place, rates, gathered, carry, count):
    sources, own, hd, _ = gathered.shape
    kernel = functools.partial(_scan_kernel, count=count, own=own, sources=sources)
    return pl.pallas_call(
        kernel,
        grid_spec=pltpu.PrefetchScalarGridSpec(
            num_scalar_prefetch=2,
            grid=(1,),
            in_specs=[
                pl.BlockSpec((sources, own, hd, hd), lambda i, p, r: (0, 0, 0, 0)),
                pl.BlockSpec((1, own, hd, hd), lambda i, p, r: (0, p[0], 0, 0)),
            ],
            out_specs=[
                pl.BlockSpec((sources, own, hd, hd), lambda i, p, r: (0, 0, 0, 0)),
                pl.BlockSpec((1, own, hd, hd), lambda i, p, r: (0, 0, 0, 0)),
            ],
        ),
        out_shape=[
            jax.ShapeDtypeStruct(gathered.shape, gathered.dtype),
            jax.ShapeDtypeStruct((1, own, hd, hd), jnp.float32),
        ],
        cost_estimate=pl.CostEstimate(
            flops=2 * gathered.size, transcendentals=0,
            bytes_accessed=4 * gathered.size + 8 * own * hd * hd,
        ),
    )(place, rates, gathered, carry)


def _summaries(rates, rows, gains, head_dim):
    _, count, width = rows.shape
    heads = width // head_dim
    hg = SUMMARY_HEADS_PER_STEP
    cw = hg * head_dim
    kernel = functools.partial(_summary_kernel, hg=hg, head_dim=head_dim, nblocks=count // BLOCK)
    return pl.pallas_call(
        kernel,
        grid_spec=pltpu.PrefetchScalarGridSpec(
            num_scalar_prefetch=1,
            grid=(heads // hg,),
            in_specs=[
                pl.BlockSpec((1, count, cw), lambda i, r: (0, 0, i)),
                pl.BlockSpec((1, 3, cw), lambda i, r: (0, 0, i)),
            ],
            out_specs=pl.BlockSpec((hg, head_dim, head_dim), lambda i, r: (i, 0, 0)),
        ),
        out_shape=jax.ShapeDtypeStruct((heads, head_dim, head_dim), jnp.bfloat16),
        cost_estimate=pl.CostEstimate(
            flops=2 * count * width * head_dim, transcendentals=count * width,
            bytes_accessed=count * width * 2 + heads * head_dim * head_dim * 4,
        ),
    )(rates, rows, gains)


def _outputs(rates, rows, gains, gain_out, states, head_dim, first, previous):
    _, count, width = rows.shape
    hg = HEADS_PER_STEP
    cw = hg * head_dim
    steps = states.shape[0] // hg
    base = first // hg
    kernel = functools.partial(
        _output_kernel, hg=hg, head_dim=head_dim, nblocks=count // BLOCK, first=base
    )
    row_spec = pl.BlockSpec((1, count, cw), lambda i, r: (0, 0, i + base))
    in_specs = [
        row_spec,
        pl.BlockSpec((1, 3, cw), lambda i, r: (0, 0, i + base)),
        pl.BlockSpec((1, cw), lambda i, r: (0, i + base)),
        pl.BlockSpec((hg, head_dim, head_dim), lambda i, r: (i, 0, 0)),
    ]
    operands = [rates, rows, gains, gain_out, states]
    aliases = {}
    if previous is not None:
        in_specs.append(pl.BlockSpec(memory_space=pl.ANY))
        operands.append(previous)
        aliases = {len(operands) - 1: 0}
    share = steps * cw
    return pl.pallas_call(
        kernel,
        grid_spec=pltpu.PrefetchScalarGridSpec(
            num_scalar_prefetch=1,
            grid=(steps,),
            in_specs=in_specs,
            out_specs=row_spec,
        ),
        out_shape=jax.ShapeDtypeStruct(rows.shape, rows.dtype),
        input_output_aliases=aliases,
        cost_estimate=pl.CostEstimate(
            flops=8 * count * BLOCK * share, transcendentals=3 * count * share,
            bytes_accessed=2 * count * share * 2 + steps * hg * head_dim * head_dim * 2,
        ),
    )(*operands)


def on_device(section_inputs, input_gains, out_gain, decay_rates, carry_state):
    _, count, width = section_inputs.shape
    rates = decay_rates[0]
    heads = rates.shape[0]
    head_dim = width // heads
    group_size = lax.axis_size("ctx")
    own_heads = heads // group_size
    place = lax.axis_index("ctx")
    count_s = lax.axis_size("section")
    pairs = [(src, (src + 1) % count_s) for src in range(count_s)]

    prev_rows, prev_gains, prev_gain_out, prev_rates = lax.ppermute(
        (section_inputs, input_gains, out_gain, decay_rates), "section", pairs
    )

    summary = _summaries(rates, section_inputs, input_gains, head_dim)
    gathered = lax.all_to_all(summary, "ctx", 0, 0, tiled=True)
    gathered = gathered.reshape(group_size, own_heads, head_dim, head_dim)
    prefixes, end_part = _scan(
        place.reshape(1).astype(jnp.int32), rates, gathered, carry_state, count
    )
    incoming = lax.all_to_all(
        prefixes.reshape(heads, head_dim, head_dim), "ctx", 0, 0, tiled=True
    )
    prev_gains, prev_gain_out, prev_rates, incoming = lax.optimization_barrier(
        (prev_gains, prev_gain_out, prev_rates, incoming)
    )
    chunk = heads // STATE_CHUNKS
    next_rows = None
    for part in range(STATE_CHUNKS):
        piece = lax.ppermute(incoming[part * chunk : (part + 1) * chunk], "section", pairs)
        next_rows = _outputs(
            prev_rates[0], prev_rows, prev_gains, prev_gain_out, piece, head_dim,
            part * chunk, next_rows,
        )
    return (next_rows, end_part)


def solution(mesh):
    return jax.shard_map(
        on_device,
        mesh=mesh,
        in_specs=(
            P("section", "ctx", None),
            P("section", None, None),
            P("section", None),
            P("section", None),
            P("section", None, None, None),
        ),
        out_specs=(P("section", "ctx", None), P("section", "ctx", None, None)),
        check_vma=False,
    )
```

```python
import functools

import jax
import jax.numpy as jnp
from jax import lax
from jax.experimental import pallas as pl
from jax.experimental.pallas import tpu as pltpu
from jax.sharding import PartitionSpec as P

BLOCK = 256
EPSILON = 1e-05
HEADS_PER_STEP = 6
SUMMARY_HEADS_PER_STEP = 12
STATE_CHUNKS = 4


def _silu(v):
    return 0.5 * v * (1.0 + jnp.tanh(0.5 * v))


def _dot_nt(a, b):
    return lax.dot_general(a, b, (((1,), (1,)), ((), ())), preferred_element_type=jnp.float32)


def _dot_tn(a, b):
    return lax.dot_general(a, b, (((0,), (0,)), ((), ())), preferred_element_type=jnp.float32)


def _dot(a, b):
    return lax.dot_general(a, b, (((1,), (0,)), ((), ())), preferred_element_type=jnp.float32)


def _block_state(keys_b, values_b, rate, pos):
    tail = jnp.exp(-rate * (BLOCK - 1 - pos))
    scaled = (keys_b.astype(jnp.float32) * tail).astype(jnp.bfloat16)
    return _dot_tn(scaled, values_b)


def _summary_kernel(rates_ref, x_ref, g_ref, o_ref, *, hg, head_dim, nblocks):
    step = pl.program_id(0)
    pos = lax.broadcasted_iota(jnp.int32, (BLOCK, 1), 0).astype(jnp.float32)
    for hh in range(hg):
        rate = jnp.full((1, 1), rates_ref[step * hg + hh], jnp.float32)
        cols = slice(hh * head_dim, (hh + 1) * head_dim)
        decay = jnp.exp(-rate * BLOCK)
        acc = None
        for b in range(nblocks):
            rows = slice(b * BLOCK, (b + 1) * BLOCK)
            x = x_ref[0, rows, cols].astype(jnp.float32)
            keys_b = (_silu(x * g_ref[0, 1:2, cols]) * head_dim ** (-0.5)).astype(jnp.bfloat16)
            values_b = (x * g_ref[0, 2:3, cols]).astype(jnp.bfloat16)
            update = _block_state(keys_b, values_b, rate, pos)
            acc = update if acc is None else decay * acc + update
        o_ref[hh] = acc.astype(o_ref.dtype)


def _output_kernel(rates_ref, x_ref, g_ref, go_ref, s_ref, *rest, hg, head_dim, nblocks, first):
    o_ref = rest[-1]
    step = pl.program_id(0) + first
    pos = lax.broadcasted_iota(jnp.int32, (BLOCK, 1), 0).astype(jnp.float32)
    pos_row = lax.broadcasted_iota(jnp.int32, (1, BLOCK), 1).astype(jnp.float32)
    row = lax.broadcasted_iota(jnp.int32, (BLOCK, BLOCK), 0)
    col = lax.broadcasted_iota(jnp.int32, (BLOCK, BLOCK), 1)
    causal = row >= col
    for hh in range(hg):
        rate = jnp.full((1, 1), rates_ref[step * hg + hh], jnp.float32)
        cols = slice(hh * head_dim, (hh + 1) * head_dim)
        lead = jnp.exp(-rate * (pos + 1.0))
        mask = jnp.where(causal, lead * jnp.exp(rate * (pos_row + 1.0)), 0.0)
        decay = jnp.exp(-rate * BLOCK)
        state = s_ref[hh].astype(jnp.float32)
        for b in range(nblocks):
            rows = slice(b * BLOCK, (b + 1) * BLOCK)
            x = x_ref[0, rows, cols].astype(jnp.float32)
            queries_b = _silu(x * g_ref[0, 0:1, cols]).astype(jnp.bfloat16)
            keys_b = (_silu(x * g_ref[0, 1:2, cols]) * head_dim ** (-0.5)).astype(jnp.bfloat16)
            values_b = (x * g_ref[0, 2:3, cols]).astype(jnp.bfloat16)
            scores = _dot_nt(queries_b, keys_b)
            weights = (scores * mask).astype(jnp.bfloat16)
            scaled_q = (queries_b.astype(jnp.float32) * lead).astype(jnp.bfloat16)
            total = _dot(
                jnp.concatenate([weights, scaled_q], axis=1),
                jnp.concatenate([values_b, state.astype(jnp.bfloat16)], axis=0),
            )
            normed = total * lax.rsqrt(jnp.mean(total * total, axis=-1, keepdims=True) + EPSILON)
            o_ref[0, rows, cols] = (x + normed * go_ref[0:1, cols]).astype(o_ref.dtype)
            if b + 1 < nblocks:
                state = decay * state + _block_state(keys_b, values_b, rate, pos)


def _scan_kernel(place_ref, rates_ref, s_ref, c_ref, p_ref, e_ref, *, count, own, sources):
    for hh in range(own):
        rate = jnp.full((1, 1), rates_ref[place_ref[0] * own + hh], jnp.float32)
        decay = jnp.exp(-rate * count)
        state = c_ref[0, hh]
        for c in range(sources):
            p_ref[c, hh] = state.astype(p_ref.dtype)
            state = decay * state + s_ref[c, hh].astype(jnp.float32)
        e_ref[0, hh] = state


def _scan(place, rates, gathered, carry, count):
    sources, own, hd, _ = gathered.shape
    kernel = functools.partial(_scan_kernel, count=count, own=own, sources=sources)
    return pl.pallas_call(
        kernel,
        grid_spec=pltpu.PrefetchScalarGridSpec(
            num_scalar_prefetch=2,
            grid=(1,),
            in_specs=[
                pl.BlockSpec((sources, own, hd, hd), lambda i, p, r: (0, 0, 0, 0)),
                pl.BlockSpec((1, own, hd, hd), lambda i, p, r: (0, p[0], 0, 0)),
            ],
            out_specs=[
                pl.BlockSpec((sources, own, hd, hd), lambda i, p, r: (0, 0, 0, 0)),
                pl.BlockSpec((1, own, hd, hd), lambda i, p, r: (0, 0, 0, 0)),
            ],
        ),
        out_shape=[
            jax.ShapeDtypeStruct(gathered.shape, gathered.dtype),
            jax.ShapeDtypeStruct((1, own, hd, hd), jnp.float32),
        ],
        cost_estimate=pl.CostEstimate(
            flops=2 * gathered.size, transcendentals=0,
            bytes_accessed=4 * gathered.size + 8 * own * hd * hd,
        ),
    )(place, rates, gathered, carry)


def _summaries(rates, rows, gains, head_dim):
    _, count, width = rows.shape
    heads = width // head_dim
    hg = SUMMARY_HEADS_PER_STEP
    cw = hg * head_dim
    kernel = functools.partial(_summary_kernel, hg=hg, head_dim=head_dim, nblocks=count // BLOCK)
    return pl.pallas_call(
        kernel,
        grid_spec=pltpu.PrefetchScalarGridSpec(
            num_scalar_prefetch=1,
            grid=(heads // hg,),
            in_specs=[
                pl.BlockSpec((1, count, cw), lambda i, r: (0, 0, i)),
                pl.BlockSpec((1, 3, cw), lambda i, r: (0, 0, i)),
            ],
            out_specs=pl.BlockSpec((hg, head_dim, head_dim), lambda i, r: (i, 0, 0)),
        ),
        out_shape=jax.ShapeDtypeStruct((heads, head_dim, head_dim), jnp.bfloat16),
        cost_estimate=pl.CostEstimate(
            flops=2 * count * width * head_dim, transcendentals=count * width,
            bytes_accessed=count * width * 2 + heads * head_dim * head_dim * 4,
        ),
    )(rates, rows, gains)


def _outputs(rates, rows, gains, gain_out, states, head_dim, first, previous):
    _, count, width = rows.shape
    hg = HEADS_PER_STEP
    cw = hg * head_dim
    steps = states.shape[0] // hg
    base = first // hg
    kernel = functools.partial(
        _output_kernel, hg=hg, head_dim=head_dim, nblocks=count // BLOCK, first=base
    )
    row_spec = pl.BlockSpec((1, count, cw), lambda i, r: (0, 0, i + base))
    in_specs = [
        row_spec,
        pl.BlockSpec((1, 3, cw), lambda i, r: (0, 0, i + base)),
        pl.BlockSpec((1, cw), lambda i, r: (0, i + base)),
        pl.BlockSpec((hg, head_dim, head_dim), lambda i, r: (i, 0, 0)),
    ]
    operands = [rates, rows, gains, gain_out, states]
    aliases = {}
    if previous is not None:
        in_specs.append(pl.BlockSpec(memory_space=pl.ANY))
        operands.append(previous)
        aliases = {len(operands) - 1: 0}
    share = steps * cw
    return pl.pallas_call(
        kernel,
        grid_spec=pltpu.PrefetchScalarGridSpec(
            num_scalar_prefetch=1,
            grid=(steps,),
            in_specs=in_specs,
            out_specs=row_spec,
        ),
        out_shape=jax.ShapeDtypeStruct(rows.shape, rows.dtype),
        input_output_aliases=aliases,
        cost_estimate=pl.CostEstimate(
            flops=8 * count * BLOCK * share, transcendentals=3 * count * share,
            bytes_accessed=2 * count * share * 2 + steps * hg * head_dim * head_dim * 2,
        ),
    )(*operands)


def on_device(section_inputs, input_gains, out_gain, decay_rates, carry_state):
    _, count, width = section_inputs.shape
    rates = decay_rates[0]
    heads = rates.shape[0]
    head_dim = width // heads
    group_size = lax.axis_size("ctx")
    own_heads = heads // group_size
    place = lax.axis_index("ctx")
    count_s = lax.axis_size("section")
    pairs = [(src, (src + 1) % count_s) for src in range(count_s)]

    prev_rows, prev_gains, prev_gain_out, prev_rates = lax.ppermute(
        (section_inputs, input_gains, out_gain, decay_rates), "section", pairs
    )

    summary = _summaries(rates, section_inputs, input_gains, head_dim)
    gathered = lax.all_to_all(summary, "ctx", 0, 0, tiled=True)
    gathered = gathered.reshape(group_size, own_heads, head_dim, head_dim)
    prefixes, end_part = _scan(
        place.reshape(1).astype(jnp.int32), rates, gathered, carry_state, count
    )
    incoming = lax.all_to_all(
        prefixes.reshape(heads, head_dim, head_dim), "ctx", 0, 0, tiled=True
    )
    prev_gains, prev_gain_out, prev_rates, incoming = lax.optimization_barrier(
        (prev_gains, prev_gain_out, prev_rates, incoming)
    )
    chunk = heads // STATE_CHUNKS
    next_rows = None
    for part in range(STATE_CHUNKS):
        piece = lax.ppermute(incoming[part * chunk : (part + 1) * chunk], "section", pairs)
        next_rows = _outputs(
            prev_rates[0], prev_rows, prev_gains, prev_gain_out, piece, head_dim,
            part * chunk, next_rows,
        )
    return (next_rows, end_part)


def solution(mesh):
    return jax.shard_map(
        on_device,
        mesh=mesh,
        in_specs=(
            P("section", "ctx", None),
            P("section", None, None),
            P("section", None),
            P("section", None),
            P("section", None, None, None),
        ),
        out_specs=(P("section", "ctx", None), P("section", "ctx", None, None)),
        check_vma=False,
    )
```

```python
import functools

import jax
import jax.numpy as jnp
from jax import lax
from jax.experimental import pallas as pl
from jax.experimental.pallas import tpu as pltpu
from jax.sharding import PartitionSpec as P

BLOCK = 256
EPSILON = 1e-05
HEADS_PER_STEP = 6
SUMMARY_HEADS_PER_STEP = 12
STATE_CHUNKS = 4


def _silu(v):
    return 0.5 * v * (1.0 + jnp.tanh(0.5 * v))


def _dot_nt(a, b):
    return lax.dot_general(a, b, (((1,), (1,)), ((), ())), preferred_element_type=jnp.float32)


def _dot_tn(a, b):
    return lax.dot_general(a, b, (((0,), (0,)), ((), ())), preferred_element_type=jnp.float32)


def _dot(a, b):
    return lax.dot_general(a, b, (((1,), (0,)), ((), ())), preferred_element_type=jnp.float32)


def _block_state(keys_b, values_b, rate, pos):
    tail = jnp.exp(-rate * (BLOCK - 1 - pos))
    scaled = (keys_b.astype(jnp.float32) * tail).astype(jnp.bfloat16)
    return _dot_tn(scaled, values_b)


def _summary_kernel(rates_ref, x_ref, g_ref, o_ref, *, hg, head_dim, nblocks):
    step = pl.program_id(0)
    pos = lax.broadcasted_iota(jnp.int32, (BLOCK, 1), 0).astype(jnp.float32)
    for hh in range(hg):
        rate = jnp.full((1, 1), rates_ref[step * hg + hh], jnp.float32)
        cols = slice(hh * head_dim, (hh + 1) * head_dim)
        decay = jnp.exp(-rate * BLOCK)
        acc = None
        for b in range(nblocks):
            rows = slice(b * BLOCK, (b + 1) * BLOCK)
            x = x_ref[0, rows, cols].astype(jnp.float32)
            keys_b = (_silu(x * g_ref[0, 1:2, cols]) * head_dim ** (-0.5)).astype(jnp.bfloat16)
            values_b = (x * g_ref[0, 2:3, cols]).astype(jnp.bfloat16)
            update = _block_state(keys_b, values_b, rate, pos)
            acc = update if acc is None else decay * acc + update
        o_ref[hh] = acc.astype(o_ref.dtype)


def _output_kernel(rates_ref, x_ref, g_ref, go_ref, s_ref, *rest, hg, head_dim, nblocks, first):
    o_ref = rest[-1]
    step = pl.program_id(0) + first
    pos = lax.broadcasted_iota(jnp.int32, (BLOCK, 1), 0).astype(jnp.float32)
    pos_row = lax.broadcasted_iota(jnp.int32, (1, BLOCK), 1).astype(jnp.float32)
    row = lax.broadcasted_iota(jnp.int32, (BLOCK, BLOCK), 0)
    col = lax.broadcasted_iota(jnp.int32, (BLOCK, BLOCK), 1)
    causal = row >= col
    for hh in range(hg):
        rate = jnp.full((1, 1), rates_ref[step * hg + hh], jnp.float32)
        cols = slice(hh * head_dim, (hh + 1) * head_dim)
        lead = jnp.exp(-rate * (pos + 1.0))
        mask = jnp.where(causal, lead * jnp.exp(rate * (pos_row + 1.0)), 0.0)
        decay = jnp.exp(-rate * BLOCK)
        state = s_ref[hh].astype(jnp.float32)
        for b in range(nblocks):
            rows = slice(b * BLOCK, (b + 1) * BLOCK)
            x = x_ref[0, rows, cols].astype(jnp.float32)
            queries_b = _silu(x * g_ref[0, 0:1, cols]).astype(jnp.bfloat16)
            keys_b = (_silu(x * g_ref[0, 1:2, cols]) * head_dim ** (-0.5)).astype(jnp.bfloat16)
            values_b = (x * g_ref[0, 2:3, cols]).astype(jnp.bfloat16)
            scores = _dot_nt(queries_b, keys_b)
            weights = (scores * mask).astype(jnp.bfloat16)
            local = _dot(weights, values_b)
            cross = _dot(queries_b, state.astype(jnp.bfloat16))
            total = local + lead * cross
            normed = total * lax.rsqrt(jnp.mean(total * total, axis=-1, keepdims=True) + EPSILON)
            o_ref[0, rows, cols] = (x + normed * go_ref[0:1, cols]).astype(o_ref.dtype)
            if b + 1 < nblocks:
                state = decay * state + _block_state(keys_b, values_b, rate, pos)


def _scan_kernel(place_ref, rates_ref, s_ref, c_ref, p_ref, e_ref, *, count, own, sources):
    rate = jnp.full((1, 1), rates_ref[place_ref[0] * own + pl.program_id(0)], jnp.float32)
    decay = jnp.exp(-rate * count)
    state = c_ref[0, 0]
    for c in range(sources):
        p_ref[c, 0] = state.astype(p_ref.dtype)
        state = decay * state + s_ref[c, 0].astype(jnp.float32)
    e_ref[0, 0] = state


def _scan(place, rates, gathered, carry, count):
    sources, own, hd, _ = gathered.shape
    kernel = functools.partial(_scan_kernel, count=count, own=own, sources=sources)
    return pl.pallas_call(
        kernel,
        grid_spec=pltpu.PrefetchScalarGridSpec(
            num_scalar_prefetch=2,
            grid=(own,),
            in_specs=[
                pl.BlockSpec((sources, 1, hd, hd), lambda i, p, r: (0, i, 0, 0)),
                pl.BlockSpec((1, 1, hd, hd), lambda i, p, r: (0, p[0] * own + i, 0, 0)),
            ],
            out_specs=[
                pl.BlockSpec((sources, 1, hd, hd), lambda i, p, r: (0, i, 0, 0)),
                pl.BlockSpec((1, 1, hd, hd), lambda i, p, r: (0, i, 0, 0)),
            ],
        ),
        out_shape=[
            jax.ShapeDtypeStruct(gathered.shape, gathered.dtype),
            jax.ShapeDtypeStruct((1, own, hd, hd), jnp.float32),
        ],
        cost_estimate=pl.CostEstimate(
            flops=2 * gathered.size, transcendentals=0,
            bytes_accessed=4 * gathered.size + 8 * own * hd * hd,
        ),
    )(place, rates, gathered, carry)


def _summaries(rates, rows, gains, head_dim):
    _, count, width = rows.shape
    heads = width // head_dim
    hg = SUMMARY_HEADS_PER_STEP
    cw = hg * head_dim
    kernel = functools.partial(_summary_kernel, hg=hg, head_dim=head_dim, nblocks=count // BLOCK)
    return pl.pallas_call(
        kernel,
        grid_spec=pltpu.PrefetchScalarGridSpec(
            num_scalar_prefetch=1,
            grid=(heads // hg,),
            in_specs=[
                pl.BlockSpec((1, count, cw), lambda i, r: (0, 0, i)),
                pl.BlockSpec((1, 3, cw), lambda i, r: (0, 0, i)),
            ],
            out_specs=pl.BlockSpec((hg, head_dim, head_dim), lambda i, r: (i, 0, 0)),
        ),
        out_shape=jax.ShapeDtypeStruct((heads, head_dim, head_dim), jnp.bfloat16),
        cost_estimate=pl.CostEstimate(
            flops=2 * count * width * head_dim, transcendentals=count * width,
            bytes_accessed=count * width * 2 + heads * head_dim * head_dim * 4,
        ),
    )(rates, rows, gains)


def _outputs(rates, rows, gains, gain_out, states, head_dim, first, previous):
    _, count, width = rows.shape
    hg = HEADS_PER_STEP
    cw = hg * head_dim
    steps = states.shape[0] // hg
    base = first // hg
    kernel = functools.partial(
        _output_kernel, hg=hg, head_dim=head_dim, nblocks=count // BLOCK, first=base
    )
    row_spec = pl.BlockSpec((1, count, cw), lambda i, r: (0, 0, i + base))
    in_specs = [
        row_spec,
        pl.BlockSpec((1, 3, cw), lambda i, r: (0, 0, i + base)),
        pl.BlockSpec((1, cw), lambda i, r: (0, i + base)),
        pl.BlockSpec((hg, head_dim, head_dim), lambda i, r: (i, 0, 0)),
    ]
    operands = [rates, rows, gains, gain_out, states]
    aliases = {}
    if previous is not None:
        in_specs.append(pl.BlockSpec(memory_space=pl.ANY))
        operands.append(previous)
        aliases = {len(operands) - 1: 0}
    share = steps * cw
    return pl.pallas_call(
        kernel,
        grid_spec=pltpu.PrefetchScalarGridSpec(
            num_scalar_prefetch=1,
            grid=(steps,),
            in_specs=in_specs,
            out_specs=row_spec,
        ),
        out_shape=jax.ShapeDtypeStruct(rows.shape, rows.dtype),
        input_output_aliases=aliases,
        cost_estimate=pl.CostEstimate(
            flops=8 * count * BLOCK * share, transcendentals=3 * count * share,
            bytes_accessed=2 * count * share * 2 + steps * hg * head_dim * head_dim * 2,
        ),
    )(*operands)


def on_device(section_inputs, input_gains, out_gain, decay_rates, carry_state):
    _, count, width = section_inputs.shape
    rates = decay_rates[0]
    heads = rates.shape[0]
    head_dim = width // heads
    group_size = lax.axis_size("ctx")
    own_heads = heads // group_size
    place = lax.axis_index("ctx")
    count_s = lax.axis_size("section")
    pairs = [(src, (src + 1) % count_s) for src in range(count_s)]

    prev_rows, prev_gains, prev_gain_out, prev_rates = lax.ppermute(
        (section_inputs, input_gains, out_gain, decay_rates), "section", pairs
    )

    summary = _summaries(rates, section_inputs, input_gains, head_dim)
    gathered = lax.all_to_all(summary, "ctx", 0, 0, tiled=True)
    gathered = gathered.reshape(group_size, own_heads, head_dim, head_dim)
    prefixes, end_part = _scan(
        place.reshape(1).astype(jnp.int32), rates, gathered, carry_state, count
    )
    incoming = lax.all_to_all(
        prefixes.reshape(heads, head_dim, head_dim), "ctx", 0, 0, tiled=True
    )
    prev_gains, prev_gain_out, prev_rates, incoming = lax.optimization_barrier(
        (prev_gains, prev_gain_out, prev_rates, incoming)
    )
    chunk = heads // STATE_CHUNKS
    next_rows = None
    for part in range(STATE_CHUNKS):
        piece = lax.ppermute(incoming[part * chunk : (part + 1) * chunk], "section", pairs)
        next_rows = _outputs(
            prev_rates[0], prev_rows, prev_gains, prev_gain_out, piece, head_dim,
            part * chunk, next_rows,
        )
    return (next_rows, end_part)


def solution(mesh):
    return jax.shard_map(
        on_device,
        mesh=mesh,
        in_specs=(
            P("section", "ctx", None),
            P("section", None, None),
            P("section", None),
            P("section", None),
            P("section", None, None, None),
        ),
        out_specs=(P("section", "ctx", None), P("section", "ctx", None, None)),
        check_vma=False,
    )
```

```python
import functools

import jax
import jax.numpy as jnp
from jax import lax
from jax.experimental import pallas as pl
from jax.experimental.pallas import tpu as pltpu
from jax.sharding import PartitionSpec as P

BLOCK = 256
EPSILON = 1e-05
HEADS_PER_STEP = 6
SUMMARY_HEADS_PER_STEP = 16
STATE_CHUNKS = 4


def _silu(v):
    return 0.5 * v * (1.0 + jnp.tanh(0.5 * v))


def _dot_nt(a, b):
    return lax.dot_general(a, b, (((1,), (1,)), ((), ())), preferred_element_type=jnp.float32)


def _dot_tn(a, b):
    return lax.dot_general(a, b, (((0,), (0,)), ((), ())), preferred_element_type=jnp.float32)


def _dot(a, b):
    return lax.dot_general(a, b, (((1,), (0,)), ((), ())), preferred_element_type=jnp.float32)


def _block_state(keys_b, values_b, rate, pos):
    tail = jnp.exp(-rate * (BLOCK - 1 - pos))
    scaled = (keys_b.astype(jnp.float32) * tail).astype(jnp.bfloat16)
    return _dot_tn(scaled, values_b)


def _summary_kernel(rates_ref, x_ref, g_ref, o_ref, *, hg, head_dim, nblocks):
    step = pl.program_id(0)
    pos = lax.broadcasted_iota(jnp.int32, (BLOCK, 1), 0).astype(jnp.float32)
    for hh in range(hg):
        rate = jnp.full((1, 1), rates_ref[step * hg + hh], jnp.float32)
        cols = slice(hh * head_dim, (hh + 1) * head_dim)
        decay = jnp.exp(-rate * BLOCK)
        acc = None
        for b in range(nblocks):
            rows = slice(b * BLOCK, (b + 1) * BLOCK)
            x = x_ref[0, rows, cols].astype(jnp.float32)
            keys_b = (_silu(x * g_ref[0, 1:2, cols]) * head_dim ** (-0.5)).astype(jnp.bfloat16)
            values_b = (x * g_ref[0, 2:3, cols]).astype(jnp.bfloat16)
            update = _block_state(keys_b, values_b, rate, pos)
            acc = update if acc is None else decay * acc + update
        o_ref[hh] = acc.astype(o_ref.dtype)


def _output_kernel(rates_ref, x_ref, g_ref, go_ref, s_ref, *rest, hg, head_dim, nblocks, first):
    o_ref = rest[-1]
    step = pl.program_id(0) + first
    pos = lax.broadcasted_iota(jnp.int32, (BLOCK, 1), 0).astype(jnp.float32)
    pos_row = lax.broadcasted_iota(jnp.int32, (1, BLOCK), 1).astype(jnp.float32)
    row = lax.broadcasted_iota(jnp.int32, (BLOCK, BLOCK), 0)
    col = lax.broadcasted_iota(jnp.int32, (BLOCK, BLOCK), 1)
    causal = row >= col
    for hh in range(hg):
        rate = jnp.full((1, 1), rates_ref[step * hg + hh], jnp.float32)
        cols = slice(hh * head_dim, (hh + 1) * head_dim)
        lead = jnp.exp(-rate * (pos + 1.0))
        mask = jnp.where(causal, lead * jnp.exp(rate * (pos_row + 1.0)), 0.0)
        decay = jnp.exp(-rate * BLOCK)
        state = s_ref[hh].astype(jnp.float32)
        for b in range(nblocks):
            rows = slice(b * BLOCK, (b + 1) * BLOCK)
            x = x_ref[0, rows, cols].astype(jnp.float32)
            queries_b = _silu(x * g_ref[0, 0:1, cols]).astype(jnp.bfloat16)
            keys_b = (_silu(x * g_ref[0, 1:2, cols]) * head_dim ** (-0.5)).astype(jnp.bfloat16)
            values_b = (x * g_ref[0, 2:3, cols]).astype(jnp.bfloat16)
            scores = _dot_nt(queries_b, keys_b)
            weights = (scores * mask).astype(jnp.bfloat16)
            local = _dot(weights, values_b)
            cross = _dot(queries_b, state.astype(jnp.bfloat16))
            total = local + lead * cross
            normed = total * lax.rsqrt(jnp.mean(total * total, axis=-1, keepdims=True) + EPSILON)
            o_ref[0, rows, cols] = (x + normed * go_ref[0:1, cols]).astype(o_ref.dtype)
            if b + 1 < nblocks:
                state = decay * state + _block_state(keys_b, values_b, rate, pos)


def _scan_kernel(place_ref, rates_ref, s_ref, c_ref, p_ref, e_ref, *, count, own, sources):
    for hh in range(own):
        rate = jnp.full((1, 1), rates_ref[place_ref[0] * own + hh], jnp.float32)
        decay = jnp.exp(-rate * count)
        state = c_ref[0, hh]
        for c in range(sources):
            p_ref[c, hh] = state.astype(p_ref.dtype)
            state = decay * state + s_ref[c, hh].astype(jnp.float32)
        e_ref[0, hh] = state


def _scan(place, rates, gathered, carry, count):
    sources, own, hd, _ = gathered.shape
    kernel = functools.partial(_scan_kernel, count=count, own=own, sources=sources)
    return pl.pallas_call(
        kernel,
        grid_spec=pltpu.PrefetchScalarGridSpec(
            num_scalar_prefetch=2,
            grid=(1,),
            in_specs=[
                pl.BlockSpec((sources, own, hd, hd), lambda i, p, r: (0, 0, 0, 0)),
                pl.BlockSpec((1, own, hd, hd), lambda i, p, r: (0, p[0], 0, 0)),
            ],
            out_specs=[
                pl.BlockSpec((sources, own, hd, hd), lambda i, p, r: (0, 0, 0, 0)),
                pl.BlockSpec((1, own, hd, hd), lambda i, p, r: (0, 0, 0, 0)),
            ],
        ),
        out_shape=[
            jax.ShapeDtypeStruct(gathered.shape, gathered.dtype),
            jax.ShapeDtypeStruct((1, own, hd, hd), jnp.float32),
        ],
        cost_estimate=pl.CostEstimate(
            flops=2 * gathered.size, transcendentals=0,
            bytes_accessed=4 * gathered.size + 8 * own * hd * hd,
        ),
    )(place, rates, gathered, carry)


def _summaries(rates, rows, gains, head_dim):
    _, count, width = rows.shape
    heads = width // head_dim
    hg = SUMMARY_HEADS_PER_STEP
    cw = hg * head_dim
    kernel = functools.partial(_summary_kernel, hg=hg, head_dim=head_dim, nblocks=count // BLOCK)
    return pl.pallas_call(
        kernel,
        grid_spec=pltpu.PrefetchScalarGridSpec(
            num_scalar_prefetch=1,
            grid=(heads // hg,),
            in_specs=[
                pl.BlockSpec((1, count, cw), lambda i, r: (0, 0, i)),
                pl.BlockSpec((1, 3, cw), lambda i, r: (0, 0, i)),
            ],
            out_specs=pl.BlockSpec((hg, head_dim, head_dim), lambda i, r: (i, 0, 0)),
        ),
        out_shape=jax.ShapeDtypeStruct((heads, head_dim, head_dim), jnp.bfloat16),
        cost_estimate=pl.CostEstimate(
            flops=2 * count * width * head_dim, transcendentals=count * width,
            bytes_accessed=count * width * 2 + heads * head_dim * head_dim * 4,
        ),
    )(rates, rows, gains)


def _outputs(rates, rows, gains, gain_out, states, head_dim, first, previous):
    _, count, width = rows.shape
    hg = HEADS_PER_STEP
    cw = hg * head_dim
    steps = states.shape[0] // hg
    base = first // hg
    kernel = functools.partial(
        _output_kernel, hg=hg, head_dim=head_dim, nblocks=count // BLOCK, first=base
    )
    row_spec = pl.BlockSpec((1, count, cw), lambda i, r: (0, 0, i + base))
    in_specs = [
        row_spec,
        pl.BlockSpec((1, 3, cw), lambda i, r: (0, 0, i + base)),
        pl.BlockSpec((1, cw), lambda i, r: (0, i + base)),
        pl.BlockSpec((hg, head_dim, head_dim), lambda i, r: (i, 0, 0)),
    ]
    operands = [rates, rows, gains, gain_out, states]
    aliases = {}
    if previous is not None:
        in_specs.append(pl.BlockSpec(memory_space=pl.ANY))
        operands.append(previous)
        aliases = {len(operands) - 1: 0}
    share = steps * cw
    return pl.pallas_call(
        kernel,
        grid_spec=pltpu.PrefetchScalarGridSpec(
            num_scalar_prefetch=1,
            grid=(steps,),
            in_specs=in_specs,
            out_specs=row_spec,
        ),
        out_shape=jax.ShapeDtypeStruct(rows.shape, rows.dtype),
        input_output_aliases=aliases,
        cost_estimate=pl.CostEstimate(
            flops=8 * count * BLOCK * share, transcendentals=3 * count * share,
            bytes_accessed=2 * count * share * 2 + steps * hg * head_dim * head_dim * 2,
        ),
    )(*operands)


def on_device(section_inputs, input_gains, out_gain, decay_rates, carry_state):
    _, count, width = section_inputs.shape
    rates = decay_rates[0]
    heads = rates.shape[0]
    head_dim = width // heads
    group_size = lax.axis_size("ctx")
    own_heads = heads // group_size
    place = lax.axis_index("ctx")
    count_s = lax.axis_size("section")
    pairs = [(src, (src + 1) % count_s) for src in range(count_s)]

    prev_rows, prev_gains, prev_gain_out, prev_rates = lax.ppermute(
        (section_inputs, input_gains, out_gain, decay_rates), "section", pairs
    )

    summary = _summaries(rates, section_inputs, input_gains, head_dim)
    gathered = lax.all_to_all(summary, "ctx", 0, 0, tiled=True)
    gathered = gathered.reshape(group_size, own_heads, head_dim, head_dim)
    prefixes, end_part = _scan(
        place.reshape(1).astype(jnp.int32), rates, gathered, carry_state, count
    )
    incoming = lax.all_to_all(
        prefixes.reshape(heads, head_dim, head_dim), "ctx", 0, 0, tiled=True
    )
    prev_gains, prev_gain_out, prev_rates, incoming = lax.optimization_barrier(
        (prev_gains, prev_gain_out, prev_rates, incoming)
    )
    chunk = heads // STATE_CHUNKS
    next_rows = None
    for part in range(STATE_CHUNKS):
        piece = lax.ppermute(incoming[part * chunk : (part + 1) * chunk], "section", pairs)
        next_rows = _outputs(
            prev_rates[0], prev_rows, prev_gains, prev_gain_out, piece, head_dim,
            part * chunk, next_rows,
        )
    return (next_rows, end_part)


def solution(mesh):
    return jax.shard_map(
        on_device,
        mesh=mesh,
        in_specs=(
            P("section", "ctx", None),
            P("section", None, None),
            P("section", None),
            P("section", None),
            P("section", None, None, None),
        ),
        out_specs=(P("section", "ctx", None), P("section", "ctx", None, None)),
        check_vma=False,
    )
```

```python
import functools

import jax
import jax.numpy as jnp
from jax import lax
from jax.experimental import pallas as pl
from jax.experimental.pallas import tpu as pltpu
from jax.sharding import PartitionSpec as P

BLOCK = 256
EPSILON = 1e-05
HEADS_PER_STEP = 6
SUMMARY_HEADS_PER_STEP = 12
STATE_CHUNKS = 4


def _silu(v):
    return 0.5 * v * (1.0 + jnp.tanh(0.5 * v))


def _dot_nt(a, b):
    return lax.dot_general(a, b, (((1,), (1,)), ((), ())), preferred_element_type=jnp.float32)


def _dot_tn(a, b):
    return lax.dot_general(a, b, (((0,), (0,)), ((), ())), preferred_element_type=jnp.float32)


def _dot(a, b):
    return lax.dot_general(a, b, (((1,), (0,)), ((), ())), preferred_element_type=jnp.float32)


def _block_state(keys_b, values_b, rate, pos):
    tail = jnp.exp(-rate * (BLOCK - 1 - pos))
    scaled = (keys_b.astype(jnp.float32) * tail).astype(jnp.bfloat16)
    return _dot_tn(scaled, values_b)


def _summary_kernel(rates_ref, x_ref, gk_ref, gv_ref, o_ref, *, hg, head_dim, nblocks):
    step = pl.program_id(0)
    pos = lax.broadcasted_iota(jnp.int32, (BLOCK, 1), 0).astype(jnp.float32)
    for hh in range(hg):
        rate = jnp.full((1, 1), rates_ref[step * hg + hh], jnp.float32)
        cols = slice(hh * head_dim, (hh + 1) * head_dim)
        decay = jnp.exp(-rate * BLOCK)
        acc = None
        for b in range(nblocks):
            rows = slice(b * BLOCK, (b + 1) * BLOCK)
            x = x_ref[0, rows, cols].astype(jnp.float32)
            keys_b = (_silu(x * gk_ref[0:1, cols]) * head_dim ** (-0.5)).astype(jnp.bfloat16)
            values_b = (x * gv_ref[0:1, cols]).astype(jnp.bfloat16)
            update = _block_state(keys_b, values_b, rate, pos)
            acc = update if acc is None else decay * acc + update
        o_ref[hh] = acc.astype(o_ref.dtype)


def _output_kernel(rates_ref, x_ref, gq_ref, gk_ref, gv_ref, go_ref, s_ref, *rest, hg, head_dim, nblocks, first):
    o_ref = rest[-1]
    step = pl.program_id(0) + first
    pos = lax.broadcasted_iota(jnp.int32, (BLOCK, 1), 0).astype(jnp.float32)
    pos_row = lax.broadcasted_iota(jnp.int32, (1, BLOCK), 1).astype(jnp.float32)
    row = lax.broadcasted_iota(jnp.int32, (BLOCK, BLOCK), 0)
    col = lax.broadcasted_iota(jnp.int32, (BLOCK, BLOCK), 1)
    causal = row >= col
    for hh in range(hg):
        rate = jnp.full((1, 1), rates_ref[step * hg + hh], jnp.float32)
        cols = slice(hh * head_dim, (hh + 1) * head_dim)
        lead = jnp.exp(-rate * (pos + 1.0))
        mask = jnp.where(causal, lead * jnp.exp(rate * (pos_row + 1.0)), 0.0)
        decay = jnp.exp(-rate * BLOCK)
        state = s_ref[hh].astype(jnp.float32)
        for b in range(nblocks):
            rows = slice(b * BLOCK, (b + 1) * BLOCK)
            x = x_ref[0, rows, cols].astype(jnp.float32)
            queries_b = _silu(x * gq_ref[0:1, cols]).astype(jnp.bfloat16)
            keys_b = (_silu(x * gk_ref[0:1, cols]) * head_dim ** (-0.5)).astype(jnp.bfloat16)
            values_b = (x * gv_ref[0:1, cols]).astype(jnp.bfloat16)
            scores = _dot_nt(queries_b, keys_b)
            weights = (scores * mask).astype(jnp.bfloat16)
            local = _dot(weights, values_b)
            cross = _dot(queries_b, state.astype(jnp.bfloat16))
            total = local + lead * cross
            normed = total * lax.rsqrt(jnp.mean(total * total, axis=-1, keepdims=True) + EPSILON)
            o_ref[0, rows, cols] = (x + normed * go_ref[0:1, cols]).astype(o_ref.dtype)
            if b + 1 < nblocks:
                state = decay * state + _block_state(keys_b, values_b, rate, pos)


def _scan_kernel(place_ref, rates_ref, s_ref, c_ref, p_ref, e_ref, *, count, own, sources):
    for hh in range(own):
        rate = jnp.full((1, 1), rates_ref[place_ref[0] * own + hh], jnp.float32)
        decay = jnp.exp(-rate * count)
        state = c_ref[0, hh]
        for c in range(sources):
            p_ref[c, hh] = state.astype(p_ref.dtype)
            state = decay * state + s_ref[c, hh].astype(jnp.float32)
        e_ref[0, hh] = state


def _scan(place, rates, gathered, carry, count):
    sources, own, hd, _ = gathered.shape
    kernel = functools.partial(_scan_kernel, count=count, own=own, sources=sources)
    return pl.pallas_call(
        kernel,
        grid_spec=pltpu.PrefetchScalarGridSpec(
            num_scalar_prefetch=2,
            grid=(1,),
            in_specs=[
                pl.BlockSpec((sources, own, hd, hd), lambda i, p, r: (0, 0, 0, 0)),
                pl.BlockSpec((1, own, hd, hd), lambda i, p, r: (0, p[0], 0, 0)),
            ],
            out_specs=[
                pl.BlockSpec((sources, own, hd, hd), lambda i, p, r: (0, 0, 0, 0)),
                pl.BlockSpec((1, own, hd, hd), lambda i, p, r: (0, 0, 0, 0)),
            ],
        ),
        out_shape=[
            jax.ShapeDtypeStruct(gathered.shape, gathered.dtype),
            jax.ShapeDtypeStruct((1, own, hd, hd), jnp.float32),
        ],
        cost_estimate=pl.CostEstimate(
            flops=2 * gathered.size, transcendentals=0,
            bytes_accessed=4 * gathered.size + 8 * own * hd * hd,
        ),
    )(place, rates, gathered, carry)


def _summaries(rates, rows, gains, head_dim):
    _, count, width = rows.shape
    heads = width // head_dim
    hg = SUMMARY_HEADS_PER_STEP
    cw = hg * head_dim
    per_row = width // cw
    kernel = functools.partial(_summary_kernel, hg=hg, head_dim=head_dim, nblocks=count // BLOCK)
    return pl.pallas_call(
        kernel,
        grid_spec=pltpu.PrefetchScalarGridSpec(
            num_scalar_prefetch=1,
            grid=(heads // hg,),
            in_specs=[
                pl.BlockSpec((1, count, cw), lambda i, r: (0, 0, i)),
                pl.BlockSpec((1, cw), lambda i, r: (0, i + per_row)),
                pl.BlockSpec((1, cw), lambda i, r: (0, i + 2 * per_row)),
            ],
            out_specs=pl.BlockSpec((hg, head_dim, head_dim), lambda i, r: (i, 0, 0)),
        ),
        out_shape=jax.ShapeDtypeStruct((heads, head_dim, head_dim), jnp.bfloat16),
        cost_estimate=pl.CostEstimate(
            flops=2 * count * width * head_dim, transcendentals=count * width,
            bytes_accessed=count * width * 2 + heads * head_dim * head_dim * 4,
        ),
    )(rates, rows, gains, gains)


def _outputs(rates, rows, gains, gain_out, states, head_dim, first, previous):
    _, count, width = rows.shape
    hg = HEADS_PER_STEP
    cw = hg * head_dim
    steps = states.shape[0] // hg
    base = first // hg
    kernel = functools.partial(
        _output_kernel, hg=hg, head_dim=head_dim, nblocks=count // BLOCK, first=base
    )
    row_spec = pl.BlockSpec((1, count, cw), lambda i, r: (0, 0, i + base))
    per_row = width // cw
    in_specs = [
        row_spec,
        pl.BlockSpec((1, cw), lambda i, r: (0, i + base)),
        pl.BlockSpec((1, cw), lambda i, r: (0, i + base + per_row)),
        pl.BlockSpec((1, cw), lambda i, r: (0, i + base + 2 * per_row)),
        pl.BlockSpec((1, cw), lambda i, r: (0, i + base)),
        pl.BlockSpec((hg, head_dim, head_dim), lambda i, r: (i, 0, 0)),
    ]
    operands = [rates, rows, gains, gains, gains, gain_out, states]
    aliases = {}
    if previous is not None:
        in_specs.append(pl.BlockSpec(memory_space=pl.ANY))
        operands.append(previous)
        aliases = {len(operands) - 1: 0}
    share = steps * cw
    return pl.pallas_call(
        kernel,
        grid_spec=pltpu.PrefetchScalarGridSpec(
            num_scalar_prefetch=1,
            grid=(steps,),
            in_specs=in_specs,
            out_specs=row_spec,
        ),
        out_shape=jax.ShapeDtypeStruct(rows.shape, rows.dtype),
        input_output_aliases=aliases,
        cost_estimate=pl.CostEstimate(
            flops=8 * count * BLOCK * share, transcendentals=3 * count * share,
            bytes_accessed=2 * count * share * 2 + steps * hg * head_dim * head_dim * 2,
        ),
    )(*operands)


def on_device(section_inputs, input_gains, out_gain, decay_rates, carry_state):
    _, count, width = section_inputs.shape
    rates = decay_rates[0]
    heads = rates.shape[0]
    head_dim = width // heads
    group_size = lax.axis_size("ctx")
    own_heads = heads // group_size
    place = lax.axis_index("ctx")
    count_s = lax.axis_size("section")
    pairs = [(src, (src + 1) % count_s) for src in range(count_s)]

    flat_gains = input_gains.reshape(1, -1)
    prev_rows, prev_gains, prev_gain_out, prev_rates = lax.ppermute(
        (section_inputs, flat_gains, out_gain, decay_rates), "section", pairs
    )

    summary = _summaries(rates, section_inputs, flat_gains, head_dim)
    gathered = lax.all_to_all(summary, "ctx", 0, 0, tiled=True)
    gathered = gathered.reshape(group_size, own_heads, head_dim, head_dim)
    prefixes, end_part = _scan(
        place.reshape(1).astype(jnp.int32), rates, gathered, carry_state, count
    )
    incoming = lax.all_to_all(
        prefixes.reshape(heads, head_dim, head_dim), "ctx", 0, 0, tiled=True
    )
    prev_gains, prev_gain_out, prev_rates, incoming = lax.optimization_barrier(
        (prev_gains, prev_gain_out, prev_rates, incoming)
    )
    chunk = heads // STATE_CHUNKS
    next_rows = None
    for part in range(STATE_CHUNKS):
        piece = lax.ppermute(incoming[part * chunk : (part + 1) * chunk], "section", pairs)
        next_rows = _outputs(
            prev_rates[0], prev_rows, prev_gains, prev_gain_out, piece, head_dim,
            part * chunk, next_rows,
        )
    return (next_rows, end_part)


def solution(mesh):
    return jax.shard_map(
        on_device,
        mesh=mesh,
        in_specs=(
            P("section", "ctx", None),
            P("section", None, None),
            P("section", None),
            P("section", None),
            P("section", None, None, None),
        ),
        out_specs=(P("section", "ctx", None), P("section", "ctx", None, None)),
        check_vma=False,
    )
```

```python
import functools

import jax
import jax.numpy as jnp
from jax import lax
from jax.experimental import pallas as pl
from jax.experimental.pallas import tpu as pltpu
from jax.sharding import PartitionSpec as P

BLOCK = 256
EPSILON = 1e-05
HEADS_PER_STEP = 6
SUMMARY_HEADS_PER_STEP = 12
STATE_CHUNKS = 2


def _silu(v):
    return 0.5 * v * (1.0 + jnp.tanh(0.5 * v))


def _dot_nt(a, b):
    return lax.dot_general(a, b, (((1,), (1,)), ((), ())), preferred_element_type=jnp.float32)


def _dot_tn(a, b):
    return lax.dot_general(a, b, (((0,), (0,)), ((), ())), preferred_element_type=jnp.float32)


def _dot(a, b):
    return lax.dot_general(a, b, (((1,), (0,)), ((), ())), preferred_element_type=jnp.float32)


def _block_state(keys_b, values_b, rate, pos):
    tail = jnp.exp(-rate * (BLOCK - 1 - pos))
    scaled = (keys_b.astype(jnp.float32) * tail).astype(jnp.bfloat16)
    return _dot_tn(scaled, values_b)


def _summary_kernel(rates_ref, x_ref, gk_ref, gv_ref, o_ref, *, hg, head_dim, nblocks):
    step = pl.program_id(0)
    pos = lax.broadcasted_iota(jnp.int32, (BLOCK, 1), 0).astype(jnp.float32)
    for hh in range(hg):
        rate = jnp.full((1, 1), rates_ref[step * hg + hh], jnp.float32)
        cols = slice(hh * head_dim, (hh + 1) * head_dim)
        decay = jnp.exp(-rate * BLOCK)
        acc = None
        for b in range(nblocks):
            rows = slice(b * BLOCK, (b + 1) * BLOCK)
            x = x_ref[0, rows, cols].astype(jnp.float32)
            keys_b = (_silu(x * gk_ref[0:1, cols]) * head_dim ** (-0.5)).astype(jnp.bfloat16)
            values_b = (x * gv_ref[0:1, cols]).astype(jnp.bfloat16)
            update = _block_state(keys_b, values_b, rate, pos)
            acc = update if acc is None else decay * acc + update
        o_ref[hh] = acc.astype(o_ref.dtype)


def _output_kernel(rates_ref, x_ref, gq_ref, gk_ref, gv_ref, go_ref, s_ref, *rest, hg, head_dim, nblocks, first):
    o_ref = rest[-1]
    step = pl.program_id(0) + first
    pos = lax.broadcasted_iota(jnp.int32, (BLOCK, 1), 0).astype(jnp.float32)
    pos_row = lax.broadcasted_iota(jnp.int32, (1, BLOCK), 1).astype(jnp.float32)
    row = lax.broadcasted_iota(jnp.int32, (BLOCK, BLOCK), 0)
    col = lax.broadcasted_iota(jnp.int32, (BLOCK, BLOCK), 1)
    causal = row >= col
    for hh in range(hg):
        rate = jnp.full((1, 1), rates_ref[step * hg + hh], jnp.float32)
        cols = slice(hh * head_dim, (hh + 1) * head_dim)
        lead = jnp.exp(-rate * (pos + 1.0))
        mask = jnp.where(causal, lead * jnp.exp(rate * (pos_row + 1.0)), 0.0)
        decay = jnp.exp(-rate * BLOCK)
        state = s_ref[hh].astype(jnp.float32)
        for b in range(nblocks):
            rows = slice(b * BLOCK, (b + 1) * BLOCK)
            x = x_ref[0, rows, cols].astype(jnp.float32)
            queries_b = _silu(x * gq_ref[0:1, cols]).astype(jnp.bfloat16)
            keys_b = (_silu(x * gk_ref[0:1, cols]) * head_dim ** (-0.5)).astype(jnp.bfloat16)
            values_b = (x * gv_ref[0:1, cols]).astype(jnp.bfloat16)
            scores = _dot_nt(queries_b, keys_b)
            weights = (scores * mask).astype(jnp.bfloat16)
            local = _dot(weights, values_b)
            cross = _dot(queries_b, state.astype(jnp.bfloat16))
            total = local + lead * cross
            normed = total * lax.rsqrt(jnp.mean(total * total, axis=-1, keepdims=True) + EPSILON)
            o_ref[0, rows, cols] = (x + normed * go_ref[0:1, cols]).astype(o_ref.dtype)
            if b + 1 < nblocks:
                state = decay * state + _block_state(keys_b, values_b, rate, pos)


def _scan_kernel(place_ref, rates_ref, s_ref, c_ref, p_ref, e_ref, *, count, own, sources):
    for hh in range(own):
        rate = jnp.full((1, 1), rates_ref[place_ref[0] * own + hh], jnp.float32)
        decay = jnp.exp(-rate * count)
        state = c_ref[0, hh]
        for c in range(sources):
            p_ref[c, hh] = state.astype(p_ref.dtype)
            state = decay * state + s_ref[c, hh].astype(jnp.float32)
        e_ref[0, hh] = state


def _scan(place, rates, gathered, carry, count):
    sources, own, hd, _ = gathered.shape
    kernel = functools.partial(_scan_kernel, count=count, own=own, sources=sources)
    return pl.pallas_call(
        kernel,
        grid_spec=pltpu.PrefetchScalarGridSpec(
            num_scalar_prefetch=2,
            grid=(1,),
            in_specs=[
                pl.BlockSpec((sources, own, hd, hd), lambda i, p, r: (0, 0, 0, 0)),
                pl.BlockSpec((1, own, hd, hd), lambda i, p, r: (0, p[0], 0, 0)),
            ],
            out_specs=[
                pl.BlockSpec((sources, own, hd, hd), lambda i, p, r: (0, 0, 0, 0)),
                pl.BlockSpec((1, own, hd, hd), lambda i, p, r: (0, 0, 0, 0)),
            ],
        ),
        out_shape=[
            jax.ShapeDtypeStruct(gathered.shape, gathered.dtype),
            jax.ShapeDtypeStruct((1, own, hd, hd), jnp.float32),
        ],
        cost_estimate=pl.CostEstimate(
            flops=2 * gathered.size, transcendentals=0,
            bytes_accessed=4 * gathered.size + 8 * own * hd * hd,
        ),
    )(place, rates, gathered, carry)


def _summaries(rates, rows, gains, head_dim):
    _, count, width = rows.shape
    heads = width // head_dim
    hg = SUMMARY_HEADS_PER_STEP
    cw = hg * head_dim
    per_row = width // cw
    kernel = functools.partial(_summary_kernel, hg=hg, head_dim=head_dim, nblocks=count // BLOCK)
    return pl.pallas_call(
        kernel,
        grid_spec=pltpu.PrefetchScalarGridSpec(
            num_scalar_prefetch=1,
            grid=(heads // hg,),
            in_specs=[
                pl.BlockSpec((1, count, cw), lambda i, r: (0, 0, i)),
                pl.BlockSpec((1, cw), lambda i, r: (0, i + per_row)),
                pl.BlockSpec((1, cw), lambda i, r: (0, i + 2 * per_row)),
            ],
            out_specs=pl.BlockSpec((hg, head_dim, head_dim), lambda i, r: (i, 0, 0)),
        ),
        out_shape=jax.ShapeDtypeStruct((heads, head_dim, head_dim), jnp.bfloat16),
        cost_estimate=pl.CostEstimate(
            flops=2 * count * width * head_dim, transcendentals=count * width,
            bytes_accessed=count * width * 2 + heads * head_dim * head_dim * 4,
        ),
    )(rates, rows, gains, gains)


def _outputs(rates, rows, gains, gain_out, states, head_dim, first, previous):
    _, count, width = rows.shape
    hg = HEADS_PER_STEP
    cw = hg * head_dim
    steps = states.shape[0] // hg
    base = first // hg
    kernel = functools.partial(
        _output_kernel, hg=hg, head_dim=head_dim, nblocks=count // BLOCK, first=base
    )
    row_spec = pl.BlockSpec((1, count, cw), lambda i, r: (0, 0, i + base))
    per_row = width // cw
    in_specs = [
        row_spec,
        pl.BlockSpec((1, cw), lambda i, r: (0, i + base)),
        pl.BlockSpec((1, cw), lambda i, r: (0, i + base + per_row)),
        pl.BlockSpec((1, cw), lambda i, r: (0, i + base + 2 * per_row)),
        pl.BlockSpec((1, cw), lambda i, r: (0, i + base)),
        pl.BlockSpec((hg, head_dim, head_dim), lambda i, r: (i, 0, 0)),
    ]
    operands = [rates, rows, gains, gains, gains, gain_out, states]
    aliases = {}
    if previous is not None:
        in_specs.append(pl.BlockSpec(memory_space=pl.ANY))
        operands.append(previous)
        aliases = {len(operands) - 1: 0}
    share = steps * cw
    return pl.pallas_call(
        kernel,
        grid_spec=pltpu.PrefetchScalarGridSpec(
            num_scalar_prefetch=1,
            grid=(steps,),
            in_specs=in_specs,
            out_specs=row_spec,
        ),
        out_shape=jax.ShapeDtypeStruct(rows.shape, rows.dtype),
        input_output_aliases=aliases,
        cost_estimate=pl.CostEstimate(
            flops=8 * count * BLOCK * share, transcendentals=3 * count * share,
            bytes_accessed=2 * count * share * 2 + steps * hg * head_dim * head_dim * 2,
        ),
    )(*operands)


def on_device(section_inputs, input_gains, out_gain, decay_rates, carry_state):
    _, count, width = section_inputs.shape
    rates = decay_rates[0]
    heads = rates.shape[0]
    head_dim = width // heads
    group_size = lax.axis_size("ctx")
    own_heads = heads // group_size
    place = lax.axis_index("ctx")
    count_s = lax.axis_size("section")
    pairs = [(src, (src + 1) % count_s) for src in range(count_s)]

    flat_gains = input_gains.reshape(1, -1)
    prev_rows, prev_gains, prev_gain_out, prev_rates = lax.ppermute(
        (section_inputs, flat_gains, out_gain, decay_rates), "section", pairs
    )

    summary = _summaries(rates, section_inputs, flat_gains, head_dim)
    gathered = lax.all_to_all(summary, "ctx", 0, 0, tiled=True)
    gathered = gathered.reshape(group_size, own_heads, head_dim, head_dim)
    prefixes, end_part = _scan(
        place.reshape(1).astype(jnp.int32), rates, gathered, carry_state, count
    )
    incoming = lax.all_to_all(
        prefixes.reshape(heads, head_dim, head_dim), "ctx", 0, 0, tiled=True
    )
    prev_gains, prev_gain_out, prev_rates, incoming = lax.optimization_barrier(
        (prev_gains, prev_gain_out, prev_rates, incoming)
    )
    chunk = heads // STATE_CHUNKS
    next_rows = None
    for part in range(STATE_CHUNKS):
        piece = lax.ppermute(incoming[part * chunk : (part + 1) * chunk], "section", pairs)
        next_rows = _outputs(
            prev_rates[0], prev_rows, prev_gains, prev_gain_out, piece, head_dim,
            part * chunk, next_rows,
        )
    return (next_rows, end_part)


def solution(mesh):
    return jax.shard_map(
        on_device,
        mesh=mesh,
        in_specs=(
            P("section", "ctx", None),
            P("section", None, None),
            P("section", None),
            P("section", None),
            P("section", None, None, None),
        ),
        out_specs=(P("section", "ctx", None), P("section", "ctx", None, None)),
        check_vma=False,
    )
```

```python
import functools

import jax
import jax.numpy as jnp
from jax import lax
from jax.experimental import pallas as pl
from jax.experimental.pallas import tpu as pltpu
from jax.sharding import PartitionSpec as P

BLOCK = 256
EPSILON = 1e-05
HEADS_PER_STEP = 6
SUMMARY_HEADS_PER_STEP = 12
FIRST_CHUNK_STEPS = 3


def _silu(v):
    return 0.5 * v * (1.0 + jnp.tanh(0.5 * v))


def _dot_nt(a, b):
    return lax.dot_general(a, b, (((1,), (1,)), ((), ())), preferred_element_type=jnp.float32)


def _dot_tn(a, b):
    return lax.dot_general(a, b, (((0,), (0,)), ((), ())), preferred_element_type=jnp.float32)


def _dot(a, b):
    return lax.dot_general(a, b, (((1,), (0,)), ((), ())), preferred_element_type=jnp.float32)


def _block_state(keys_b, values_b, rate, pos):
    tail = jnp.exp(-rate * (BLOCK - 1 - pos))
    scaled = (keys_b.astype(jnp.float32) * tail).astype(jnp.bfloat16)
    return _dot_tn(scaled, values_b)


def _summary_kernel(rates_ref, x_ref, gk_ref, gv_ref, o_ref, *, hg, head_dim, nblocks):
    step = pl.program_id(0)
    pos = lax.broadcasted_iota(jnp.int32, (BLOCK, 1), 0).astype(jnp.float32)
    for hh in range(hg):
        rate = jnp.full((1, 1), rates_ref[step * hg + hh], jnp.float32)
        cols = slice(hh * head_dim, (hh + 1) * head_dim)
        decay = jnp.exp(-rate * BLOCK)
        acc = None
        for b in range(nblocks):
            rows = slice(b * BLOCK, (b + 1) * BLOCK)
            x = x_ref[0, rows, cols].astype(jnp.float32)
            keys_b = (_silu(x * gk_ref[0:1, cols]) * head_dim ** (-0.5)).astype(jnp.bfloat16)
            values_b = (x * gv_ref[0:1, cols]).astype(jnp.bfloat16)
            update = _block_state(keys_b, values_b, rate, pos)
            acc = update if acc is None else decay * acc + update
        o_ref[hh] = acc.astype(o_ref.dtype)


def _output_kernel(rates_ref, x_ref, gq_ref, gk_ref, gv_ref, go_ref, s_ref, *rest, hg, head_dim, nblocks, first):
    o_ref = rest[-1]
    step = pl.program_id(0) + first
    pos = lax.broadcasted_iota(jnp.int32, (BLOCK, 1), 0).astype(jnp.float32)
    pos_row = lax.broadcasted_iota(jnp.int32, (1, BLOCK), 1).astype(jnp.float32)
    row = lax.broadcasted_iota(jnp.int32, (BLOCK, BLOCK), 0)
    col = lax.broadcasted_iota(jnp.int32, (BLOCK, BLOCK), 1)
    causal = row >= col
    for hh in range(hg):
        rate = jnp.full((1, 1), rates_ref[step * hg + hh], jnp.float32)
        cols = slice(hh * head_dim, (hh + 1) * head_dim)
        lead = jnp.exp(-rate * (pos + 1.0))
        mask = jnp.where(causal, lead * jnp.exp(rate * (pos_row + 1.0)), 0.0)
        decay = jnp.exp(-rate * BLOCK)
        state = s_ref[hh].astype(jnp.float32)
        for b in range(nblocks):
            rows = slice(b * BLOCK, (b + 1) * BLOCK)
            x = x_ref[0, rows, cols].astype(jnp.float32)
            queries_b = _silu(x * gq_ref[0:1, cols]).astype(jnp.bfloat16)
            keys_b = (_silu(x * gk_ref[0:1, cols]) * head_dim ** (-0.5)).astype(jnp.bfloat16)
            values_b = (x * gv_ref[0:1, cols]).astype(jnp.bfloat16)
            scores = _dot_nt(queries_b, keys_b)
            weights = (scores * mask).astype(jnp.bfloat16)
            local = _dot(weights, values_b)
            cross = _dot(queries_b, state.astype(jnp.bfloat16))
            total = local + lead * cross
            normed = total * lax.rsqrt(jnp.mean(total * total, axis=-1, keepdims=True) + EPSILON)
            o_ref[0, rows, cols] = (x + normed * go_ref[0:1, cols]).astype(o_ref.dtype)
            if b + 1 < nblocks:
                state = decay * state + _block_state(keys_b, values_b, rate, pos)


def _scan_kernel(place_ref, rates_ref, s_ref, c_ref, p_ref, e_ref, *, count, own, sources):
    for hh in range(own):
        rate = jnp.full((1, 1), rates_ref[place_ref[0] * own + hh], jnp.float32)
        decay = jnp.exp(-rate * count)
        state = c_ref[0, hh]
        for c in range(sources):
            p_ref[c, hh] = state.astype(p_ref.dtype)
            state = decay * state + s_ref[c, hh].astype(jnp.float32)
        e_ref[0, hh] = state


def _scan(place, rates, gathered, carry, count):
    sources, own, hd, _ = gathered.shape
    kernel = functools.partial(_scan_kernel, count=count, own=own, sources=sources)
    return pl.pallas_call(
        kernel,
        grid_spec=pltpu.PrefetchScalarGridSpec(
            num_scalar_prefetch=2,
            grid=(1,),
            in_specs=[
                pl.BlockSpec((sources, own, hd, hd), lambda i, p, r: (0, 0, 0, 0)),
                pl.BlockSpec((1, own, hd, hd), lambda i, p, r: (0, p[0], 0, 0)),
            ],
            out_specs=[
                pl.BlockSpec((sources, own, hd, hd), lambda i, p, r: (0, 0, 0, 0)),
                pl.BlockSpec((1, own, hd, hd), lambda i, p, r: (0, 0, 0, 0)),
            ],
        ),
        out_shape=[
            jax.ShapeDtypeStruct(gathered.shape, gathered.dtype),
            jax.ShapeDtypeStruct((1, own, hd, hd), jnp.float32),
        ],
        cost_estimate=pl.CostEstimate(
            flops=2 * gathered.size, transcendentals=0,
            bytes_accessed=4 * gathered.size + 8 * own * hd * hd,
        ),
    )(place, rates, gathered, carry)


def _summaries(rates, rows, gains, head_dim):
    _, count, width = rows.shape
    heads = width // head_dim
    hg = SUMMARY_HEADS_PER_STEP
    cw = hg * head_dim
    per_row = width // cw
    kernel = functools.partial(_summary_kernel, hg=hg, head_dim=head_dim, nblocks=count // BLOCK)
    return pl.pallas_call(
        kernel,
        grid_spec=pltpu.PrefetchScalarGridSpec(
            num_scalar_prefetch=1,
            grid=(heads // hg,),
            in_specs=[
                pl.BlockSpec((1, count, cw), lambda i, r: (0, 0, i)),
                pl.BlockSpec((1, cw), lambda i, r: (0, i + per_row)),
                pl.BlockSpec((1, cw), lambda i, r: (0, i + 2 * per_row)),
            ],
            out_specs=pl.BlockSpec((hg, head_dim, head_dim), lambda i, r: (i, 0, 0)),
        ),
        out_shape=jax.ShapeDtypeStruct((heads, head_dim, head_dim), jnp.bfloat16),
        cost_estimate=pl.CostEstimate(
            flops=2 * count * width * head_dim, transcendentals=count * width,
            bytes_accessed=count * width * 2 + heads * head_dim * head_dim * 4,
        ),
    )(rates, rows, gains, gains)


def _outputs(rates, rows, gains, gain_out, states, head_dim, first, previous):
    _, count, width = rows.shape
    hg = HEADS_PER_STEP
    cw = hg * head_dim
    steps = states.shape[0] // hg
    base = first // hg
    kernel = functools.partial(
        _output_kernel, hg=hg, head_dim=head_dim, nblocks=count // BLOCK, first=base
    )
    row_spec = pl.BlockSpec((1, count, cw), lambda i, r: (0, 0, i + base))
    per_row = width // cw
    in_specs = [
        row_spec,
        pl.BlockSpec((1, cw), lambda i, r: (0, i + base)),
        pl.BlockSpec((1, cw), lambda i, r: (0, i + base + per_row)),
        pl.BlockSpec((1, cw), lambda i, r: (0, i + base + 2 * per_row)),
        pl.BlockSpec((1, cw), lambda i, r: (0, i + base)),
        pl.BlockSpec((hg, head_dim, head_dim), lambda i, r: (i, 0, 0)),
    ]
    operands = [rates, rows, gains, gains, gains, gain_out, states]
    aliases = {}
    if previous is not None:
        in_specs.append(pl.BlockSpec(memory_space=pl.ANY))
        operands.append(previous)
        aliases = {len(operands) - 1: 0}
    share = steps * cw
    return pl.pallas_call(
        kernel,
        grid_spec=pltpu.PrefetchScalarGridSpec(
            num_scalar_prefetch=1,
            grid=(steps,),
            in_specs=in_specs,
            out_specs=row_spec,
        ),
        out_shape=jax.ShapeDtypeStruct(rows.shape, rows.dtype),
        input_output_aliases=aliases,
        cost_estimate=pl.CostEstimate(
            flops=8 * count * BLOCK * share, transcendentals=3 * count * share,
            bytes_accessed=2 * count * share * 2 + steps * hg * head_dim * head_dim * 2,
        ),
    )(*operands)


def on_device(section_inputs, input_gains, out_gain, decay_rates, carry_state):
    _, count, width = section_inputs.shape
    rates = decay_rates[0]
    heads = rates.shape[0]
    head_dim = width // heads
    group_size = lax.axis_size("ctx")
    own_heads = heads // group_size
    place = lax.axis_index("ctx")
    count_s = lax.axis_size("section")
    pairs = [(src, (src + 1) % count_s) for src in range(count_s)]

    flat_gains = input_gains.reshape(1, -1)
    prev_rows, prev_gains, prev_gain_out, prev_rates = lax.ppermute(
        (section_inputs, flat_gains, out_gain, decay_rates), "section", pairs
    )

    summary = _summaries(rates, section_inputs, flat_gains, head_dim)
    gathered = lax.all_to_all(summary, "ctx", 0, 0, tiled=True)
    gathered = gathered.reshape(group_size, own_heads, head_dim, head_dim)
    prefixes, end_part = _scan(
        place.reshape(1).astype(jnp.int32), rates, gathered, carry_state, count
    )
    incoming = lax.all_to_all(
        prefixes.reshape(heads, head_dim, head_dim), "ctx", 0, 0, tiled=True
    )
    prev_gains, prev_gain_out, prev_rates, incoming = lax.optimization_barrier(
        (prev_gains, prev_gain_out, prev_rates, incoming)
    )
    first_chunk = min(FIRST_CHUNK_STEPS * HEADS_PER_STEP, heads)
    bounds = [0, first_chunk, heads] if first_chunk < heads else [0, heads]
    next_rows = None
    for lo, hi in zip(bounds[:-1], bounds[1:]):
        piece = lax.ppermute(incoming[lo:hi], "section", pairs)
        next_rows = _outputs(
            prev_rates[0], prev_rows, prev_gains, prev_gain_out, piece, head_dim,
            lo, next_rows,
        )
    return (next_rows, end_part)


def solution(mesh):
    return jax.shard_map(
        on_device,
        mesh=mesh,
        in_specs=(
            P("section", "ctx", None),
            P("section", None, None),
            P("section", None),
            P("section", None),
            P("section", None, None, None),
        ),
        out_specs=(P("section", "ctx", None), P("section", "ctx", None, None)),
        check_vma=False,
    )
```

```python
import functools

import jax
import jax.numpy as jnp
from jax import lax
from jax.experimental import pallas as pl
from jax.experimental.pallas import tpu as pltpu
from jax.sharding import PartitionSpec as P

BLOCK = 256
EPSILON = 1e-05
HEADS_PER_STEP = 12
SUMMARY_HEADS_PER_STEP = 12
STATE_CHUNKS = 2


def _silu(v):
    return 0.5 * v * (1.0 + jnp.tanh(0.5 * v))


def _dot_nt(a, b):
    return lax.dot_general(a, b, (((1,), (1,)), ((), ())), preferred_element_type=jnp.float32)


def _dot_tn(a, b):
    return lax.dot_general(a, b, (((0,), (0,)), ((), ())), preferred_element_type=jnp.float32)


def _dot(a, b):
    return lax.dot_general(a, b, (((1,), (0,)), ((), ())), preferred_element_type=jnp.float32)


def _block_state(keys_b, values_b, rate, pos):
    tail = jnp.exp(-rate * (BLOCK - 1 - pos))
    scaled = (keys_b.astype(jnp.float32) * tail).astype(jnp.bfloat16)
    return _dot_tn(scaled, values_b)


def _summary_kernel(rates_ref, x_ref, gk_ref, gv_ref, o_ref, *, hg, head_dim, nblocks):
    step = pl.program_id(0)
    pos = lax.broadcasted_iota(jnp.int32, (BLOCK, 1), 0).astype(jnp.float32)
    for hh in range(hg):
        rate = jnp.full((1, 1), rates_ref[step * hg + hh], jnp.float32)
        cols = slice(hh * head_dim, (hh + 1) * head_dim)
        decay = jnp.exp(-rate * BLOCK)
        acc = None
        for b in range(nblocks):
            rows = slice(b * BLOCK, (b + 1) * BLOCK)
            x = x_ref[0, rows, cols].astype(jnp.float32)
            keys_b = (_silu(x * gk_ref[0:1, cols]) * head_dim ** (-0.5)).astype(jnp.bfloat16)
            values_b = (x * gv_ref[0:1, cols]).astype(jnp.bfloat16)
            update = _block_state(keys_b, values_b, rate, pos)
            acc = update if acc is None else decay * acc + update
        o_ref[hh] = acc.astype(o_ref.dtype)


def _output_kernel(rates_ref, x_ref, gq_ref, gk_ref, gv_ref, go_ref, s_ref, *rest, hg, head_dim, nblocks, first):
    o_ref = rest[-1]
    step = pl.program_id(0) + first
    pos = lax.broadcasted_iota(jnp.int32, (BLOCK, 1), 0).astype(jnp.float32)
    pos_row = lax.broadcasted_iota(jnp.int32, (1, BLOCK), 1).astype(jnp.float32)
    row = lax.broadcasted_iota(jnp.int32, (BLOCK, BLOCK), 0)
    col = lax.broadcasted_iota(jnp.int32, (BLOCK, BLOCK), 1)
    causal = row >= col
    for hh in range(hg):
        rate = jnp.full((1, 1), rates_ref[step * hg + hh], jnp.float32)
        cols = slice(hh * head_dim, (hh + 1) * head_dim)
        lead = jnp.exp(-rate * (pos + 1.0))
        mask = jnp.where(causal, lead * jnp.exp(rate * (pos_row + 1.0)), 0.0)
        decay = jnp.exp(-rate * BLOCK)
        state = s_ref[hh].astype(jnp.float32)
        for b in range(nblocks):
            rows = slice(b * BLOCK, (b + 1) * BLOCK)
            x = x_ref[0, rows, cols].astype(jnp.float32)
            queries_b = _silu(x * gq_ref[0:1, cols]).astype(jnp.bfloat16)
            keys_b = (_silu(x * gk_ref[0:1, cols]) * head_dim ** (-0.5)).astype(jnp.bfloat16)
            values_b = (x * gv_ref[0:1, cols]).astype(jnp.bfloat16)
            scores = _dot_nt(queries_b, keys_b)
            weights = (scores * mask).astype(jnp.bfloat16)
            local = _dot(weights, values_b)
            cross = _dot(queries_b, state.astype(jnp.bfloat16))
            total = local + lead * cross
            normed = total * lax.rsqrt(jnp.mean(total * total, axis=-1, keepdims=True) + EPSILON)
            o_ref[0, rows, cols] = (x + normed * go_ref[0:1, cols]).astype(o_ref.dtype)
            if b + 1 < nblocks:
                state = decay * state + _block_state(keys_b, values_b, rate, pos)


def _scan_kernel(place_ref, rates_ref, s_ref, c_ref, p_ref, e_ref, *, count, own, sources):
    for hh in range(own):
        rate = jnp.full((1, 1), rates_ref[place_ref[0] * own + hh], jnp.float32)
        decay = jnp.exp(-rate * count)
        state = c_ref[0, hh]
        for c in range(sources):
            p_ref[c, hh] = state.astype(p_ref.dtype)
            state = decay * state + s_ref[c, hh].astype(jnp.float32)
        e_ref[0, hh] = state


def _scan(place, rates, gathered, carry, count):
    sources, own, hd, _ = gathered.shape
    kernel = functools.partial(_scan_kernel, count=count, own=own, sources=sources)
    return pl.pallas_call(
        kernel,
        grid_spec=pltpu.PrefetchScalarGridSpec(
            num_scalar_prefetch=2,
            grid=(1,),
            in_specs=[
                pl.BlockSpec((sources, own, hd, hd), lambda i, p, r: (0, 0, 0, 0)),
                pl.BlockSpec((1, own, hd, hd), lambda i, p, r: (0, p[0], 0, 0)),
            ],
            out_specs=[
                pl.BlockSpec((sources, own, hd, hd), lambda i, p, r: (0, 0, 0, 0)),
                pl.BlockSpec((1, own, hd, hd), lambda i, p, r: (0, 0, 0, 0)),
            ],
        ),
        out_shape=[
            jax.ShapeDtypeStruct(gathered.shape, gathered.dtype),
            jax.ShapeDtypeStruct((1, own, hd, hd), jnp.float32),
        ],
        cost_estimate=pl.CostEstimate(
            flops=2 * gathered.size, transcendentals=0,
            bytes_accessed=4 * gathered.size + 8 * own * hd * hd,
        ),
    )(place, rates, gathered, carry)


def _summaries(rates, rows, gains, head_dim):
    _, count, width = rows.shape
    heads = width // head_dim
    hg = SUMMARY_HEADS_PER_STEP
    cw = hg * head_dim
    per_row = width // cw
    kernel = functools.partial(_summary_kernel, hg=hg, head_dim=head_dim, nblocks=count // BLOCK)
    return pl.pallas_call(
        kernel,
        grid_spec=pltpu.PrefetchScalarGridSpec(
            num_scalar_prefetch=1,
            grid=(heads // hg,),
            in_specs=[
                pl.BlockSpec((1, count, cw), lambda i, r: (0, 0, i)),
                pl.BlockSpec((1, cw), lambda i, r: (0, i + per_row)),
                pl.BlockSpec((1, cw), lambda i, r: (0, i + 2 * per_row)),
            ],
            out_specs=pl.BlockSpec((hg, head_dim, head_dim), lambda i, r: (i, 0, 0)),
        ),
        out_shape=jax.ShapeDtypeStruct((heads, head_dim, head_dim), jnp.bfloat16),
        cost_estimate=pl.CostEstimate(
            flops=2 * count * width * head_dim, transcendentals=count * width,
            bytes_accessed=count * width * 2 + heads * head_dim * head_dim * 4,
        ),
    )(rates, rows, gains, gains)


def _outputs(rates, rows, gains, gain_out, states, head_dim, first, previous):
    _, count, width = rows.shape
    hg = HEADS_PER_STEP
    cw = hg * head_dim
    steps = states.shape[0] // hg
    base = first // hg
    kernel = functools.partial(
        _output_kernel, hg=hg, head_dim=head_dim, nblocks=count // BLOCK, first=base
    )
    row_spec = pl.BlockSpec((1, count, cw), lambda i, r: (0, 0, i + base))
    per_row = width // cw
    in_specs = [
        row_spec,
        pl.BlockSpec((1, cw), lambda i, r: (0, i + base)),
        pl.BlockSpec((1, cw), lambda i, r: (0, i + base + per_row)),
        pl.BlockSpec((1, cw), lambda i, r: (0, i + base + 2 * per_row)),
        pl.BlockSpec((1, cw), lambda i, r: (0, i + base)),
        pl.BlockSpec((hg, head_dim, head_dim), lambda i, r: (i, 0, 0)),
    ]
    operands = [rates, rows, gains, gains, gains, gain_out, states]
    aliases = {}
    if previous is not None:
        in_specs.append(pl.BlockSpec(memory_space=pl.ANY))
        operands.append(previous)
        aliases = {len(operands) - 1: 0}
    share = steps * cw
    return pl.pallas_call(
        kernel,
        grid_spec=pltpu.PrefetchScalarGridSpec(
            num_scalar_prefetch=1,
            grid=(steps,),
            in_specs=in_specs,
            out_specs=row_spec,
        ),
        out_shape=jax.ShapeDtypeStruct(rows.shape, rows.dtype),
        input_output_aliases=aliases,
        cost_estimate=pl.CostEstimate(
            flops=8 * count * BLOCK * share, transcendentals=3 * count * share,
            bytes_accessed=2 * count * share * 2 + steps * hg * head_dim * head_dim * 2,
        ),
    )(*operands)


def on_device(section_inputs, input_gains, out_gain, decay_rates, carry_state):
    _, count, width = section_inputs.shape
    rates = decay_rates[0]
    heads = rates.shape[0]
    head_dim = width // heads
    group_size = lax.axis_size("ctx")
    own_heads = heads // group_size
    place = lax.axis_index("ctx")
    count_s = lax.axis_size("section")
    pairs = [(src, (src + 1) % count_s) for src in range(count_s)]

    flat_gains = input_gains.reshape(1, -1)
    prev_rows, prev_gains, prev_gain_out, prev_rates = lax.ppermute(
        (section_inputs, flat_gains, out_gain, decay_rates), "section", pairs
    )

    summary = _summaries(rates, section_inputs, flat_gains, head_dim)
    gathered = lax.all_to_all(summary, "ctx", 0, 0, tiled=True)
    gathered = gathered.reshape(group_size, own_heads, head_dim, head_dim)
    prefixes, end_part = _scan(
        place.reshape(1).astype(jnp.int32), rates, gathered, carry_state, count
    )
    incoming = lax.all_to_all(
        prefixes.reshape(heads, head_dim, head_dim), "ctx", 0, 0, tiled=True
    )
    prev_gains, prev_gain_out, prev_rates, incoming = lax.optimization_barrier(
        (prev_gains, prev_gain_out, prev_rates, incoming)
    )
    chunk = heads // STATE_CHUNKS
    next_rows = None
    for part in range(STATE_CHUNKS):
        piece = lax.ppermute(incoming[part * chunk : (part + 1) * chunk], "section", pairs)
        next_rows = _outputs(
            prev_rates[0], prev_rows, prev_gains, prev_gain_out, piece, head_dim,
            part * chunk, next_rows,
        )
    return (next_rows, end_part)


def solution(mesh):
    return jax.shard_map(
        on_device,
        mesh=mesh,
        in_specs=(
            P("section", "ctx", None),
            P("section", None, None),
            P("section", None),
            P("section", None),
            P("section", None, None, None),
        ),
        out_specs=(P("section", "ctx", None), P("section", "ctx", None, None)),
        check_vma=False,
    )
```

```python
import functools

import jax
import jax.numpy as jnp
from jax import lax
from jax.experimental import pallas as pl
from jax.experimental.pallas import tpu as pltpu
from jax.sharding import PartitionSpec as P

BLOCK = 256
EPSILON = 1e-05
HEADS_PER_STEP = 8
SUMMARY_HEADS_PER_STEP = 12
STATE_CHUNKS = 3


def _silu(v):
    return 0.5 * v * (1.0 + jnp.tanh(0.5 * v))


def _dot_nt(a, b):
    return lax.dot_general(a, b, (((1,), (1,)), ((), ())), preferred_element_type=jnp.float32)


def _dot_tn(a, b):
    return lax.dot_general(a, b, (((0,), (0,)), ((), ())), preferred_element_type=jnp.float32)


def _dot(a, b):
    return lax.dot_general(a, b, (((1,), (0,)), ((), ())), preferred_element_type=jnp.float32)


def _block_state(keys_b, values_b, rate, pos):
    tail = jnp.exp(-rate * (BLOCK - 1 - pos))
    scaled = (keys_b.astype(jnp.float32) * tail).astype(jnp.bfloat16)
    return _dot_tn(scaled, values_b)


def _summary_kernel(rates_ref, x_ref, gk_ref, gv_ref, o_ref, *, hg, head_dim, nblocks):
    step = pl.program_id(0)
    pos = lax.broadcasted_iota(jnp.int32, (BLOCK, 1), 0).astype(jnp.float32)
    for hh in range(hg):
        rate = jnp.full((1, 1), rates_ref[step * hg + hh], jnp.float32)
        cols = slice(hh * head_dim, (hh + 1) * head_dim)
        decay = jnp.exp(-rate * BLOCK)
        acc = None
        for b in range(nblocks):
            rows = slice(b * BLOCK, (b + 1) * BLOCK)
            x = x_ref[0, rows, cols].astype(jnp.float32)
            keys_b = (_silu(x * gk_ref[0:1, cols]) * head_dim ** (-0.5)).astype(jnp.bfloat16)
            values_b = (x * gv_ref[0:1, cols]).astype(jnp.bfloat16)
            update = _block_state(keys_b, values_b, rate, pos)
            acc = update if acc is None else decay * acc + update
        o_ref[hh] = acc.astype(o_ref.dtype)


def _output_kernel(rates_ref, x_ref, gq_ref, gk_ref, gv_ref, go_ref, s_ref, *rest, hg, head_dim, nblocks, first):
    o_ref = rest[-1]
    step = pl.program_id(0) + first
    pos = lax.broadcasted_iota(jnp.int32, (BLOCK, 1), 0).astype(jnp.float32)
    pos_row = lax.broadcasted_iota(jnp.int32, (1, BLOCK), 1).astype(jnp.float32)
    row = lax.broadcasted_iota(jnp.int32, (BLOCK, BLOCK), 0)
    col = lax.broadcasted_iota(jnp.int32, (BLOCK, BLOCK), 1)
    causal = row >= col
    for hh in range(hg):
        rate = jnp.full((1, 1), rates_ref[step * hg + hh], jnp.float32)
        cols = slice(hh * head_dim, (hh + 1) * head_dim)
        lead = jnp.exp(-rate * (pos + 1.0))
        mask = jnp.where(causal, lead * jnp.exp(rate * (pos_row + 1.0)), 0.0)
        decay = jnp.exp(-rate * BLOCK)
        state = s_ref[hh].astype(jnp.float32)
        for b in range(nblocks):
            rows = slice(b * BLOCK, (b + 1) * BLOCK)
            x = x_ref[0, rows, cols].astype(jnp.float32)
            queries_b = _silu(x * gq_ref[0:1, cols]).astype(jnp.bfloat16)
            keys_b = (_silu(x * gk_ref[0:1, cols]) * head_dim ** (-0.5)).astype(jnp.bfloat16)
            values_b = (x * gv_ref[0:1, cols]).astype(jnp.bfloat16)
            scores = _dot_nt(queries_b, keys_b)
            weights = (scores * mask).astype(jnp.bfloat16)
            local = _dot(weights, values_b)
            cross = _dot(queries_b, state.astype(jnp.bfloat16))
            total = local + lead * cross
            normed = total * lax.rsqrt(jnp.mean(total * total, axis=-1, keepdims=True) + EPSILON)
            o_ref[0, rows, cols] = (x + normed * go_ref[0:1, cols]).astype(o_ref.dtype)
            if b + 1 < nblocks:
                state = decay * state + _block_state(keys_b, values_b, rate, pos)


def _scan_kernel(place_ref, rates_ref, s_ref, c_ref, p_ref, e_ref, *, count, own, sources):
    for hh in range(own):
        rate = jnp.full((1, 1), rates_ref[place_ref[0] * own + hh], jnp.float32)
        decay = jnp.exp(-rate * count)
        state = c_ref[0, hh]
        for c in range(sources):
            p_ref[c, hh] = state.astype(p_ref.dtype)
            state = decay * state + s_ref[c, hh].astype(jnp.float32)
        e_ref[0, hh] = state


def _scan(place, rates, gathered, carry, count):
    sources, own, hd, _ = gathered.shape
    kernel = functools.partial(_scan_kernel, count=count, own=own, sources=sources)
    return pl.pallas_call(
        kernel,
        grid_spec=pltpu.PrefetchScalarGridSpec(
            num_scalar_prefetch=2,
            grid=(1,),
            in_specs=[
                pl.BlockSpec((sources, own, hd, hd), lambda i, p, r: (0, 0, 0, 0)),
                pl.BlockSpec((1, own, hd, hd), lambda i, p, r: (0, p[0], 0, 0)),
            ],
            out_specs=[
                pl.BlockSpec((sources, own, hd, hd), lambda i, p, r: (0, 0, 0, 0)),
                pl.BlockSpec((1, own, hd, hd), lambda i, p, r: (0, 0, 0, 0)),
            ],
        ),
        out_shape=[
            jax.ShapeDtypeStruct(gathered.shape, gathered.dtype),
            jax.ShapeDtypeStruct((1, own, hd, hd), jnp.float32),
        ],
        cost_estimate=pl.CostEstimate(
            flops=2 * gathered.size, transcendentals=0,
            bytes_accessed=4 * gathered.size + 8 * own * hd * hd,
        ),
    )(place, rates, gathered, carry)


def _summaries(rates, rows, gains, head_dim):
    _, count, width = rows.shape
    heads = width // head_dim
    hg = SUMMARY_HEADS_PER_STEP
    cw = hg * head_dim
    per_row = width // cw
    kernel = functools.partial(_summary_kernel, hg=hg, head_dim=head_dim, nblocks=count // BLOCK)
    return pl.pallas_call(
        kernel,
        grid_spec=pltpu.PrefetchScalarGridSpec(
            num_scalar_prefetch=1,
            grid=(heads // hg,),
            in_specs=[
                pl.BlockSpec((1, count, cw), lambda i, r: (0, 0, i)),
                pl.BlockSpec((1, cw), lambda i, r: (0, i + per_row)),
                pl.BlockSpec((1, cw), lambda i, r: (0, i + 2 * per_row)),
            ],
            out_specs=pl.BlockSpec((hg, head_dim, head_dim), lambda i, r: (i, 0, 0)),
        ),
        out_shape=jax.ShapeDtypeStruct((heads, head_dim, head_dim), jnp.bfloat16),
        cost_estimate=pl.CostEstimate(
            flops=2 * count * width * head_dim, transcendentals=count * width,
            bytes_accessed=count * width * 2 + heads * head_dim * head_dim * 4,
        ),
    )(rates, rows, gains, gains)


def _outputs(rates, rows, gains, gain_out, states, head_dim, first, previous):
    _, count, width = rows.shape
    hg = HEADS_PER_STEP
    cw = hg * head_dim
    steps = states.shape[0] // hg
    base = first // hg
    kernel = functools.partial(
        _output_kernel, hg=hg, head_dim=head_dim, nblocks=count // BLOCK, first=base
    )
    row_spec = pl.BlockSpec((1, count, cw), lambda i, r: (0, 0, i + base))
    per_row = width // cw
    in_specs = [
        row_spec,
        pl.BlockSpec((1, cw), lambda i, r: (0, i + base)),
        pl.BlockSpec((1, cw), lambda i, r: (0, i + base + per_row)),
        pl.BlockSpec((1, cw), lambda i, r: (0, i + base + 2 * per_row)),
        pl.BlockSpec((1, cw), lambda i, r: (0, i + base)),
        pl.BlockSpec((hg, head_dim, head_dim), lambda i, r: (i, 0, 0)),
    ]
    operands = [rates, rows, gains, gains, gains, gain_out, states]
    aliases = {}
    if previous is not None:
        in_specs.append(pl.BlockSpec(memory_space=pl.ANY))
        operands.append(previous)
        aliases = {len(operands) - 1: 0}
    share = steps * cw
    return pl.pallas_call(
        kernel,
        grid_spec=pltpu.PrefetchScalarGridSpec(
            num_scalar_prefetch=1,
            grid=(steps,),
            in_specs=in_specs,
            out_specs=row_spec,
        ),
        out_shape=jax.ShapeDtypeStruct(rows.shape, rows.dtype),
        input_output_aliases=aliases,
        cost_estimate=pl.CostEstimate(
            flops=8 * count * BLOCK * share, transcendentals=3 * count * share,
            bytes_accessed=2 * count * share * 2 + steps * hg * head_dim * head_dim * 2,
        ),
    )(*operands)


def on_device(section_inputs, input_gains, out_gain, decay_rates, carry_state):
    _, count, width = section_inputs.shape
    rates = decay_rates[0]
    heads = rates.shape[0]
    head_dim = width // heads
    group_size = lax.axis_size("ctx")
    own_heads = heads // group_size
    place = lax.axis_index("ctx")
    count_s = lax.axis_size("section")
    pairs = [(src, (src + 1) % count_s) for src in range(count_s)]

    flat_gains = input_gains.reshape(1, -1)
    prev_rows, prev_gains, prev_gain_out, prev_rates = lax.ppermute(
        (section_inputs, flat_gains, out_gain, decay_rates), "section", pairs
    )

    summary = _summaries(rates, section_inputs, flat_gains, head_dim)
    gathered = lax.all_to_all(summary, "ctx", 0, 0, tiled=True)
    gathered = gathered.reshape(group_size, own_heads, head_dim, head_dim)
    prefixes, end_part = _scan(
        place.reshape(1).astype(jnp.int32), rates, gathered, carry_state, count
    )
    incoming = lax.all_to_all(
        prefixes.reshape(heads, head_dim, head_dim), "ctx", 0, 0, tiled=True
    )
    prev_gains, prev_gain_out, prev_rates, incoming = lax.optimization_barrier(
        (prev_gains, prev_gain_out, prev_rates, incoming)
    )
    chunk = heads // STATE_CHUNKS
    next_rows = None
    for part in range(STATE_CHUNKS):
        piece = lax.ppermute(incoming[part * chunk : (part + 1) * chunk], "section", pairs)
        next_rows = _outputs(
            prev_rates[0], prev_rows, prev_gains, prev_gain_out, piece, head_dim,
            part * chunk, next_rows,
        )
    return (next_rows, end_part)


def solution(mesh):
    return jax.shard_map(
        on_device,
        mesh=mesh,
        in_specs=(
            P("section", "ctx", None),
            P("section", None, None),
            P("section", None),
            P("section", None),
            P("section", None, None, None),
        ),
        out_specs=(P("section", "ctx", None), P("section", "ctx", None, None)),
        check_vma=False,
    )
```
